256 devices in a mesh: tm: 16 (over z, x_hi), height: 4 (over x_lo, core), mp: 4 (over y).
Axes of the slice: x: 4 (x_hi: 2, x_lo: 2; x = x_hi * 2 + x_lo), y: 4, z: 8, core: 2. Of those that a mesh axis runs over, the one named last changes fastest.
Arguments:
- image_q: bfloat16 [16, 4, 384, 3072], P('tm', 'height', None, 'mp'), may hold values from -8 to 8
- image_kv: bfloat16 [16, 4, 2, 384, 3072], P('tm', 'height', None, None, 'mp'), may hold values from -8 to 8
- text_kv: bfloat16 [2, 256, 3072], P(None, 'tm', 'mp'), may hold values from -8 to 8
- residual: bfloat16 [16, 4, 384, 3072], P('tm', 'height', None, 'mp'), may hold values from -3 to 3
- out_weight: bfloat16 [3072, 3072], P('mp'), may hold values from -0.109375 to 0.109375
- out_gate: float32 [3072], P('mp'), may hold values from 0.5 to 2
- head_reach: int32 [24, 2], P('mp'), may hold values from 0 to 1, as said below
- tile_extent: int32 [2, 16, 4], replicated, may hold values from 1 to 8, as said below
Outputs:
- updated_tokens: bfloat16 [16, 4, 384, 3072], P('tm', 'height', None, 'mp')
The draws below stay inside these ranges and needn't reach their ends.
Inputs may be any that keep to these rules, and one draw needn't show every extreme that they name: `head_reach`: in each column exactly 16 heads have reach 1, the others 0. `tile_extent`: valid frames are 6 except in the last tile row along time, where they are below 6; valid rows are 8 except in the last tile row along height, where they are below 8.
All inputs are finite; a program needn't handle non-finite values.
Results may differ from the reference program's by a relative error of at most 0.015.
Values may be sent and summed in bfloat16 or wider, within the bound.
No kernel may reach another device: no remote copies, remote signals or barrier semaphores. Data moves between devices by JAX's collectives and lax.ppermute only.
A program may use at most 128 MiB of HBM per device.

```python
import math
import jax
import jax.numpy as jnp
from jax import lax

D = 3072
HEADS = 24
HD = 128
TXT = 256
TILE_F = 6
TILE_R = 8
TILE_C = 8
TILE = 384
TILES_T = 16
TILES_H = 4
HEAD_GROUPS = 4


def draw_image_q(key, part):
    full_shape = (TILES_T, TILES_H, TILE_F * TILE_R * TILE_C, HEADS * HD)
    base_key = jax.random.fold_in(key, 1)
    values = jnp.clip(1.6 * jax.random.normal(base_key, full_shape, jnp.float32), -8.0, 8.0)
    return values.astype(jnp.bfloat16)


def draw_image_kv(key, part):
    full_shape = (TILES_T, TILES_H, TILE_F * TILE_R * TILE_C, HEADS * HD)
    key_base = jax.random.fold_in(key, 2)
    value_base = jax.random.fold_in(key, 3)
    key_values = jnp.clip(1.6 * jax.random.normal(key_base, full_shape, jnp.float32), -8.0, 8.0)
    value_values = jnp.clip(jax.random.normal(value_base, full_shape, jnp.float32), -6.0, 6.0)
    return jnp.stack([key_values, value_values], axis=2).astype(jnp.bfloat16)


def draw_head_reach(key, part):
    columns = []
    for column in range(2):
        shuffled = jax.random.permutation(jax.random.fold_in(key, 20 + column), HEADS)
        columns.append((shuffled < 2 * HEADS // 3).astype(jnp.int32))
    return jnp.stack(columns, axis=1)


def draw_tile_extent(key, part):
    frame_counts = jnp.full((TILES_T, TILES_H), TILE_F, jnp.int32)
    frame_edge = jax.random.randint(jax.random.fold_in(key, 30), (TILES_H,), 1, TILE_F, dtype=jnp.int32)
    frame_spot = jax.random.randint(jax.random.fold_in(key, 32), (), 0, TILES_H, dtype=jnp.int32)
    frame_edge = jnp.where(jnp.arange(TILES_H, dtype=jnp.int32) == frame_spot, 1, frame_edge)
    frame_counts = frame_counts.at[TILES_T - 1].set(frame_edge)
    row_counts = jnp.full((TILES_T, TILES_H), TILE_R, jnp.int32)
    row_edge = jax.random.randint(jax.random.fold_in(key, 31), (TILES_T,), 1, TILE_R, dtype=jnp.int32)
    row_spot = jax.random.randint(jax.random.fold_in(key, 33), (), 0, TILES_T, dtype=jnp.int32)
    row_edge = jnp.where(jnp.arange(TILES_T, dtype=jnp.int32) == row_spot, 1, row_edge)
    row_counts = row_counts.at[:, TILES_H - 1].set(row_edge)
    return jnp.stack([frame_counts, row_counts], axis=0)


def level_of(stream_key, extent, split, low, high):
    gain, own = 1.0, jax.random.fold_in(stream_key, 6)
    for dim, shards_of in split:
        draws = jnp.exp(jax.random.uniform(jax.random.fold_in(own, dim), (shards_of,), jnp.float32, low / len(split), high / len(split)))
        gain = gain * jnp.repeat(draws, extent[dim] // shards_of).reshape([-1 if axis == dim else 1 for axis in range(len(extent))])
    return gain


def bell_draw(stream_key, extent, scale, limit, pieces=(), kind=jnp.bfloat16):
    level = level_of(stream_key, extent, pieces, -0.22, 0.18) if pieces else 1.0
    values = jax.random.normal(stream_key, extent, jnp.float32) * scale * level
    return jnp.minimum(jnp.maximum(values, -limit), limit).astype(kind)


def setup_inputs(seed: int = 0) -> dict:
    keys = jax.random.split(jax.random.key(seed), 9)
    return {
        "image_q": draw_image_q(jax.random.fold_in(keys[8], 71), 0),
        "image_kv": draw_image_kv(jax.random.fold_in(keys[8], 71), 0),
        "text_kv": bell_draw(keys[2], (2, TXT, HEADS * HD), 1.8, 8.0, ((1, 16), (2, 4))),
        "residual": bell_draw(keys[3], (TILES_T, TILES_H, TILE, D), 0.5, 3.0, ((0, 16), (1, 4), (3, 4))),
        "out_weight": bell_draw(keys[4], (HEADS * HD, D), (HEADS * HD) ** -0.5, 0.109375, ((0, 4),)),
        "out_gate": jnp.clip(0.5 + 1.5 * jax.random.uniform(keys[5], (D,), jnp.float32) ** level_of(keys[5], (D,), ((0, 4),), -0.2, 0.2), 0.5, 2.0),
        "head_reach": draw_head_reach(jax.random.fold_in(keys[8], 71), 0),
        "tile_extent": draw_tile_extent(jax.random.fold_in(keys[8], 71), 0),
    }


def token_masks(extent_pair):
    positions = jnp.arange(TILE_F * TILE_R * TILE_C, dtype=jnp.int32)
    frame_of = positions // (TILE_R * TILE_C)
    row_of = positions // TILE_C % TILE_R
    frame_ok = frame_of < extent_pair[0][..., None]
    row_ok = row_of < extent_pair[1][..., None]
    return jnp.logical_and(frame_ok, row_ok)

def reference(image_q, image_kv, text_kv, residual, out_weight, out_gate, head_reach, tile_extent):
    tiles_time = image_q.shape[0]
    tiles_height = image_q.shape[1]
    tile_len = image_q.shape[2]
    col_width = image_q.shape[3]
    head_count = col_width // HD
    model_width = residual.shape[3]
    padded_kv = jnp.pad(image_kv, ((1, 1), (1, 1), (0, 0), (0, 0), (0, 0)))
    padded_ext = jnp.pad(tile_extent, ((0, 0), (1, 1), (1, 1)))
    key_valid = token_masks(padded_ext)
    query_valid = token_masks(tile_extent).reshape(-1, tile_len)
    flat_q = image_q.reshape(-1, tile_len, col_width)
    offsets = jnp.abs(jnp.arange(3, dtype=jnp.int32) - 1)
    scale_factor = 1.0 / math.sqrt(HD)
    text_keys = text_kv[0].astype(jnp.float32).reshape(TXT, head_count, HD)
    text_values = text_kv[1].astype(jnp.float32).reshape(TXT, head_count, HD)
    zero_index = jnp.int32(0)
    reach_time = head_reach[:, 0]
    reach_height = head_reach[:, 1]

    def one_tile(tile_index):
        time_tile = tile_index // tiles_height
        height_tile = tile_index % tiles_height
        window = lax.dynamic_slice(padded_kv, (time_tile, height_tile, zero_index, zero_index, zero_index), (3, 3, 2, tile_len, col_width))
        key_ok = lax.dynamic_slice(key_valid, (time_tile, height_tile, zero_index), (3, 3, tile_len))
        key_rows = jnp.concatenate([window[:, :, 0].astype(jnp.float32).reshape(-1, head_count, HD), text_keys], axis=0)
        value_rows = jnp.concatenate([window[:, :, 1].astype(jnp.float32).reshape(-1, head_count, HD), text_values], axis=0)
        image_ok = key_ok[None]
        image_ok = jnp.logical_and(image_ok, offsets[None, :, None, None] <= reach_time[:, None, None, None])
        image_ok = jnp.logical_and(image_ok, offsets[None, None, :, None] <= reach_height[:, None, None, None])
        allowed = jnp.concatenate([image_ok.reshape(head_count, -1), jnp.ones((head_count, TXT), jnp.bool_)], axis=1)
        query_f32 = flat_q[tile_index].astype(jnp.float32).reshape(tile_len, head_count, HD)
        scores = jnp.einsum('ind,jnd->nij', query_f32, key_rows) * scale_factor
        masked = jnp.where(allowed[:, None, :], scores, -1e+30)
        top_score = lax.optimization_barrier(jnp.max(masked, axis=2, keepdims=True))
        weights = jnp.where(allowed[:, None, :], jnp.exp(masked - top_score), 0.0)
        row_total = lax.optimization_barrier(jnp.sum(weights, axis=2))
        rounded = lax.optimization_barrier(weights.astype(jnp.bfloat16)).astype(jnp.float32)
        attended = jnp.einsum('nij,jnd->ind', rounded, value_rows) / jnp.transpose(row_total)[:, :, None]
        attended = jnp.where(query_valid[tile_index][:, None, None], attended, 0.0)
        return attended.reshape(tile_len, col_width).astype(jnp.bfloat16)
    attended = lax.map(one_tile, jnp.arange(flat_q.shape[0], dtype=jnp.int32))
    flat_rows = attended.reshape(-1, col_width)
    group_width = col_width // HEAD_GROUPS
    branch = jnp.zeros((flat_rows.shape[0], model_width), jnp.float32)
    for group_index in range(HEAD_GROUPS):
        low_col = group_index * group_width
        part_sum = jnp.dot(flat_rows[:, low_col:low_col + group_width], out_weight[low_col:low_col + group_width], preferred_element_type=jnp.float32).astype(jnp.bfloat16)
        branch = branch + lax.optimization_barrier(part_sum).astype(jnp.float32)
    updated = residual.astype(jnp.float32).reshape(-1, model_width) + out_gate[None, :] * branch
    return updated.astype(jnp.bfloat16).reshape(residual.shape)
```

```python
import math

import jax
import jax.numpy as jnp
from jax import lax
from jax.experimental import pallas as pl
from jax.experimental.pallas import tpu as pltpu
from jax.sharding import PartitionSpec as P

HD = 128
TXT = 256
TILE_F = 6
TILE_R = 8
TILE_C = 8
NEG = -1e30


def token_masks(extent_pair):
    positions = jnp.arange(TILE_F * TILE_R * TILE_C, dtype=jnp.int32)
    frame_of = positions // (TILE_R * TILE_C)
    row_of = positions // TILE_C % TILE_R
    frame_ok = frame_of < extent_pair[0][..., None]
    row_ok = row_of < extent_pair[1][..., None]
    return jnp.logical_and(frame_ok, row_ok)


def shift_pairs(devices, step):
    return [(i, i + step) for i in range(devices) if 0 <= i + step < devices]


def attention_kernel(reach_ref, q_ref, text_ref, *rest):
    tile_refs = rest[:9]
    bias_ref, qvalid_ref, o_ref, m_ref, l_ref, acc_ref = rest[9:]
    head = pl.program_id(0)
    scale = 1.0 / math.sqrt(HD)
    q = q_ref[...]
    dims = (((1,), (1,)), ((), ()))
    s = lax.dot_general(q, text_ref[0], dims, preferred_element_type=jnp.float32) * scale
    m = jnp.max(s, axis=1, keepdims=True)
    p = jnp.exp(s - m)
    m_ref[...] = m
    l_ref[...] = jnp.sum(p, axis=1, keepdims=True)
    acc_ref[...] = jnp.dot(p.astype(jnp.bfloat16), text_ref[1], preferred_element_type=jnp.float32)
    reach_t = reach_ref[head, 0]
    reach_h = reach_ref[head, 1]
    for b in range(9):
        off_t, off_h = abs(b // 3 - 1), abs(b % 3 - 1)
        tile_ref = tile_refs[b]

        def block(tile_ref=tile_ref, b=b):
            s = lax.dot_general(q, tile_ref[0], dims, preferred_element_type=jnp.float32)
            s = s * scale + bias_ref[b]
            m_old = m_ref[...]
            m_new = jnp.maximum(m_old, jnp.max(s, axis=1, keepdims=True))
            alpha = jnp.exp(m_old - m_new)
            p = jnp.exp(s - m_new)
            l_ref[...] = alpha * l_ref[...] + jnp.sum(p, axis=1, keepdims=True)
            acc_ref[...] = alpha * acc_ref[...] + jnp.dot(
                p.astype(jnp.bfloat16), tile_ref[1], preferred_element_type=jnp.float32
            )
            m_ref[...] = m_new

        if off_t == 0 and off_h == 0:
            block()
        else:
            pl.when(jnp.logical_and(reach_t >= off_t, reach_h >= off_h))(block)
    out = acc_ref[...] / l_ref[...]
    out = jnp.where(qvalid_ref[...] > 0, out, 0.0)
    o_ref[...] = out.astype(o_ref.dtype)


def attend(reach, queries, text, tiles, bias, qvalid):
    tile_len, col_width = queries.shape
    heads = col_width // HD
    tile_specs = []
    tile_args = []
    for array, index in tiles:
        if index is None:
            tile_specs.append(pl.BlockSpec((2, tile_len, HD), lambda h, r: (0, 0, h)))
        else:
            tile_specs.append(
                pl.BlockSpec((None, 2, tile_len, HD), lambda h, r, i=index: (i, 0, 0, h))
            )
        tile_args.append(array)
    grid_spec = pltpu.PrefetchScalarGridSpec(
        num_scalar_prefetch=1,
        grid=(heads,),
        in_specs=[
            pl.BlockSpec((tile_len, HD), lambda h, r: (0, h)),
            pl.BlockSpec((2, text.shape[1], HD), lambda h, r: (0, 0, h)),
            *tile_specs,
            pl.BlockSpec(bias.shape, lambda h, r: (0, 0, 0)),
            pl.BlockSpec(qvalid.shape, lambda h, r: (0, 0)),
        ],
        out_specs=pl.BlockSpec((tile_len, HD), lambda h, r: (0, h)),
        scratch_shapes=[
            pltpu.VMEM((tile_len, 1), jnp.float32),
            pltpu.VMEM((tile_len, 1), jnp.float32),
            pltpu.VMEM((tile_len, HD), jnp.float32),
        ],
    )
    return pl.pallas_call(
        attention_kernel,
        grid_spec=grid_spec,
        out_shape=jax.ShapeDtypeStruct((tile_len, col_width), jnp.bfloat16),
    )(reach, queries, text, *tile_args, bias, qvalid)


def per_device(image_q, image_kv, text_kv, residual, out_weight, out_gate, head_reach, tile_extent):
    tile_len = image_q.shape[2]
    col_width = image_q.shape[3]
    tm_size = lax.axis_size("tm")
    height_size = lax.axis_size("height")
    mp_size = lax.axis_size("mp")

    gathered = lax.all_gather(text_kv, "tm", axis=0)
    text = jnp.transpose(gathered, (1, 0, 2, 3)).reshape(2, -1, col_width)

    own = image_kv[0, 0]
    t_before = lax.ppermute(own, "tm", shift_pairs(tm_size, 1))
    t_after = lax.ppermute(own, "tm", shift_pairs(tm_size, -1))
    h_before = lax.ppermute(own, "height", shift_pairs(height_size, 1))
    h_after = lax.ppermute(own, "height", shift_pairs(height_size, -1))
    time_pair = jnp.stack([t_before, t_after])
    c_before = lax.ppermute(time_pair, "height", shift_pairs(height_size, 1))
    c_after = lax.ppermute(time_pair, "height", shift_pairs(height_size, -1))
    tiles = [
        (c_before, 0), (t_before, None), (c_after, 0),
        (h_before, None), (own, None), (h_after, None),
        (c_before, 1), (t_after, None), (c_after, 1),
    ]

    time_start = lax.axis_index("tm")
    height_start = lax.axis_index("height")
    zero_index = jnp.int32(0)
    padded_ext = jnp.pad(tile_extent, ((0, 0), (1, 1), (1, 1)))
    local_ext = lax.dynamic_slice(padded_ext, (zero_index, time_start, height_start), (2, 3, 3))
    key_valid = token_masks(local_ext)
    bias = jnp.where(key_valid, 0.0, NEG).astype(jnp.float32).reshape(9, 1, tile_len)
    qvalid = key_valid[1, 1].astype(jnp.float32).reshape(tile_len, 1)

    attended = attend(head_reach, image_q[0, 0], text, tiles, bias, qvalid)

    mp_index = lax.axis_index("mp")
    chunk = out_weight.shape[1] // mp_size
    received = []
    for step in (2, 1, 3):
        target = (mp_index + step) % mp_size
        w_part = lax.dynamic_slice_in_dim(out_weight, target * chunk, chunk, 1)
        part = jnp.dot(attended, w_part, preferred_element_type=jnp.float32).astype(jnp.bfloat16)
        pairs = [(i, (i + step) % mp_size) for i in range(mp_size)]
        received.append(lax.ppermute(part, "mp", pairs))
    w_own = lax.dynamic_slice_in_dim(out_weight, mp_index * chunk, chunk, 1)
    branch = jnp.dot(attended, w_own, preferred_element_type=jnp.float32).astype(jnp.bfloat16)
    branch = branch.astype(jnp.float32)
    for part in received:
        branch = branch + part.astype(jnp.float32)
    updated = residual[0, 0].astype(jnp.float32) + out_gate * branch
    return updated.astype(jnp.bfloat16)[None, None]


def solution(mesh):
    return jax.shard_map(
        per_device,
        mesh=mesh,
        in_specs=(
            P("tm", "height", None, "mp"),
            P("tm", "height", None, None, "mp"),
            P(None, "tm", "mp"),
            P("tm", "height", None, "mp"),
            P("mp", None),
            P("mp"),
            P("mp", None),
            P(),
        ),
        out_specs=P("tm", "height", None, "mp"),
        check_vma=False,
    )
```

```python
import math

import jax
import jax.numpy as jnp
from jax import lax
from jax.experimental import pallas as pl
from jax.experimental.pallas import tpu as pltpu
from jax.sharding import PartitionSpec as P

HD = 128
TXT = 256
TILE_F = 6
TILE_R = 8
TILE_C = 8
NEG = -1e30


def token_masks(extent_pair):
    positions = jnp.arange(TILE_F * TILE_R * TILE_C, dtype=jnp.int32)
    frame_of = positions // (TILE_R * TILE_C)
    row_of = positions // TILE_C % TILE_R
    frame_ok = frame_of < extent_pair[0][..., None]
    row_ok = row_of < extent_pair[1][..., None]
    return jnp.logical_and(frame_ok, row_ok)


def shift_pairs(devices, step):
    return [(i, i + step) for i in range(devices) if 0 <= i + step < devices]


def gather_text(text_kv, devices):
    position = lax.axis_index("tm")
    gathered = text_kv
    step = 1
    while step < devices:
        other = lax.ppermute(gathered, "tm", [(i, i ^ step) for i in range(devices)])
        low_first = jnp.concatenate([gathered, other], axis=1)
        high_first = jnp.concatenate([other, gathered], axis=1)
        gathered = jnp.where((position & step) == 0, low_first, high_first)
        step *= 2
    return gathered


def make_kernel(blocks, has_text, has_state, final):
    count = len(blocks)

    def kernel(reach_ref, q_ref, *rest):
        rest = list(rest)
        text_ref = rest.pop(0) if has_text else None
        tile_refs = rest[:count]
        rest = rest[count:]
        bias_ref = rest.pop(0)
        if has_state:
            m_in, l_in, acc_in = rest[:3]
            rest = rest[3:]
        if final:
            qvalid_ref = rest.pop(0)
            o_ref = rest.pop(0)
        else:
            m_out, l_out, acc_out = rest[:3]
            rest = rest[3:]
        m_ref, l_ref, acc_ref = rest
        head = pl.program_id(0)
        scale = 1.0 / math.sqrt(HD)
        q = q_ref[...]
        dims = (((1,), (1,)), ((), ()))
        if has_state:
            m_ref[...] = m_in[...]
            l_ref[...] = l_in[...]
            acc_ref[...] = acc_in[...]
        else:
            m_ref[...] = jnp.full(m_ref.shape, NEG, jnp.float32)
            l_ref[...] = jnp.zeros(l_ref.shape, jnp.float32)
            acc_ref[...] = jnp.zeros(acc_ref.shape, jnp.float32)
        if has_text:
            s = lax.dot_general(q, text_ref[0], dims, preferred_element_type=jnp.float32) * scale
            m_old = m_ref[...]
            m_new = jnp.maximum(m_old, jnp.max(s, axis=1, keepdims=True))
            alpha = jnp.exp(m_old - m_new)
            p = jnp.exp(s - m_new)
            l_ref[...] = alpha * l_ref[...] + jnp.sum(p, axis=1, keepdims=True)
            acc_ref[...] = alpha * acc_ref[...] + jnp.dot(
                p.astype(jnp.bfloat16), text_ref[1], preferred_element_type=jnp.float32
            )
            m_ref[...] = m_new
        reach_t = reach_ref[head, 0]
        reach_h = reach_ref[head, 1]
        for tile_ref, b in zip(tile_refs, blocks):
            off_t, off_h = abs(b // 3 - 1), abs(b % 3 - 1)

            def block(tile_ref=tile_ref, b=b):
                s = lax.dot_general(q, tile_ref[0], dims, preferred_element_type=jnp.float32)
                s = s * scale + bias_ref[b]
                m_old = m_ref[...]
                m_new = jnp.maximum(m_old, jnp.max(s, axis=1, keepdims=True))
                alpha = jnp.exp(m_old - m_new)
                p = jnp.exp(s - m_new)
                l_ref[...] = alpha * l_ref[...] + jnp.sum(p, axis=1, keepdims=True)
                acc_ref[...] = alpha * acc_ref[...] + jnp.dot(
                    p.astype(jnp.bfloat16), tile_ref[1], preferred_element_type=jnp.float32
                )
                m_ref[...] = m_new

            if off_t == 0 and off_h == 0:
                block()
            else:
                pl.when(jnp.logical_and(reach_t >= off_t, reach_h >= off_h))(block)
        if final:
            out = acc_ref[...] / l_ref[...]
            out = jnp.where(qvalid_ref[...] > 0, out, 0.0)
            o_ref[...] = out.astype(o_ref.dtype)
        else:
            m_out[...] = m_ref[...]
            l_out[...] = l_ref[...]
            acc_out[...] = acc_ref[...]

    return kernel


def attend(reach, queries, text, tiles, bias, state=None, qvalid=None):
    tile_len, col_width = queries.shape
    heads = col_width // HD
    blocks = [b for _, _, b in tiles]
    specs = [pl.BlockSpec((tile_len, HD), lambda h, r: (0, h))]
    args = [queries]
    if text is not None:
        specs.append(pl.BlockSpec((2, text.shape[1], HD), lambda h, r: (0, 0, h)))
        args.append(text)
    for array, index, _ in tiles:
        if index is None:
            specs.append(pl.BlockSpec((2, tile_len, HD), lambda h, r: (0, 0, h)))
        else:
            specs.append(
                pl.BlockSpec((None, 2, tile_len, HD), lambda h, r, i=index: (i, 0, 0, h))
            )
        args.append(array)
    specs.append(pl.BlockSpec(bias.shape, lambda h, r: (0, 0, 0)))
    args.append(bias)
    row_spec = pl.BlockSpec((None, tile_len, 1), lambda h, r: (h, 0, 0))
    acc_spec = pl.BlockSpec((tile_len, HD), lambda h, r: (0, h))
    if state is not None:
        specs += [row_spec, row_spec, acc_spec]
        args += list(state)
    final = qvalid is not None
    if final:
        specs.append(pl.BlockSpec(qvalid.shape, lambda h, r: (0, 0)))
        args.append(qvalid)
        out_specs = pl.BlockSpec((tile_len, HD), lambda h, r: (0, h))
        out_shape = jax.ShapeDtypeStruct((tile_len, col_width), jnp.bfloat16)
    else:
        out_specs = [row_spec, row_spec, acc_spec]
        row_shape = jax.ShapeDtypeStruct((heads, tile_len, 1), jnp.float32)
        out_shape = [row_shape, row_shape, jax.ShapeDtypeStruct((tile_len, col_width), jnp.float32)]
    grid_spec = pltpu.PrefetchScalarGridSpec(
        num_scalar_prefetch=1,
        grid=(heads,),
        in_specs=specs,
        out_specs=out_specs,
        scratch_shapes=[
            pltpu.VMEM((tile_len, 1), jnp.float32),
            pltpu.VMEM((tile_len, 1), jnp.float32),
            pltpu.VMEM((tile_len, HD), jnp.float32),
        ],
    )
    kernel = make_kernel(blocks, text is not None, state is not None, final)
    return pl.pallas_call(kernel, grid_spec=grid_spec, out_shape=out_shape)(reach, *args)


def per_device(image_q, image_kv, text_kv, residual, out_weight, out_gate, head_reach, tile_extent):
    tile_len = image_q.shape[2]
    col_width = image_q.shape[3]
    tm_size = lax.axis_size("tm")
    height_size = lax.axis_size("height")
    mp_size = lax.axis_size("mp")

    own = image_kv[0, 0]
    t_before = lax.ppermute(own, "tm", shift_pairs(tm_size, 1))
    t_after = lax.ppermute(own, "tm", shift_pairs(tm_size, -1))
    h_before = lax.ppermute(own, "height", shift_pairs(height_size, 1))
    h_after = lax.ppermute(own, "height", shift_pairs(height_size, -1))
    text = gather_text(text_kv, tm_size)
    time_start = lax.axis_index("tm")
    height_start = lax.axis_index("height")
    zero_index = jnp.int32(0)
    padded_ext = jnp.pad(tile_extent, ((0, 0), (1, 1), (1, 1)))
    local_ext = lax.dynamic_slice(padded_ext, (zero_index, time_start, height_start), (2, 3, 3))
    key_valid = token_masks(local_ext)
    bias = jnp.where(key_valid, 0.0, NEG).astype(jnp.float32).reshape(9, 1, tile_len)
    qvalid = key_valid[1, 1].astype(jnp.float32).reshape(tile_len, 1)

    queries = image_q[0, 0]
    near = [(own, None, 4), (h_before, None, 3), (h_after, None, 5)]
    state = attend(head_reach, queries, None, near, bias)
    t_before, t_after, state = lax.optimization_barrier((t_before, t_after, state))
    time_pair = jnp.stack([t_before, t_after])
    c_before = lax.ppermute(time_pair, "height", shift_pairs(height_size, 1))
    c_after = lax.ppermute(time_pair, "height", shift_pairs(height_size, -1))
    across = [(t_before, None, 1), (t_after, None, 7)]
    state = attend(head_reach, queries, text, across, bias, state)
    corners = [(c_before, 0, 0), (c_after, 0, 2), (c_before, 1, 6), (c_after, 1, 8)]
    attended = attend(head_reach, queries, None, corners, bias, state, qvalid)

    mp_index = lax.axis_index("mp")
    chunk = out_weight.shape[1] // mp_size
    received = []
    for step in (2, 1, 3):
        target = (mp_index + step) % mp_size
        w_part = lax.dynamic_slice_in_dim(out_weight, target * chunk, chunk, 1)
        part = jnp.dot(attended, w_part, preferred_element_type=jnp.float32).astype(jnp.bfloat16)
        pairs = [(i, (i + step) % mp_size) for i in range(mp_size)]
        received.append(lax.ppermute(part, "mp", pairs))
    w_own = lax.dynamic_slice_in_dim(out_weight, mp_index * chunk, chunk, 1)
    branch = jnp.dot(attended, w_own, preferred_element_type=jnp.float32).astype(jnp.bfloat16)
    branch = branch.astype(jnp.float32)
    for part in received:
        branch = branch + part.astype(jnp.float32)
    updated = residual[0, 0].astype(jnp.float32) + out_gate * branch
    return updated.astype(jnp.bfloat16)[None, None]


def solution(mesh):
    return jax.shard_map(
        per_device,
        mesh=mesh,
        in_specs=(
            P("tm", "height", None, "mp"),
            P("tm", "height", None, None, "mp"),
            P(None, "tm", "mp"),
            P("tm", "height", None, "mp"),
            P("mp", None),
            P("mp"),
            P("mp", None),
            P(),
        ),
        out_specs=P("tm", "height", None, "mp"),
        check_vma=False,
    )
```

```python
import math

import jax
import jax.numpy as jnp
from jax import lax
from jax.experimental import pallas as pl
from jax.experimental.pallas import tpu as pltpu
from jax.sharding import PartitionSpec as P

HD = 128
TXT = 256
TILE_F = 6
TILE_R = 8
TILE_C = 8
NEG = -1e30


def token_masks(extent_pair):
    positions = jnp.arange(TILE_F * TILE_R * TILE_C, dtype=jnp.int32)
    frame_of = positions // (TILE_R * TILE_C)
    row_of = positions // TILE_C % TILE_R
    frame_ok = frame_of < extent_pair[0][..., None]
    row_ok = row_of < extent_pair[1][..., None]
    return jnp.logical_and(frame_ok, row_ok)


def shift_pairs(devices, step):
    return [(i, i + step) for i in range(devices) if 0 <= i + step < devices]


def gather_text(text_kv, devices):
    position = lax.axis_index("tm")
    gathered = text_kv
    step = 1
    while step < devices:
        other = lax.ppermute(gathered, "tm", [(i, i ^ step) for i in range(devices)])
        low_first = jnp.concatenate([gathered, other], axis=1)
        high_first = jnp.concatenate([other, gathered], axis=1)
        gathered = jnp.where((position & step) == 0, low_first, high_first)
        step *= 2
    return gathered


def make_kernel(blocks, has_text, has_state, final):
    count = len(blocks)

    def kernel(reach_ref, q_ref, *rest):
        rest = list(rest)
        text_ref = rest.pop(0) if has_text else None
        tile_refs = rest[:count]
        rest = rest[count:]
        bias_ref = rest.pop(0)
        if has_state:
            m_in, l_in, acc_in = rest[:3]
            rest = rest[3:]
        if final:
            qvalid_ref = rest.pop(0)
            o_ref = rest.pop(0)
        else:
            m_out, l_out, acc_out = rest[:3]
            rest = rest[3:]
        m_ref, l_ref, acc_ref = rest
        head = pl.program_id(0)
        scale = 1.0 / math.sqrt(HD)
        q = q_ref[...]
        dims = (((1,), (1,)), ((), ()))
        if has_state:
            m_ref[...] = m_in[...]
            l_ref[...] = l_in[...]
            acc_ref[...] = acc_in[...]
        else:
            m_ref[...] = jnp.full(m_ref.shape, NEG, jnp.float32)
            l_ref[...] = jnp.zeros(l_ref.shape, jnp.float32)
            acc_ref[...] = jnp.zeros(acc_ref.shape, jnp.float32)
        if has_text:
            s = lax.dot_general(q, text_ref[0], dims, preferred_element_type=jnp.float32) * scale
            m_old = m_ref[...]
            m_new = jnp.maximum(m_old, jnp.max(s, axis=1, keepdims=True))
            alpha = jnp.exp(m_old - m_new)
            p = jnp.exp(s - m_new)
            l_ref[...] = alpha * l_ref[...] + jnp.sum(p, axis=1, keepdims=True)
            acc_ref[...] = alpha * acc_ref[...] + jnp.dot(
                p.astype(jnp.bfloat16), text_ref[1], preferred_element_type=jnp.float32
            )
            m_ref[...] = m_new
        reach_t = reach_ref[head, 0]
        reach_h = reach_ref[head, 1]
        for tile_ref, b in zip(tile_refs, blocks):
            off_t, off_h = abs(b // 3 - 1), abs(b % 3 - 1)

            def block(tile_ref=tile_ref, b=b):
                s = lax.dot_general(q, tile_ref[0], dims, preferred_element_type=jnp.float32)
                s = s * scale + bias_ref[b]
                m_old = m_ref[...]
                m_new = jnp.maximum(m_old, jnp.max(s, axis=1, keepdims=True))
                alpha = jnp.exp(m_old - m_new)
                p = jnp.exp(s - m_new)
                l_ref[...] = alpha * l_ref[...] + jnp.sum(p, axis=1, keepdims=True)
                acc_ref[...] = alpha * acc_ref[...] + jnp.dot(
                    p.astype(jnp.bfloat16), tile_ref[1], preferred_element_type=jnp.float32
                )
                m_ref[...] = m_new

            if off_t == 0 and off_h == 0:
                block()
            else:
                pl.when(jnp.logical_and(reach_t >= off_t, reach_h >= off_h))(block)
        if final:
            out = acc_ref[...] / l_ref[...]
            out = jnp.where(qvalid_ref[...] > 0, out, 0.0)
            o_ref[...] = out.astype(o_ref.dtype)
        else:
            m_out[...] = m_ref[...]
            l_out[...] = l_ref[...]
            acc_out[...] = acc_ref[...]

    return kernel


def attend(reach, queries, text, tiles, bias, state=None, qvalid=None):
    tile_len, col_width = queries.shape
    heads = col_width // HD
    blocks = [b for _, _, b in tiles]
    specs = [pl.BlockSpec((tile_len, HD), lambda h, r: (0, h))]
    args = [queries]
    if text is not None:
        specs.append(pl.BlockSpec((2, text.shape[1], HD), lambda h, r: (0, 0, h)))
        args.append(text)
    for array, index, _ in tiles:
        if index is None:
            specs.append(pl.BlockSpec((2, tile_len, HD), lambda h, r: (0, 0, h)))
        else:
            specs.append(
                pl.BlockSpec((None, 2, tile_len, HD), lambda h, r, i=index: (i, 0, 0, h))
            )
        args.append(array)
    specs.append(pl.BlockSpec(bias.shape, lambda h, r: (0, 0, 0)))
    args.append(bias)
    row_spec = pl.BlockSpec((None, tile_len, 1), lambda h, r: (h, 0, 0))
    acc_spec = pl.BlockSpec((tile_len, HD), lambda h, r: (0, h))
    if state is not None:
        specs += [row_spec, row_spec, acc_spec]
        args += list(state)
    final = qvalid is not None
    if final:
        specs.append(pl.BlockSpec(qvalid.shape, lambda h, r: (0, 0)))
        args.append(qvalid)
        out_specs = pl.BlockSpec((tile_len, HD), lambda h, r: (0, h))
        out_shape = jax.ShapeDtypeStruct((tile_len, col_width), jnp.bfloat16)
    else:
        out_specs = [row_spec, row_spec, acc_spec]
        row_shape = jax.ShapeDtypeStruct((heads, tile_len, 1), jnp.float32)
        out_shape = [row_shape, row_shape, jax.ShapeDtypeStruct((tile_len, col_width), jnp.float32)]
    grid_spec = pltpu.PrefetchScalarGridSpec(
        num_scalar_prefetch=1,
        grid=(heads,),
        in_specs=specs,
        out_specs=out_specs,
        scratch_shapes=[
            pltpu.VMEM((tile_len, 1), jnp.float32),
            pltpu.VMEM((tile_len, 1), jnp.float32),
            pltpu.VMEM((tile_len, HD), jnp.float32),
        ],
    )
    kernel = make_kernel(blocks, text is not None, state is not None, final)
    return pl.pallas_call(kernel, grid_spec=grid_spec, out_shape=out_shape)(reach, *args)


def per_device(image_q, image_kv, text_kv, residual, out_weight, out_gate, head_reach, tile_extent):
    tile_len = image_q.shape[2]
    col_width = image_q.shape[3]
    tm_size = lax.axis_size("tm")
    height_size = lax.axis_size("height")
    mp_size = lax.axis_size("mp")

    own = image_kv[0, 0]
    t_before = lax.ppermute(own, "tm", shift_pairs(tm_size, 1))
    t_after = lax.ppermute(own, "tm", shift_pairs(tm_size, -1))
    h_before = lax.ppermute(own, "height", shift_pairs(height_size, 1))
    h_after = lax.ppermute(own, "height", shift_pairs(height_size, -1))
    text = gather_text(text_kv, tm_size)
    time_start = lax.axis_index("tm")
    height_start = lax.axis_index("height")
    zero_index = jnp.int32(0)
    padded_ext = jnp.pad(tile_extent, ((0, 0), (1, 1), (1, 1)))
    local_ext = lax.dynamic_slice(padded_ext, (zero_index, time_start, height_start), (2, 3, 3))
    key_valid = token_masks(local_ext)
    bias = jnp.where(key_valid, 0.0, NEG).astype(jnp.float32).reshape(9, 1, tile_len)
    qvalid = key_valid[1, 1].astype(jnp.float32).reshape(tile_len, 1)

    queries = image_q[0, 0]
    near = [(own, None, 4), (h_before, None, 3), (h_after, None, 5)]
    state = attend(head_reach, queries, text, near, bias)
    t_before, t_after, state = lax.optimization_barrier((t_before, t_after, state))
    time_pair = jnp.stack([t_before, t_after])
    c_before = lax.ppermute(time_pair, "height", shift_pairs(height_size, 1))
    c_after = lax.ppermute(time_pair, "height", shift_pairs(height_size, -1))
    across = [(t_before, None, 1), (t_after, None, 7)]
    state = attend(head_reach, queries, None, across, bias, state)
    corners = [(c_before, 0, 0), (c_after, 0, 2), (c_before, 1, 6), (c_after, 1, 8)]
    attended = attend(head_reach, queries, None, corners, bias, state, qvalid)

    mp_index = lax.axis_index("mp")
    chunk = out_weight.shape[1] // mp_size
    received = []
    for step in (2, 1, 3):
        target = (mp_index + step) % mp_size
        w_part = lax.dynamic_slice_in_dim(out_weight, target * chunk, chunk, 1)
        part = jnp.dot(attended, w_part, preferred_element_type=jnp.float32).astype(jnp.bfloat16)
        pairs = [(i, (i + step) % mp_size) for i in range(mp_size)]
        received.append(lax.ppermute(part, "mp", pairs))
    w_own = lax.dynamic_slice_in_dim(out_weight, mp_index * chunk, chunk, 1)
    branch = jnp.dot(attended, w_own, preferred_element_type=jnp.float32).astype(jnp.bfloat16)
    branch = branch.astype(jnp.float32)
    for part in received:
        branch = branch + part.astype(jnp.float32)
    updated = residual[0, 0].astype(jnp.float32) + out_gate * branch
    return updated.astype(jnp.bfloat16)[None, None]


def solution(mesh):
    return jax.shard_map(
        per_device,
        mesh=mesh,
        in_specs=(
            P("tm", "height", None, "mp"),
            P("tm", "height", None, None, "mp"),
            P(None, "tm", "mp"),
            P("tm", "height", None, "mp"),
            P("mp", None),
            P("mp"),
            P("mp", None),
            P(),
        ),
        out_specs=P("tm", "height", None, "mp"),
        check_vma=False,
    )
```

```python
import math

import jax
import jax.numpy as jnp
from jax import lax
from jax.experimental import pallas as pl
from jax.experimental.pallas import tpu as pltpu
from jax.sharding import PartitionSpec as P

HD = 128
TXT = 256
TILE_F = 6
TILE_R = 8
TILE_C = 8
NEG = -1e30
OFFLOAD_BYTES = 1 << 20


def token_masks(extent_pair):
    positions = jnp.arange(TILE_F * TILE_R * TILE_C, dtype=jnp.int32)
    frame_of = positions // (TILE_R * TILE_C)
    row_of = positions // TILE_C % TILE_R
    frame_ok = frame_of < extent_pair[0][..., None]
    row_ok = row_of < extent_pair[1][..., None]
    return jnp.logical_and(frame_ok, row_ok)


def shift_pairs(devices, step):
    return [(i, i + step) for i in range(devices) if 0 <= i + step < devices]


def gather_text(text_kv, devices):
    tokens = text_kv.shape[1]
    shard_bytes = 2 * text_kv.shape[2] * text_kv.dtype.itemsize
    padded = max(tokens, -(-OFFLOAD_BYTES // (devices * shard_bytes)))
    padded = -(-padded // 2) * 2
    grown = jnp.pad(text_kv, ((0, 0), (0, padded - tokens), (0, 0)))
    gathered = lax.all_gather(grown, "tm", axis=0)[:, :, :tokens]
    return jnp.transpose(gathered, (1, 0, 2, 3)).reshape(2, -1, text_kv.shape[2])


def make_kernel(blocks, has_text, has_state, final):
    count = len(blocks)

    def kernel(reach_ref, q_ref, *rest):
        rest = list(rest)
        text_ref = rest.pop(0) if has_text else None
        tile_refs = rest[:count]
        rest = rest[count:]
        bias_ref = rest.pop(0)
        if has_state:
            m_in, l_in, acc_in = rest[:3]
            rest = rest[3:]
        if final:
            qvalid_ref = rest.pop(0)
            o_ref = rest.pop(0)
        else:
            m_out, l_out, acc_out = rest[:3]
            rest = rest[3:]
        m_ref, l_ref, acc_ref = rest
        head = pl.program_id(0)
        scale = 1.0 / math.sqrt(HD)
        q = q_ref[...]
        dims = (((1,), (1,)), ((), ()))
        if has_state:
            m_ref[...] = m_in[...]
            l_ref[...] = l_in[...]
            acc_ref[...] = acc_in[...]
        else:
            m_ref[...] = jnp.full(m_ref.shape, NEG, jnp.float32)
            l_ref[...] = jnp.zeros(l_ref.shape, jnp.float32)
            acc_ref[...] = jnp.zeros(acc_ref.shape, jnp.float32)
        if has_text:
            s = lax.dot_general(q, text_ref[0], dims, preferred_element_type=jnp.float32) * scale
            m_old = m_ref[...]
            m_new = jnp.maximum(m_old, jnp.max(s, axis=1, keepdims=True))
            alpha = jnp.exp(m_old - m_new)
            p = jnp.exp(s - m_new)
            l_ref[...] = alpha * l_ref[...] + jnp.sum(p, axis=1, keepdims=True)
            acc_ref[...] = alpha * acc_ref[...] + jnp.dot(
                p.astype(jnp.bfloat16), text_ref[1], preferred_element_type=jnp.float32
            )
            m_ref[...] = m_new
        reach_t = reach_ref[head, 0]
        reach_h = reach_ref[head, 1]
        for tile_ref, b in zip(tile_refs, blocks):
            off_t, off_h = abs(b // 3 - 1), abs(b % 3 - 1)

            def block(tile_ref=tile_ref, b=b):
                s = lax.dot_general(q, tile_ref[0], dims, preferred_element_type=jnp.float32)
                s = s * scale + bias_ref[b]
                m_old = m_ref[...]
                m_new = jnp.maximum(m_old, jnp.max(s, axis=1, keepdims=True))
                alpha = jnp.exp(m_old - m_new)
                p = jnp.exp(s - m_new)
                l_ref[...] = alpha * l_ref[...] + jnp.sum(p, axis=1, keepdims=True)
                acc_ref[...] = alpha * acc_ref[...] + jnp.dot(
                    p.astype(jnp.bfloat16), tile_ref[1], preferred_element_type=jnp.float32
                )
                m_ref[...] = m_new

            if off_t == 0 and off_h == 0:
                block()
            else:
                pl.when(jnp.logical_and(reach_t >= off_t, reach_h >= off_h))(block)
        if final:
            out = acc_ref[...] / l_ref[...]
            out = jnp.where(qvalid_ref[...] > 0, out, 0.0)
            o_ref[...] = out.astype(o_ref.dtype)
        else:
            m_out[...] = m_ref[...]
            l_out[...] = l_ref[...]
            acc_out[...] = acc_ref[...]

    return kernel


def attend(reach, queries, text, tiles, bias, state=None, qvalid=None):
    tile_len, col_width = queries.shape
    heads = col_width // HD
    blocks = [b for _, _, b in tiles]
    specs = [pl.BlockSpec((tile_len, HD), lambda h, r: (0, h))]
    args = [queries]
    if text is not None:
        specs.append(pl.BlockSpec((2, text.shape[1], HD), lambda h, r: (0, 0, h)))
        args.append(text)
    for array, index, _ in tiles:
        if index is None:
            specs.append(pl.BlockSpec((2, tile_len, HD), lambda h, r: (0, 0, h)))
        else:
            specs.append(
                pl.BlockSpec((None, 2, tile_len, HD), lambda h, r, i=index: (i, 0, 0, h))
            )
        args.append(array)
    specs.append(pl.BlockSpec(bias.shape, lambda h, r: (0, 0, 0)))
    args.append(bias)
    row_spec = pl.BlockSpec((None, tile_len, 1), lambda h, r: (h, 0, 0))
    acc_spec = pl.BlockSpec((tile_len, HD), lambda h, r: (0, h))
    if state is not None:
        specs += [row_spec, row_spec, acc_spec]
        args += list(state)
    final = qvalid is not None
    if final:
        specs.append(pl.BlockSpec(qvalid.shape, lambda h, r: (0, 0)))
        args.append(qvalid)
        out_specs = pl.BlockSpec((tile_len, HD), lambda h, r: (0, h))
        out_shape = jax.ShapeDtypeStruct((tile_len, col_width), jnp.bfloat16)
    else:
        out_specs = [row_spec, row_spec, acc_spec]
        row_shape = jax.ShapeDtypeStruct((heads, tile_len, 1), jnp.float32)
        out_shape = [row_shape, row_shape, jax.ShapeDtypeStruct((tile_len, col_width), jnp.float32)]
    grid_spec = pltpu.PrefetchScalarGridSpec(
        num_scalar_prefetch=1,
        grid=(heads,),
        in_specs=specs,
        out_specs=out_specs,
        scratch_shapes=[
            pltpu.VMEM((tile_len, 1), jnp.float32),
            pltpu.VMEM((tile_len, 1), jnp.float32),
            pltpu.VMEM((tile_len, HD), jnp.float32),
        ],
    )
    kernel = make_kernel(blocks, text is not None, state is not None, final)
    return pl.pallas_call(kernel, grid_spec=grid_spec, out_shape=out_shape)(reach, *args)


def per_device(image_q, image_kv, text_kv, residual, out_weight, out_gate, head_reach, tile_extent):
    tile_len = image_q.shape[2]
    col_width = image_q.shape[3]
    tm_size = lax.axis_size("tm")
    height_size = lax.axis_size("height")
    mp_size = lax.axis_size("mp")

    own = image_kv[0, 0]
    t_before = lax.ppermute(own, "tm", shift_pairs(tm_size, 1))
    t_after = lax.ppermute(own, "tm", shift_pairs(tm_size, -1))
    h_before = lax.ppermute(own, "height", shift_pairs(height_size, 1))
    h_after = lax.ppermute(own, "height", shift_pairs(height_size, -1))
    text = gather_text(text_kv, tm_size)
    time_start = lax.axis_index("tm")
    height_start = lax.axis_index("height")
    zero_index = jnp.int32(0)
    padded_ext = jnp.pad(tile_extent, ((0, 0), (1, 1), (1, 1)))
    local_ext = lax.dynamic_slice(padded_ext, (zero_index, time_start, height_start), (2, 3, 3))
    key_valid = token_masks(local_ext)
    bias = jnp.where(key_valid, 0.0, NEG).astype(jnp.float32).reshape(9, 1, tile_len)
    qvalid = key_valid[1, 1].astype(jnp.float32).reshape(tile_len, 1)

    queries = image_q[0, 0]
    near = [(own, None, 4), (h_before, None, 3), (h_after, None, 5)]
    state = attend(head_reach, queries, text, near, bias)
    t_before, t_after, state = lax.optimization_barrier((t_before, t_after, state))
    time_pair = jnp.stack([t_before, t_after])
    c_before = lax.ppermute(time_pair, "height", shift_pairs(height_size, 1))
    c_after = lax.ppermute(time_pair, "height", shift_pairs(height_size, -1))
    across = [(t_before, None, 1), (t_after, None, 7)]
    state = attend(head_reach, queries, None, across, bias, state)
    corners = [(c_before, 0, 0), (c_after, 0, 2), (c_before, 1, 6), (c_after, 1, 8)]
    attended = attend(head_reach, queries, None, corners, bias, state, qvalid)

    mp_index = lax.axis_index("mp")
    chunk = out_weight.shape[1] // mp_size
    received = []
    for step in (2, 1, 3):
        target = (mp_index + step) % mp_size
        w_part = lax.dynamic_slice_in_dim(out_weight, target * chunk, chunk, 1)
        part = jnp.dot(attended, w_part, preferred_element_type=jnp.float32).astype(jnp.bfloat16)
        pairs = [(i, (i + step) % mp_size) for i in range(mp_size)]
        received.append(lax.ppermute(part, "mp", pairs))
    w_own = lax.dynamic_slice_in_dim(out_weight, mp_index * chunk, chunk, 1)
    branch = jnp.dot(attended, w_own, preferred_element_type=jnp.float32).astype(jnp.bfloat16)
    branch = branch.astype(jnp.float32)
    for part in received:
        branch = branch + part.astype(jnp.float32)
    updated = residual[0, 0].astype(jnp.float32) + out_gate * branch
    return updated.astype(jnp.bfloat16)[None, None]


def solution(mesh):
    return jax.shard_map(
        per_device,
        mesh=mesh,
        in_specs=(
            P("tm", "height", None, "mp"),
            P("tm", "height", None, None, "mp"),
            P(None, "tm", "mp"),
            P("tm", "height", None, "mp"),
            P("mp", None),
            P("mp"),
            P("mp", None),
            P(),
        ),
        out_specs=P("tm", "height", None, "mp"),
        check_vma=False,
    )
```

```python
import math

import jax
import jax.numpy as jnp
from jax import lax
from jax.experimental import pallas as pl
from jax.experimental.pallas import tpu as pltpu
from jax.sharding import PartitionSpec as P

HD = 128
TXT = 256
TILE_F = 6
TILE_R = 8
TILE_C = 8
NEG = -1e30


def token_masks(extent_pair):
    positions = jnp.arange(TILE_F * TILE_R * TILE_C, dtype=jnp.int32)
    frame_of = positions // (TILE_R * TILE_C)
    row_of = positions // TILE_C % TILE_R
    frame_ok = frame_of < extent_pair[0][..., None]
    row_ok = row_of < extent_pair[1][..., None]
    return jnp.logical_and(frame_ok, row_ok)


def shift_pairs(devices, step):
    return [(i, i + step) for i in range(devices) if 0 <= i + step < devices]


def text_halves(text_kv):
    half_width = text_kv.shape[2] // 2
    half = lax.axis_index("height") % 2
    return lax.dynamic_slice_in_dim(text_kv, half * half_width, half_width, 2)


def exchange(block, devices, steps):
    parts = [block]
    for step in steps:
        parts.append(lax.ppermute(block, "tm", [(i, i ^ step) for i in range(devices)]))
    return jnp.concatenate(parts, axis=1)


def join_halves(mine):
    half = lax.axis_index("height") % 2
    pairs = [(i, i ^ 1) for i in range(lax.axis_size("height"))]
    other = lax.ppermute(mine, "height", pairs)
    low_first = jnp.concatenate([mine, other], axis=2)
    high_first = jnp.concatenate([other, mine], axis=2)
    return jnp.where(half == 0, low_first, high_first)


def make_kernel(blocks, has_text, has_state, final):
    count = len(blocks)

    def kernel(reach_ref, q_ref, *rest):
        rest = list(rest)
        text_ref = rest.pop(0) if has_text else None
        tile_refs = rest[:count]
        rest = rest[count:]
        bias_ref = rest.pop(0)
        if has_state:
            m_in, l_in, acc_in = rest[:3]
            rest = rest[3:]
        if final:
            qvalid_ref = rest.pop(0)
            o_ref = rest.pop(0)
        else:
            m_out, l_out, acc_out = rest[:3]
            rest = rest[3:]
        m_ref, l_ref, acc_ref = rest
        head = pl.program_id(0)
        scale = 1.0 / math.sqrt(HD)
        q = q_ref[...]
        dims = (((1,), (1,)), ((), ()))
        if has_state:
            m_ref[...] = m_in[...]
            l_ref[...] = l_in[...]
            acc_ref[...] = acc_in[...]
        else:
            m_ref[...] = jnp.full(m_ref.shape, NEG, jnp.float32)
            l_ref[...] = jnp.zeros(l_ref.shape, jnp.float32)
            acc_ref[...] = jnp.zeros(acc_ref.shape, jnp.float32)
        if has_text:
            s = lax.dot_general(q, text_ref[0], dims, preferred_element_type=jnp.float32) * scale
            m_old = m_ref[...]
            m_new = jnp.maximum(m_old, jnp.max(s, axis=1, keepdims=True))
            alpha = jnp.exp(m_old - m_new)
            p = jnp.exp(s - m_new)
            l_ref[...] = alpha * l_ref[...] + jnp.sum(p, axis=1, keepdims=True)
            acc_ref[...] = alpha * acc_ref[...] + jnp.dot(
                p.astype(jnp.bfloat16), text_ref[1], preferred_element_type=jnp.float32
            )
            m_ref[...] = m_new
        reach_t = reach_ref[head, 0]
        reach_h = reach_ref[head, 1]
        for tile_ref, b in zip(tile_refs, blocks):
            off_t, off_h = abs(b // 3 - 1), abs(b % 3 - 1)

            def block(tile_ref=tile_ref, b=b):
                s = lax.dot_general(q, tile_ref[0], dims, preferred_element_type=jnp.float32)
                s = s * scale + bias_ref[b]
                m_old = m_ref[...]
                m_new = jnp.maximum(m_old, jnp.max(s, axis=1, keepdims=True))
                alpha = jnp.exp(m_old - m_new)
                p = jnp.exp(s - m_new)
                l_ref[...] = alpha * l_ref[...] + jnp.sum(p, axis=1, keepdims=True)
                acc_ref[...] = alpha * acc_ref[...] + jnp.dot(
                    p.astype(jnp.bfloat16), tile_ref[1], preferred_element_type=jnp.float32
                )
                m_ref[...] = m_new

            if off_t == 0 and off_h == 0:
                block()
            else:
                pl.when(jnp.logical_and(reach_t >= off_t, reach_h >= off_h))(block)
        if final:
            out = acc_ref[...] / l_ref[...]
            out = jnp.where(qvalid_ref[...] > 0, out, 0.0)
            o_ref[...] = out.astype(o_ref.dtype)
        else:
            m_out[...] = m_ref[...]
            l_out[...] = l_ref[...]
            acc_out[...] = acc_ref[...]

    return kernel


def attend(reach, queries, text, tiles, bias, state=None, qvalid=None):
    tile_len, col_width = queries.shape
    heads = col_width // HD
    blocks = [b for _, _, b in tiles]
    specs = [pl.BlockSpec((tile_len, HD), lambda h, r: (0, h))]
    args = [queries]
    if text is not None:
        specs.append(pl.BlockSpec((2, text.shape[1], HD), lambda h, r: (0, 0, h)))
        args.append(text)
    for array, index, _ in tiles:
        if index is None:
            specs.append(pl.BlockSpec((2, tile_len, HD), lambda h, r: (0, 0, h)))
        else:
            specs.append(
                pl.BlockSpec((None, 2, tile_len, HD), lambda h, r, i=index: (i, 0, 0, h))
            )
        args.append(array)
    specs.append(pl.BlockSpec(bias.shape, lambda h, r: (0, 0, 0)))
    args.append(bias)
    row_spec = pl.BlockSpec((None, tile_len, 1), lambda h, r: (h, 0, 0))
    acc_spec = pl.BlockSpec((tile_len, HD), lambda h, r: (0, h))
    if state is not None:
        specs += [row_spec, row_spec, acc_spec]
        args += list(state)
    final = qvalid is not None
    if final:
        specs.append(pl.BlockSpec(qvalid.shape, lambda h, r: (0, 0)))
        args.append(qvalid)
        out_specs = pl.BlockSpec((tile_len, HD), lambda h, r: (0, h))
        out_shape = jax.ShapeDtypeStruct((tile_len, col_width), jnp.bfloat16)
    else:
        out_specs = [row_spec, row_spec, acc_spec]
        row_shape = jax.ShapeDtypeStruct((heads, tile_len, 1), jnp.float32)
        out_shape = [row_shape, row_shape, jax.ShapeDtypeStruct((tile_len, col_width), jnp.float32)]
    grid_spec = pltpu.PrefetchScalarGridSpec(
        num_scalar_prefetch=1,
        grid=(heads,),
        in_specs=specs,
        out_specs=out_specs,
        scratch_shapes=[
            pltpu.VMEM((tile_len, 1), jnp.float32),
            pltpu.VMEM((tile_len, 1), jnp.float32),
            pltpu.VMEM((tile_len, HD), jnp.float32),
        ],
    )
    kernel = make_kernel(blocks, text is not None, state is not None, final)
    return pl.pallas_call(kernel, grid_spec=grid_spec, out_shape=out_shape)(reach, *args)


def per_device(image_q, image_kv, text_kv, residual, out_weight, out_gate, head_reach, tile_extent):
    tile_len = image_q.shape[2]
    col_width = image_q.shape[3]
    tm_size = lax.axis_size("tm")
    height_size = lax.axis_size("height")
    mp_size = lax.axis_size("mp")

    own = image_kv[0, 0]
    t_before = lax.ppermute(own, "tm", shift_pairs(tm_size, 1))
    t_after = lax.ppermute(own, "tm", shift_pairs(tm_size, -1))
    h_before = lax.ppermute(own, "height", shift_pairs(height_size, 1))
    h_after = lax.ppermute(own, "height", shift_pairs(height_size, -1))
    text_group = exchange(text_halves(text_kv), tm_size, (1, 2, 3))
    time_start = lax.axis_index("tm")
    height_start = lax.axis_index("height")
    zero_index = jnp.int32(0)
    padded_ext = jnp.pad(tile_extent, ((0, 0), (1, 1), (1, 1)))
    local_ext = lax.dynamic_slice(padded_ext, (zero_index, time_start, height_start), (2, 3, 3))
    key_valid = token_masks(local_ext)
    bias = jnp.where(key_valid, 0.0, NEG).astype(jnp.float32).reshape(9, 1, tile_len)
    qvalid = key_valid[1, 1].astype(jnp.float32).reshape(tile_len, 1)

    queries = image_q[0, 0]
    near = [(own, None, 4), (h_before, None, 3), (h_after, None, 5)]
    state = attend(head_reach, queries, None, near, bias)
    text_group, state = lax.optimization_barrier((text_group, state))
    text = join_halves(exchange(text_group, tm_size, (4, 8, 12)))
    t_before, t_after, state = lax.optimization_barrier((t_before, t_after, state))
    time_pair = jnp.stack([t_before, t_after])
    c_before = lax.ppermute(time_pair, "height", shift_pairs(height_size, 1))
    c_after = lax.ppermute(time_pair, "height", shift_pairs(height_size, -1))
    across = [(t_before, None, 1), (t_after, None, 7)]
    state = attend(head_reach, queries, text, across, bias, state)
    corners = [(c_before, 0, 0), (c_after, 0, 2), (c_before, 1, 6), (c_after, 1, 8)]
    attended = attend(head_reach, queries, None, corners, bias, state, qvalid)

    mp_index = lax.axis_index("mp")
    chunk = out_weight.shape[1] // mp_size
    received = []
    for step in (2, 1, 3):
        target = (mp_index + step) % mp_size
        w_part = lax.dynamic_slice_in_dim(out_weight, target * chunk, chunk, 1)
        part = jnp.dot(attended, w_part, preferred_element_type=jnp.float32).astype(jnp.bfloat16)
        pairs = [(i, (i + step) % mp_size) for i in range(mp_size)]
        received.append(lax.ppermute(part, "mp", pairs))
    w_own = lax.dynamic_slice_in_dim(out_weight, mp_index * chunk, chunk, 1)
    branch = jnp.dot(attended, w_own, preferred_element_type=jnp.float32).astype(jnp.bfloat16)
    branch = branch.astype(jnp.float32)
    for part in received:
        branch = branch + part.astype(jnp.float32)
    updated = residual[0, 0].astype(jnp.float32) + out_gate * branch
    return updated.astype(jnp.bfloat16)[None, None]


def solution(mesh):
    return jax.shard_map(
        per_device,
        mesh=mesh,
        in_specs=(
            P("tm", "height", None, "mp"),
            P("tm", "height", None, None, "mp"),
            P(None, "tm", "mp"),
            P("tm", "height", None, "mp"),
            P("mp", None),
            P("mp"),
            P("mp", None),
            P(),
        ),
        out_specs=P("tm", "height", None, "mp"),
        check_vma=False,
    )
```

```python
import math

import jax
import jax.numpy as jnp
from jax import lax
from jax.experimental import pallas as pl
from jax.experimental.pallas import tpu as pltpu
from jax.sharding import PartitionSpec as P

HD = 128
TXT = 256
TILE_F = 6
TILE_R = 8
TILE_C = 8
NEG = -1e30


def token_masks(extent_pair):
    positions = jnp.arange(TILE_F * TILE_R * TILE_C, dtype=jnp.int32)
    frame_of = positions // (TILE_R * TILE_C)
    row_of = positions // TILE_C % TILE_R
    frame_ok = frame_of < extent_pair[0][..., None]
    row_ok = row_of < extent_pair[1][..., None]
    return jnp.logical_and(frame_ok, row_ok)


def shift_pairs(devices, step):
    return [(i, i + step) for i in range(devices) if 0 <= i + step < devices]


def text_halves(text_kv):
    half_width = text_kv.shape[2] // 2
    half = lax.axis_index("height") % 2
    return lax.dynamic_slice_in_dim(text_kv, half * half_width, half_width, 2)


def exchange(block, devices, step):
    position = lax.axis_index("tm")
    other = lax.ppermute(block, "tm", [(i, i ^ step) for i in range(devices)])
    low_first = jnp.concatenate([block, other], axis=1)
    high_first = jnp.concatenate([other, block], axis=1)
    return jnp.where((position & step) == 0, low_first, high_first)


def join_halves(mine):
    half = lax.axis_index("height") % 2
    pairs = [(i, i ^ 1) for i in range(lax.axis_size("height"))]
    other = lax.ppermute(mine, "height", pairs)
    low_first = jnp.concatenate([mine, other], axis=2)
    high_first = jnp.concatenate([other, mine], axis=2)
    return jnp.where(half == 0, low_first, high_first)


def make_kernel(blocks, has_text, has_state, final):
    count = len(blocks)

    def kernel(reach_ref, q_ref, *rest):
        rest = list(rest)
        text_ref = rest.pop(0) if has_text else None
        tile_refs = rest[:count]
        rest = rest[count:]
        bias_ref = rest.pop(0)
        if has_state:
            m_in, l_in, acc_in = rest[:3]
            rest = rest[3:]
        if final:
            qvalid_ref = rest.pop(0)
            o_ref = rest.pop(0)
        else:
            m_out, l_out, acc_out = rest[:3]
            rest = rest[3:]
        m_ref, l_ref, acc_ref = rest
        head = pl.program_id(0)
        scale = 1.0 / math.sqrt(HD)
        q = q_ref[...]
        dims = (((1,), (1,)), ((), ()))
        if has_state:
            m_ref[...] = m_in[...]
            l_ref[...] = l_in[...]
            acc_ref[...] = acc_in[...]
        else:
            m_ref[...] = jnp.full(m_ref.shape, NEG, jnp.float32)
            l_ref[...] = jnp.zeros(l_ref.shape, jnp.float32)
            acc_ref[...] = jnp.zeros(acc_ref.shape, jnp.float32)
        if has_text:
            s = lax.dot_general(q, text_ref[0], dims, preferred_element_type=jnp.float32) * scale
            m_old = m_ref[...]
            m_new = jnp.maximum(m_old, jnp.max(s, axis=1, keepdims=True))
            alpha = jnp.exp(m_old - m_new)
            p = jnp.exp(s - m_new)
            l_ref[...] = alpha * l_ref[...] + jnp.sum(p, axis=1, keepdims=True)
            acc_ref[...] = alpha * acc_ref[...] + jnp.dot(
                p.astype(jnp.bfloat16), text_ref[1], preferred_element_type=jnp.float32
            )
            m_ref[...] = m_new
        reach_t = reach_ref[head, 0]
        reach_h = reach_ref[head, 1]
        for tile_ref, b in zip(tile_refs, blocks):
            off_t, off_h = abs(b // 3 - 1), abs(b % 3 - 1)

            def block(tile_ref=tile_ref, b=b):
                s = lax.dot_general(q, tile_ref[0], dims, preferred_element_type=jnp.float32)
                s = s * scale + bias_ref[b]
                m_old = m_ref[...]
                m_new = jnp.maximum(m_old, jnp.max(s, axis=1, keepdims=True))
                alpha = jnp.exp(m_old - m_new)
                p = jnp.exp(s - m_new)
                l_ref[...] = alpha * l_ref[...] + jnp.sum(p, axis=1, keepdims=True)
                acc_ref[...] = alpha * acc_ref[...] + jnp.dot(
                    p.astype(jnp.bfloat16), tile_ref[1], preferred_element_type=jnp.float32
                )
                m_ref[...] = m_new

            if off_t == 0 and off_h == 0:
                block()
            else:
                pl.when(jnp.logical_and(reach_t >= off_t, reach_h >= off_h))(block)
        if final:
            out = acc_ref[...] / l_ref[...]
            out = jnp.where(qvalid_ref[...] > 0, out, 0.0)
            o_ref[...] = out.astype(o_ref.dtype)
        else:
            m_out[...] = m_ref[...]
            l_out[...] = l_ref[...]
            acc_out[...] = acc_ref[...]

    return kernel


def attend(reach, queries, text, tiles, bias, state=None, qvalid=None):
    tile_len, col_width = queries.shape
    heads = col_width // HD
    blocks = [b for _, _, b in tiles]
    specs = [pl.BlockSpec((tile_len, HD), lambda h, r: (0, h))]
    args = [queries]
    if text is not None:
        specs.append(pl.BlockSpec((2, text.shape[1], HD), lambda h, r: (0, 0, h)))
        args.append(text)
    for array, index, _ in tiles:
        if index is None:
            specs.append(pl.BlockSpec((2, tile_len, HD), lambda h, r: (0, 0, h)))
        else:
            specs.append(
                pl.BlockSpec((None, 2, tile_len, HD), lambda h, r, i=index: (i, 0, 0, h))
            )
        args.append(array)
    specs.append(pl.BlockSpec(bias.shape, lambda h, r: (0, 0, 0)))
    args.append(bias)
    row_spec = pl.BlockSpec((None, tile_len, 1), lambda h, r: (h, 0, 0))
    acc_spec = pl.BlockSpec((tile_len, HD), lambda h, r: (0, h))
    if state is not None:
        specs += [row_spec, row_spec, acc_spec]
        args += list(state)
    final = qvalid is not None
    if final:
        specs.append(pl.BlockSpec(qvalid.shape, lambda h, r: (0, 0)))
        args.append(qvalid)
        out_specs = pl.BlockSpec((tile_len, HD), lambda h, r: (0, h))
        out_shape = jax.ShapeDtypeStruct((tile_len, col_width), jnp.bfloat16)
    else:
        out_specs = [row_spec, row_spec, acc_spec]
        row_shape = jax.ShapeDtypeStruct((heads, tile_len, 1), jnp.float32)
        out_shape = [row_shape, row_shape, jax.ShapeDtypeStruct((tile_len, col_width), jnp.float32)]
    grid_spec = pltpu.PrefetchScalarGridSpec(
        num_scalar_prefetch=1,
        grid=(heads,),
        in_specs=specs,
        out_specs=out_specs,
        scratch_shapes=[
            pltpu.VMEM((tile_len, 1), jnp.float32),
            pltpu.VMEM((tile_len, 1), jnp.float32),
            pltpu.VMEM((tile_len, HD), jnp.float32),
        ],
    )
    kernel = make_kernel(blocks, text is not None, state is not None, final)
    return pl.pallas_call(kernel, grid_spec=grid_spec, out_shape=out_shape)(reach, *args)


def per_device(image_q, image_kv, text_kv, residual, out_weight, out_gate, head_reach, tile_extent):
    tile_len = image_q.shape[2]
    col_width = image_q.shape[3]
    tm_size = lax.axis_size("tm")
    height_size = lax.axis_size("height")
    mp_size = lax.axis_size("mp")

    own = image_kv[0, 0]
    h_before = lax.ppermute(own, "height", shift_pairs(height_size, 1))
    h_after = lax.ppermute(own, "height", shift_pairs(height_size, -1))
    text_group = text_halves(text_kv)
    step = 1
    while step < tm_size:
        text_group = exchange(text_group, tm_size, step)
        step *= 2
    text = join_halves(text_group)
    sent, text = lax.optimization_barrier((own, text))
    t_before = lax.ppermute(sent, "tm", shift_pairs(tm_size, 1))
    t_after = lax.ppermute(sent, "tm", shift_pairs(tm_size, -1))
    time_start = lax.axis_index("tm")
    height_start = lax.axis_index("height")
    zero_index = jnp.int32(0)
    padded_ext = jnp.pad(tile_extent, ((0, 0), (1, 1), (1, 1)))
    local_ext = lax.dynamic_slice(padded_ext, (zero_index, time_start, height_start), (2, 3, 3))
    key_valid = token_masks(local_ext)
    bias = jnp.where(key_valid, 0.0, NEG).astype(jnp.float32).reshape(9, 1, tile_len)
    qvalid = key_valid[1, 1].astype(jnp.float32).reshape(tile_len, 1)

    queries = image_q[0, 0]
    near = [(own, None, 4), (h_before, None, 3), (h_after, None, 5)]
    state = attend(head_reach, queries, None, near, bias)
    t_before, t_after, state = lax.optimization_barrier((t_before, t_after, state))
    time_pair = jnp.stack([t_before, t_after])
    c_before = lax.ppermute(time_pair, "height", shift_pairs(height_size, 1))
    c_after = lax.ppermute(time_pair, "height", shift_pairs(height_size, -1))
    across = [(t_before, None, 1), (t_after, None, 7)]
    state = attend(head_reach, queries, text, across, bias, state)
    corners = [(c_before, 0, 0), (c_after, 0, 2), (c_before, 1, 6), (c_after, 1, 8)]
    attended = attend(head_reach, queries, None, corners, bias, state, qvalid)

    mp_index = lax.axis_index("mp")
    chunk = out_weight.shape[1] // mp_size
    received = []
    for step in (2, 1, 3):
        target = (mp_index + step) % mp_size
        w_part = lax.dynamic_slice_in_dim(out_weight, target * chunk, chunk, 1)
        part = jnp.dot(attended, w_part, preferred_element_type=jnp.float32).astype(jnp.bfloat16)
        pairs = [(i, (i + step) % mp_size) for i in range(mp_size)]
        received.append(lax.ppermute(part, "mp", pairs))
    w_own = lax.dynamic_slice_in_dim(out_weight, mp_index * chunk, chunk, 1)
    branch = jnp.dot(attended, w_own, preferred_element_type=jnp.float32).astype(jnp.bfloat16)
    branch = branch.astype(jnp.float32)
    for part in received:
        branch = branch + part.astype(jnp.float32)
    updated = residual[0, 0].astype(jnp.float32) + out_gate * branch
    return updated.astype(jnp.bfloat16)[None, None]


def solution(mesh):
    return jax.shard_map(
        per_device,
        mesh=mesh,
        in_specs=(
            P("tm", "height", None, "mp"),
            P("tm", "height", None, None, "mp"),
            P(None, "tm", "mp"),
            P("tm", "height", None, "mp"),
            P("mp", None),
            P("mp"),
            P("mp", None),
            P(),
        ),
        out_specs=P("tm", "height", None, "mp"),
        check_vma=False,
    )
```

```python
import math

import jax
import jax.numpy as jnp
from jax import lax
from jax.experimental import pallas as pl
from jax.experimental.pallas import tpu as pltpu
from jax.sharding import PartitionSpec as P

HD = 128
TXT = 256
TILE_F = 6
TILE_R = 8
TILE_C = 8
NEG = -1e30


def token_masks(extent_pair):
    positions = jnp.arange(TILE_F * TILE_R * TILE_C, dtype=jnp.int32)
    frame_of = positions // (TILE_R * TILE_C)
    row_of = positions // TILE_C % TILE_R
    frame_ok = frame_of < extent_pair[0][..., None]
    row_ok = row_of < extent_pair[1][..., None]
    return jnp.logical_and(frame_ok, row_ok)


def shift_pairs(devices, step):
    return [(i, i + step) for i in range(devices) if 0 <= i + step < devices]


def text_halves(text_kv):
    half_width = text_kv.shape[2] // 2
    half = lax.axis_index("height") % 2
    return lax.dynamic_slice_in_dim(text_kv, half * half_width, half_width, 2)


def exchange(block, devices, group):
    position = lax.axis_index("tm")
    parts = [block]
    for offset in range(1, 4):
        step = offset * group
        parts.append(lax.ppermute(block, "tm", [(i, i ^ step) for i in range(devices)]))
    return jnp.concatenate(parts, axis=1)


def join_halves(mine):
    half = lax.axis_index("height") % 2
    pairs = [(i, i ^ 1) for i in range(lax.axis_size("height"))]
    other = lax.ppermute(mine, "height", pairs)
    low_first = jnp.concatenate([mine, other], axis=2)
    high_first = jnp.concatenate([other, mine], axis=2)
    return jnp.where(half == 0, low_first, high_first)


def make_kernel(blocks, has_text, has_state, final):
    count = len(blocks)

    def kernel(reach_ref, q_ref, *rest):
        rest = list(rest)
        text_ref = rest.pop(0) if has_text else None
        tile_refs = rest[:count]
        rest = rest[count:]
        bias_ref = rest.pop(0)
        if has_state:
            m_in, l_in, acc_in = rest[:3]
            rest = rest[3:]
        if final:
            qvalid_ref = rest.pop(0)
            o_ref = rest.pop(0)
        else:
            m_out, l_out, acc_out = rest[:3]
            rest = rest[3:]
        m_ref, l_ref, acc_ref = rest
        head = pl.program_id(0)
        scale = 1.0 / math.sqrt(HD)
        q = q_ref[...]
        dims = (((1,), (1,)), ((), ()))
        if has_state:
            m_ref[...] = m_in[...]
            l_ref[...] = l_in[...]
            acc_ref[...] = acc_in[...]
        else:
            m_ref[...] = jnp.full(m_ref.shape, NEG, jnp.float32)
            l_ref[...] = jnp.zeros(l_ref.shape, jnp.float32)
            acc_ref[...] = jnp.zeros(acc_ref.shape, jnp.float32)
        if has_text:
            s = lax.dot_general(q, text_ref[0], dims, preferred_element_type=jnp.float32) * scale
            m_old = m_ref[...]
            m_new = jnp.maximum(m_old, jnp.max(s, axis=1, keepdims=True))
            alpha = jnp.exp(m_old - m_new)
            p = jnp.exp(s - m_new)
            l_ref[...] = alpha * l_ref[...] + jnp.sum(p, axis=1, keepdims=True)
            acc_ref[...] = alpha * acc_ref[...] + jnp.dot(
                p.astype(jnp.bfloat16), text_ref[1], preferred_element_type=jnp.float32
            )
            m_ref[...] = m_new
        reach_t = reach_ref[head, 0]
        reach_h = reach_ref[head, 1]
        for tile_ref, b in zip(tile_refs, blocks):
            off_t, off_h = abs(b // 3 - 1), abs(b % 3 - 1)

            def block(tile_ref=tile_ref, b=b):
                s = lax.dot_general(q, tile_ref[0], dims, preferred_element_type=jnp.float32)
                s = s * scale + bias_ref[b]
                m_old = m_ref[...]
                m_new = jnp.maximum(m_old, jnp.max(s, axis=1, keepdims=True))
                alpha = jnp.exp(m_old - m_new)
                p = jnp.exp(s - m_new)
                l_ref[...] = alpha * l_ref[...] + jnp.sum(p, axis=1, keepdims=True)
                acc_ref[...] = alpha * acc_ref[...] + jnp.dot(
                    p.astype(jnp.bfloat16), tile_ref[1], preferred_element_type=jnp.float32
                )
                m_ref[...] = m_new

            if off_t == 0 and off_h == 0:
                block()
            else:
                pl.when(jnp.logical_and(reach_t >= off_t, reach_h >= off_h))(block)
        if final:
            out = acc_ref[...] / l_ref[...]
            out = jnp.where(qvalid_ref[...] > 0, out, 0.0)
            o_ref[...] = out.astype(o_ref.dtype)
        else:
            m_out[...] = m_ref[...]
            l_out[...] = l_ref[...]
            acc_out[...] = acc_ref[...]

    return kernel


def attend(reach, queries, text, tiles, bias, state=None, qvalid=None):
    tile_len, col_width = queries.shape
    heads = col_width // HD
    blocks = [b for _, _, b in tiles]
    specs = [pl.BlockSpec((tile_len, HD), lambda h, r: (0, h))]
    args = [queries]
    if text is not None:
        specs.append(pl.BlockSpec((2, text.shape[1], HD), lambda h, r: (0, 0, h)))
        args.append(text)
    for array, index, _ in tiles:
        if index is None:
            specs.append(pl.BlockSpec((2, tile_len, HD), lambda h, r: (0, 0, h)))
        else:
            specs.append(
                pl.BlockSpec((None, 2, tile_len, HD), lambda h, r, i=index: (i, 0, 0, h))
            )
        args.append(array)
    specs.append(pl.BlockSpec(bias.shape, lambda h, r: (0, 0, 0)))
    args.append(bias)
    row_spec = pl.BlockSpec((None, tile_len, 1), lambda h, r: (h, 0, 0))
    acc_spec = pl.BlockSpec((tile_len, HD), lambda h, r: (0, h))
    if state is not None:
        specs += [row_spec, row_spec, acc_spec]
        args += list(state)
    final = qvalid is not None
    if final:
        specs.append(pl.BlockSpec(qvalid.shape, lambda h, r: (0, 0)))
        args.append(qvalid)
        out_specs = pl.BlockSpec((tile_len, HD), lambda h, r: (0, h))
        out_shape = jax.ShapeDtypeStruct((tile_len, col_width), jnp.bfloat16)
    else:
        out_specs = [row_spec, row_spec, acc_spec]
        row_shape = jax.ShapeDtypeStruct((heads, tile_len, 1), jnp.float32)
        out_shape = [row_shape, row_shape, jax.ShapeDtypeStruct((tile_len, col_width), jnp.float32)]
    grid_spec = pltpu.PrefetchScalarGridSpec(
        num_scalar_prefetch=1,
        grid=(heads,),
        in_specs=specs,
        out_specs=out_specs,
        scratch_shapes=[
            pltpu.VMEM((tile_len, 1), jnp.float32),
            pltpu.VMEM((tile_len, 1), jnp.float32),
            pltpu.VMEM((tile_len, HD), jnp.float32),
        ],
    )
    kernel = make_kernel(blocks, text is not None, state is not None, final)
    return pl.pallas_call(kernel, grid_spec=grid_spec, out_shape=out_shape)(reach, *args)


def per_device(image_q, image_kv, text_kv, residual, out_weight, out_gate, head_reach, tile_extent):
    tile_len = image_q.shape[2]
    col_width = image_q.shape[3]
    tm_size = lax.axis_size("tm")
    height_size = lax.axis_size("height")
    mp_size = lax.axis_size("mp")

    own = image_kv[0, 0]
    h_before = lax.ppermute(own, "height", shift_pairs(height_size, 1))
    h_after = lax.ppermute(own, "height", shift_pairs(height_size, -1))
    text_group = text_halves(text_kv)
    group = 1
    while group < tm_size:
        text_group = exchange(text_group, tm_size, group)
        group *= 4
    text = join_halves(text_group)
    sent, text = lax.optimization_barrier((own, text))
    t_before = lax.ppermute(sent, "tm", shift_pairs(tm_size, 1))
    t_after = lax.ppermute(sent, "tm", shift_pairs(tm_size, -1))
    time_start = lax.axis_index("tm")
    height_start = lax.axis_index("height")
    zero_index = jnp.int32(0)
    padded_ext = jnp.pad(tile_extent, ((0, 0), (1, 1), (1, 1)))
    local_ext = lax.dynamic_slice(padded_ext, (zero_index, time_start, height_start), (2, 3, 3))
    key_valid = token_masks(local_ext)
    bias = jnp.where(key_valid, 0.0, NEG).astype(jnp.float32).reshape(9, 1, tile_len)
    qvalid = key_valid[1, 1].astype(jnp.float32).reshape(tile_len, 1)

    queries = image_q[0, 0]
    near = [(own, None, 4), (h_before, None, 3), (h_after, None, 5)]
    state = attend(head_reach, queries, None, near, bias)
    t_before, t_after, state = lax.optimization_barrier((t_before, t_after, state))
    time_pair = jnp.stack([t_before, t_after])
    c_before = lax.ppermute(time_pair, "height", shift_pairs(height_size, 1))
    c_after = lax.ppermute(time_pair, "height", shift_pairs(height_size, -1))
    across = [(t_before, None, 1), (t_after, None, 7)]
    state = attend(head_reach, queries, text, across, bias, state)
    corners = [(c_before, 0, 0), (c_after, 0, 2), (c_before, 1, 6), (c_after, 1, 8)]
    attended = attend(head_reach, queries, None, corners, bias, state, qvalid)

    mp_index = lax.axis_index("mp")
    chunk = out_weight.shape[1] // mp_size
    received = []
    for step in (2, 1, 3):
        target = (mp_index + step) % mp_size
        w_part = lax.dynamic_slice_in_dim(out_weight, target * chunk, chunk, 1)
        part = jnp.dot(attended, w_part, preferred_element_type=jnp.float32).astype(jnp.bfloat16)
        pairs = [(i, (i + step) % mp_size) for i in range(mp_size)]
        received.append(lax.ppermute(part, "mp", pairs))
    w_own = lax.dynamic_slice_in_dim(out_weight, mp_index * chunk, chunk, 1)
    branch = jnp.dot(attended, w_own, preferred_element_type=jnp.float32).astype(jnp.bfloat16)
    branch = branch.astype(jnp.float32)
    for part in received:
        branch = branch + part.astype(jnp.float32)
    updated = residual[0, 0].astype(jnp.float32) + out_gate * branch
    return updated.astype(jnp.bfloat16)[None, None]


def solution(mesh):
    return jax.shard_map(
        per_device,
        mesh=mesh,
        in_specs=(
            P("tm", "height", None, "mp"),
            P("tm", "height", None, None, "mp"),
            P(None, "tm", "mp"),
            P("tm", "height", None, "mp"),
            P("mp", None),
            P("mp"),
            P("mp", None),
            P(),
        ),
        out_specs=P("tm", "height", None, "mp"),
        check_vma=False,
    )
```

```python
import math

import jax
import jax.numpy as jnp
from jax import lax
from jax.experimental import pallas as pl
from jax.experimental.pallas import tpu as pltpu
from jax.sharding import PartitionSpec as P

HD = 128
TXT = 256
TILE_F = 6
TILE_R = 8
TILE_C = 8
NEG = -1e30


def token_masks(extent_pair):
    positions = jnp.arange(TILE_F * TILE_R * TILE_C, dtype=jnp.int32)
    frame_of = positions // (TILE_R * TILE_C)
    row_of = positions // TILE_C % TILE_R
    frame_ok = frame_of < extent_pair[0][..., None]
    row_ok = row_of < extent_pair[1][..., None]
    return jnp.logical_and(frame_ok, row_ok)


def shift_pairs(devices, step):
    return [(i, i + step) for i in range(devices) if 0 <= i + step < devices]


def text_halves(text_kv):
    half_width = text_kv.shape[2] // 2
    half = lax.axis_index("height") % 2
    return lax.dynamic_slice_in_dim(text_kv, half * half_width, half_width, 2)


def exchange(block, devices, step):
    position = lax.axis_index("tm")
    other = lax.ppermute(block, "tm", [(i, i ^ step) for i in range(devices)])
    low_first = jnp.concatenate([block, other], axis=1)
    high_first = jnp.concatenate([other, block], axis=1)
    return jnp.where((position & step) == 0, low_first, high_first)


def join_halves(mine):
    half = lax.axis_index("height") % 2
    pairs = [(i, i ^ 1) for i in range(lax.axis_size("height"))]
    other = lax.ppermute(mine, "height", pairs)
    low_first = jnp.concatenate([mine, other], axis=2)
    high_first = jnp.concatenate([other, mine], axis=2)
    return jnp.where(half == 0, low_first, high_first)


def make_kernel(blocks, has_text, has_state, final):
    count = len(blocks)

    def kernel(reach_ref, q_ref, *rest):
        rest = list(rest)
        text_ref = rest.pop(0) if has_text else None
        tile_refs = rest[:count]
        rest = rest[count:]
        bias_ref = rest.pop(0)
        if has_state:
            m_in, l_in, acc_in = rest[:3]
            rest = rest[3:]
        if final:
            qvalid_ref = rest.pop(0)
            o_ref = rest.pop(0)
        else:
            m_out, l_out, acc_out = rest[:3]
            rest = rest[3:]
        m_ref, l_ref, acc_ref = rest
        head = pl.program_id(0)
        scale = 1.0 / math.sqrt(HD)
        q = q_ref[...]
        dims = (((1,), (1,)), ((), ()))
        if has_state:
            m_ref[...] = m_in[...]
            l_ref[...] = l_in[...]
            acc_ref[...] = acc_in[...]
        else:
            m_ref[...] = jnp.full(m_ref.shape, NEG, jnp.float32)
            l_ref[...] = jnp.zeros(l_ref.shape, jnp.float32)
            acc_ref[...] = jnp.zeros(acc_ref.shape, jnp.float32)
        if has_text:
            s = lax.dot_general(q, text_ref[0], dims, preferred_element_type=jnp.float32) * scale
            m_old = m_ref[...]
            m_new = jnp.maximum(m_old, jnp.max(s, axis=1, keepdims=True))
            alpha = jnp.exp(m_old - m_new)
            p = jnp.exp(s - m_new)
            l_ref[...] = alpha * l_ref[...] + jnp.sum(p, axis=1, keepdims=True)
            acc_ref[...] = alpha * acc_ref[...] + jnp.dot(
                p.astype(jnp.bfloat16), text_ref[1], preferred_element_type=jnp.float32
            )
            m_ref[...] = m_new
        reach_t = reach_ref[head, 0]
        reach_h = reach_ref[head, 1]
        for tile_ref, b in zip(tile_refs, blocks):
            off_t, off_h = abs(b // 3 - 1), abs(b % 3 - 1)

            def block(tile_ref=tile_ref, b=b):
                s = lax.dot_general(q, tile_ref[0], dims, preferred_element_type=jnp.float32)
                s = s * scale + bias_ref[b]
                m_old = m_ref[...]
                m_new = jnp.maximum(m_old, jnp.max(s, axis=1, keepdims=True))
                alpha = jnp.exp(m_old - m_new)
                p = jnp.exp(s - m_new)
                l_ref[...] = alpha * l_ref[...] + jnp.sum(p, axis=1, keepdims=True)
                acc_ref[...] = alpha * acc_ref[...] + jnp.dot(
                    p.astype(jnp.bfloat16), tile_ref[1], preferred_element_type=jnp.float32
                )
                m_ref[...] = m_new

            if off_t == 0 and off_h == 0:
                block()
            else:
                pl.when(jnp.logical_and(reach_t >= off_t, reach_h >= off_h))(block)
        if final:
            out = acc_ref[...] / l_ref[...]
            out = jnp.where(qvalid_ref[...] > 0, out, 0.0)
            o_ref[...] = out.astype(o_ref.dtype)
        else:
            m_out[...] = m_ref[...]
            l_out[...] = l_ref[...]
            acc_out[...] = acc_ref[...]

    return kernel


def attend(reach, queries, text, tiles, bias, state=None, qvalid=None):
    tile_len, col_width = queries.shape
    heads = col_width // HD
    blocks = [b for _, _, b in tiles]
    specs = [pl.BlockSpec((tile_len, HD), lambda h, r: (0, h))]
    args = [queries]
    if text is not None:
        specs.append(pl.BlockSpec((2, text.shape[1], HD), lambda h, r: (0, 0, h)))
        args.append(text)
    for array, index, _ in tiles:
        if index is None:
            specs.append(pl.BlockSpec((2, tile_len, HD), lambda h, r: (0, 0, h)))
        else:
            specs.append(
                pl.BlockSpec((None, 2, tile_len, HD), lambda h, r, i=index: (i, 0, 0, h))
            )
        args.append(array)
    specs.append(pl.BlockSpec(bias.shape, lambda h, r: (0, 0, 0)))
    args.append(bias)
    row_spec = pl.BlockSpec((None, tile_len, 1), lambda h, r: (h, 0, 0))
    acc_spec = pl.BlockSpec((tile_len, HD), lambda h, r: (0, h))
    if state is not None:
        specs += [row_spec, row_spec, acc_spec]
        args += list(state)
    final = qvalid is not None
    if final:
        specs.append(pl.BlockSpec(qvalid.shape, lambda h, r: (0, 0)))
        args.append(qvalid)
        out_specs = pl.BlockSpec((tile_len, HD), lambda h, r: (0, h))
        out_shape = jax.ShapeDtypeStruct((tile_len, col_width), jnp.bfloat16)
    else:
        out_specs = [row_spec, row_spec, acc_spec]
        row_shape = jax.ShapeDtypeStruct((heads, tile_len, 1), jnp.float32)
        out_shape = [row_shape, row_shape, jax.ShapeDtypeStruct((tile_len, col_width), jnp.float32)]
    grid_spec = pltpu.PrefetchScalarGridSpec(
        num_scalar_prefetch=1,
        grid=(heads,),
        in_specs=specs,
        out_specs=out_specs,
        scratch_shapes=[
            pltpu.VMEM((tile_len, 1), jnp.float32),
            pltpu.VMEM((tile_len, 1), jnp.float32),
            pltpu.VMEM((tile_len, HD), jnp.float32),
        ],
    )
    kernel = make_kernel(blocks, text is not None, state is not None, final)
    return pl.pallas_call(kernel, grid_spec=grid_spec, out_shape=out_shape)(reach, *args)


def per_device(image_q, image_kv, text_kv, residual, out_weight, out_gate, head_reach, tile_extent):
    tile_len = image_q.shape[2]
    col_width = image_q.shape[3]
    tm_size = lax.axis_size("tm")
    height_size = lax.axis_size("height")
    mp_size = lax.axis_size("mp")

    own = image_kv[0, 0]
    h_before = lax.ppermute(own, "height", shift_pairs(height_size, 1))
    h_after = lax.ppermute(own, "height", shift_pairs(height_size, -1))
    text_group = text_halves(text_kv)
    step = 1
    while step < tm_size:
        text_group = exchange(text_group, tm_size, step)
        step *= 2
    text = join_halves(text_group)
    sent, text, h_before, h_after = lax.optimization_barrier((own, text, h_before, h_after))
    t_before = lax.ppermute(sent, "tm", shift_pairs(tm_size, 1))
    t_after = lax.ppermute(sent, "tm", shift_pairs(tm_size, -1))
    time_start = lax.axis_index("tm")
    height_start = lax.axis_index("height")
    zero_index = jnp.int32(0)
    padded_ext = jnp.pad(tile_extent, ((0, 0), (1, 1), (1, 1)))
    local_ext = lax.dynamic_slice(padded_ext, (zero_index, time_start, height_start), (2, 3, 3))
    key_valid = token_masks(local_ext)
    bias = jnp.where(key_valid, 0.0, NEG).astype(jnp.float32).reshape(9, 1, tile_len)
    qvalid = key_valid[1, 1].astype(jnp.float32).reshape(tile_len, 1)

    queries = image_q[0, 0]
    near = [(own, None, 4), (h_before, None, 3), (h_after, None, 5)]
    state = attend(head_reach, queries, None, near, bias)
    t_before, t_after, state = lax.optimization_barrier((t_before, t_after, state))
    time_pair = jnp.stack([t_before, t_after])
    c_before = lax.ppermute(time_pair, "height", shift_pairs(height_size, 1))
    c_after = lax.ppermute(time_pair, "height", shift_pairs(height_size, -1))
    across = [(t_before, None, 1), (t_after, None, 7)]
    state = attend(head_reach, queries, text, across, bias, state)
    corners = [(c_before, 0, 0), (c_after, 0, 2), (c_before, 1, 6), (c_after, 1, 8)]
    attended = attend(head_reach, queries, None, corners, bias, state, qvalid)

    mp_index = lax.axis_index("mp")
    chunk = out_weight.shape[1] // mp_size
    received = []
    for step in (2, 1, 3):
        target = (mp_index + step) % mp_size
        w_part = lax.dynamic_slice_in_dim(out_weight, target * chunk, chunk, 1)
        part = jnp.dot(attended, w_part, preferred_element_type=jnp.float32).astype(jnp.bfloat16)
        pairs = [(i, (i + step) % mp_size) for i in range(mp_size)]
        received.append(lax.ppermute(part, "mp", pairs))
    w_own = lax.dynamic_slice_in_dim(out_weight, mp_index * chunk, chunk, 1)
    branch = jnp.dot(attended, w_own, preferred_element_type=jnp.float32).astype(jnp.bfloat16)
    branch = branch.astype(jnp.float32)
    for part in received:
        branch = branch + part.astype(jnp.float32)
    updated = residual[0, 0].astype(jnp.float32) + out_gate * branch
    return updated.astype(jnp.bfloat16)[None, None]


def solution(mesh):
    return jax.shard_map(
        per_device,
        mesh=mesh,
        in_specs=(
            P("tm", "height", None, "mp"),
            P("tm", "height", None, None, "mp"),
            P(None, "tm", "mp"),
            P("tm", "height", None, "mp"),
            P("mp", None),
            P("mp"),
            P("mp", None),
            P(),
        ),
        out_specs=P("tm", "height", None, "mp"),
        check_vma=False,
    )
```

```python
import math

import jax
import jax.numpy as jnp
from jax import lax
from jax.experimental import pallas as pl
from jax.experimental.pallas import tpu as pltpu
from jax.sharding import PartitionSpec as P

HD = 128
TXT = 256
TILE_F = 6
TILE_R = 8
TILE_C = 8
NEG = -1e30


def token_masks(extent_pair):
    positions = jnp.arange(TILE_F * TILE_R * TILE_C, dtype=jnp.int32)
    frame_of = positions // (TILE_R * TILE_C)
    row_of = positions // TILE_C % TILE_R
    frame_ok = frame_of < extent_pair[0][..., None]
    row_ok = row_of < extent_pair[1][..., None]
    return jnp.logical_and(frame_ok, row_ok)


def shift_pairs(devices, step):
    return [(i, i + step) for i in range(devices) if 0 <= i + step < devices]


def text_halves(text_kv):
    half_width = text_kv.shape[2] // 2
    half = lax.axis_index("height") % 2
    return lax.dynamic_slice_in_dim(text_kv, half * half_width, half_width, 2)


def exchange(block, devices, step):
    position = lax.axis_index("tm")
    other = lax.ppermute(block, "tm", [(i, i ^ step) for i in range(devices)])
    low_first = jnp.concatenate([block, other], axis=1)
    high_first = jnp.concatenate([other, block], axis=1)
    return jnp.where((position & step) == 0, low_first, high_first)


def join_halves(mine):
    half = lax.axis_index("height") % 2
    pairs = [(i, i ^ 1) for i in range(lax.axis_size("height"))]
    other = lax.ppermute(mine, "height", pairs)
    low_first = jnp.concatenate([mine, other], axis=2)
    high_first = jnp.concatenate([other, mine], axis=2)
    return jnp.where(half == 0, low_first, high_first)


def make_kernel(blocks, has_text, has_state, final):
    count = len(blocks)

    def kernel(reach_ref, q_ref, *rest):
        rest = list(rest)
        text_ref = rest.pop(0) if has_text else None
        tile_refs = rest[:count]
        rest = rest[count:]
        bias_ref = rest.pop(0)
        if has_state:
            m_in, l_in, acc_in = rest[:3]
            rest = rest[3:]
        if final:
            qvalid_ref = rest.pop(0)
            o_ref = rest.pop(0)
        else:
            m_out, l_out, acc_out = rest[:3]
            rest = rest[3:]
        m_ref, l_ref, acc_ref = rest
        head = pl.program_id(0)
        scale = 1.0 / math.sqrt(HD)
        q = q_ref[...]
        dims = (((1,), (1,)), ((), ()))
        if has_state:
            m_ref[...] = m_in[...]
            l_ref[...] = l_in[...]
            acc_ref[...] = acc_in[...]
        else:
            m_ref[...] = jnp.full(m_ref.shape, NEG, jnp.float32)
            l_ref[...] = jnp.zeros(l_ref.shape, jnp.float32)
            acc_ref[...] = jnp.zeros(acc_ref.shape, jnp.float32)
        if has_text:
            s = lax.dot_general(q, text_ref[0], dims, preferred_element_type=jnp.float32) * scale
            m_old = m_ref[...]
            m_new = jnp.maximum(m_old, jnp.max(s, axis=1, keepdims=True))
            alpha = jnp.exp(m_old - m_new)
            p = jnp.exp(s - m_new)
            l_ref[...] = alpha * l_ref[...] + jnp.sum(p, axis=1, keepdims=True)
            acc_ref[...] = alpha * acc_ref[...] + jnp.dot(
                p.astype(jnp.bfloat16), text_ref[1], preferred_element_type=jnp.float32
            )
            m_ref[...] = m_new
        reach_t = reach_ref[head, 0]
        reach_h = reach_ref[head, 1]
        for tile_ref, b in zip(tile_refs, blocks):
            off_t, off_h = abs(b // 3 - 1), abs(b % 3 - 1)

            def block(tile_ref=tile_ref, b=b):
                s = lax.dot_general(q, tile_ref[0], dims, preferred_element_type=jnp.float32)
                s = s * scale + bias_ref[b]
                m_old = m_ref[...]
                m_new = jnp.maximum(m_old, jnp.max(s, axis=1, keepdims=True))
                alpha = jnp.exp(m_old - m_new)
                p = jnp.exp(s - m_new)
                l_ref[...] = alpha * l_ref[...] + jnp.sum(p, axis=1, keepdims=True)
                acc_ref[...] = alpha * acc_ref[...] + jnp.dot(
                    p.astype(jnp.bfloat16), tile_ref[1], preferred_element_type=jnp.float32
                )
                m_ref[...] = m_new

            if off_t == 0 and off_h == 0:
                block()
            else:
                pl.when(jnp.logical_and(reach_t >= off_t, reach_h >= off_h))(block)
        if final:
            out = acc_ref[...] / l_ref[...]
            out = jnp.where(qvalid_ref[...] > 0, out, 0.0)
            o_ref[...] = out.astype(o_ref.dtype)
        else:
            m_out[...] = m_ref[...]
            l_out[...] = l_ref[...]
            acc_out[...] = acc_ref[...]

    return kernel


def attend(reach, queries, text, tiles, bias, state=None, qvalid=None):
    tile_len, col_width = queries.shape
    key_len = tiles[0][0].shape[-2]
    heads = col_width // HD
    blocks = [b for _, _, b in tiles]
    specs = [pl.BlockSpec((tile_len, HD), lambda h, r: (0, h))]
    args = [queries]
    if text is not None:
        specs.append(pl.BlockSpec((2, text.shape[1], HD), lambda h, r: (0, 0, h)))
        args.append(text)
    for array, index, _ in tiles:
        if index is None:
            specs.append(pl.BlockSpec((2, key_len, HD), lambda h, r: (0, 0, h)))
        else:
            specs.append(
                pl.BlockSpec((None, 2, key_len, HD), lambda h, r, i=index: (i, 0, 0, h))
            )
        args.append(array)
    specs.append(pl.BlockSpec(bias.shape, lambda h, r: (0, 0, 0)))
    args.append(bias)
    row_spec = pl.BlockSpec((None, tile_len, 1), lambda h, r: (h, 0, 0))
    acc_spec = pl.BlockSpec((tile_len, HD), lambda h, r: (0, h))
    if state is not None:
        specs += [row_spec, row_spec, acc_spec]
        args += list(state)
    final = qvalid is not None
    if final:
        specs.append(pl.BlockSpec(qvalid.shape, lambda h, r: (0, 0)))
        args.append(qvalid)
        out_specs = pl.BlockSpec((tile_len, HD), lambda h, r: (0, h))
        out_shape = jax.ShapeDtypeStruct((tile_len, col_width), jnp.bfloat16)
    else:
        out_specs = [row_spec, row_spec, acc_spec]
        row_shape = jax.ShapeDtypeStruct((heads, tile_len, 1), jnp.float32)
        out_shape = [row_shape, row_shape, jax.ShapeDtypeStruct((tile_len, col_width), jnp.float32)]
    grid_spec = pltpu.PrefetchScalarGridSpec(
        num_scalar_prefetch=1,
        grid=(heads,),
        in_specs=specs,
        out_specs=out_specs,
        scratch_shapes=[
            pltpu.VMEM((tile_len, 1), jnp.float32),
            pltpu.VMEM((tile_len, 1), jnp.float32),
            pltpu.VMEM((tile_len, HD), jnp.float32),
        ],
    )
    kernel = make_kernel(blocks, text is not None, state is not None, final)
    return pl.pallas_call(kernel, grid_spec=grid_spec, out_shape=out_shape)(reach, *args)


def per_device(image_q, image_kv, text_kv, residual, out_weight, out_gate, head_reach, tile_extent):
    tile_len = image_q.shape[2]
    col_width = image_q.shape[3]
    tm_size = lax.axis_size("tm")
    height_size = lax.axis_size("height")
    mp_size = lax.axis_size("mp")

    own = image_kv[0, 0]
    h_before = lax.ppermute(own, "height", shift_pairs(height_size, 1))
    h_after = lax.ppermute(own, "height", shift_pairs(height_size, -1))
    text_group = text_halves(text_kv)
    step = 1
    while step < tm_size:
        text_group = exchange(text_group, tm_size, step)
        step *= 2
    text = join_halves(text_group)
    sent, text, h_before, h_after = lax.optimization_barrier((own, text, h_before, h_after))
    t_before = lax.ppermute(sent, "tm", shift_pairs(tm_size, 1))
    t_after = lax.ppermute(sent, "tm", shift_pairs(tm_size, -1))
    time_start = lax.axis_index("tm")
    height_start = lax.axis_index("height")
    zero_index = jnp.int32(0)
    padded_ext = jnp.pad(tile_extent, ((0, 0), (1, 1), (1, 1)))
    local_ext = lax.dynamic_slice(padded_ext, (zero_index, time_start, height_start), (2, 3, 3))
    key_valid = token_masks(local_ext)
    bias = jnp.where(key_valid, 0.0, NEG).astype(jnp.float32).reshape(9, 1, tile_len)
    qvalid = key_valid[1, 1].astype(jnp.float32).reshape(tile_len, 1)

    queries = image_q[0, 0]
    near = [(own, None, 4), (h_before, None, 3), (h_after, None, 5)]
    state = attend(head_reach, queries, None, near, bias)
    t_before, t_after, state = lax.optimization_barrier((t_before, t_after, state))
    time_pair = jnp.stack([t_before, t_after])
    c_before = lax.ppermute(time_pair, "height", shift_pairs(height_size, 1))
    c_after = lax.ppermute(time_pair, "height", shift_pairs(height_size, -1))
    across = [(t_before, None, 1), (t_after, None, 7)]
    state = attend(head_reach, queries, text, across, bias, state)
    corners = [(c_before, 0, 0), (c_after, 0, 2), (c_before, 1, 6), (c_after, 1, 8)]
    mp_index = lax.axis_index("mp")
    chunk = out_weight.shape[1] // mp_size
    rows = tile_len // 2
    outputs = []
    for start in (0, rows):
        part_state = (
            state[0][:, start:start + rows],
            state[1][:, start:start + rows],
            state[2][start:start + rows],
        )
        attended = attend(
            head_reach, queries[start:start + rows], None, corners, bias, part_state,
            qvalid[start:start + rows],
        )
        outputs.append(
            project(attended, out_weight, out_gate, residual[0, 0, start:start + rows],
                    mp_index, mp_size, chunk)
        )
    return jnp.concatenate(outputs, axis=0)[None, None]


def project(attended, out_weight, out_gate, residual, mp_index, mp_size, chunk):
    received = []
    for step in (2, 1, 3):
        target = (mp_index + step) % mp_size
        w_part = lax.dynamic_slice_in_dim(out_weight, target * chunk, chunk, 1)
        part = jnp.dot(attended, w_part, preferred_element_type=jnp.float32).astype(jnp.bfloat16)
        pairs = [(i, (i + step) % mp_size) for i in range(mp_size)]
        received.append(lax.ppermute(part, "mp", pairs))
    w_own = lax.dynamic_slice_in_dim(out_weight, mp_index * chunk, chunk, 1)
    branch = jnp.dot(attended, w_own, preferred_element_type=jnp.float32).astype(jnp.bfloat16)
    branch = branch.astype(jnp.float32)
    for part in received:
        branch = branch + part.astype(jnp.float32)
    updated = residual.astype(jnp.float32) + out_gate * branch
    return updated.astype(jnp.bfloat16)


def solution(mesh):
    return jax.shard_map(
        per_device,
        mesh=mesh,
        in_specs=(
            P("tm", "height", None, "mp"),
            P("tm", "height", None, None, "mp"),
            P(None, "tm", "mp"),
            P("tm", "height", None, "mp"),
            P("mp", None),
            P("mp"),
            P("mp", None),
            P(),
        ),
        out_specs=P("tm", "height", None, "mp"),
        check_vma=False,
    )
```

```python
import math

import jax
import jax.numpy as jnp
from jax import lax
from jax.experimental import pallas as pl
from jax.experimental.pallas import tpu as pltpu
from jax.sharding import PartitionSpec as P

HD = 128
TXT = 256
TILE_F = 6
TILE_R = 8
TILE_C = 8
NEG = -1e30


def token_masks(extent_pair):
    positions = jnp.arange(TILE_F * TILE_R * TILE_C, dtype=jnp.int32)
    frame_of = positions // (TILE_R * TILE_C)
    row_of = positions // TILE_C % TILE_R
    frame_ok = frame_of < extent_pair[0][..., None]
    row_ok = row_of < extent_pair[1][..., None]
    return jnp.logical_and(frame_ok, row_ok)


def shift_pairs(devices, step):
    return [(i, i + step) for i in range(devices) if 0 <= i + step < devices]


def text_halves(text_kv):
    half_width = text_kv.shape[2] // 2
    half = lax.axis_index("height") % 2
    return lax.dynamic_slice_in_dim(text_kv, half * half_width, half_width, 2)


def exchange(block, devices, step):
    position = lax.axis_index("tm")
    other = lax.ppermute(block, "tm", [(i, i ^ step) for i in range(devices)])
    low_first = jnp.concatenate([block, other], axis=1)
    high_first = jnp.concatenate([other, block], axis=1)
    return jnp.where((position & step) == 0, low_first, high_first)


def join_halves(mine):
    half = lax.axis_index("height") % 2
    pairs = [(i, i ^ 1) for i in range(lax.axis_size("height"))]
    other = lax.ppermute(mine, "height", pairs)
    low_first = jnp.concatenate([mine, other], axis=2)
    high_first = jnp.concatenate([other, mine], axis=2)
    return jnp.where(half == 0, low_first, high_first)


def make_kernel(blocks, has_text, has_state, final):
    count = len(blocks)

    def kernel(reach_ref, q_ref, *rest):
        rest = list(rest)
        text_ref = rest.pop(0) if has_text else None
        tile_refs = rest[:count]
        rest = rest[count:]
        bias_ref = rest.pop(0)
        if has_state:
            m_in, l_in, acc_in = rest[:3]
            rest = rest[3:]
        if final:
            qvalid_ref = rest.pop(0)
            o_ref = rest.pop(0)
        else:
            m_out, l_out, acc_out = rest[:3]
            rest = rest[3:]
        m_ref, l_ref, acc_ref = rest
        head = pl.program_id(0)
        scale = 1.0 / math.sqrt(HD)
        q = q_ref[...]
        dims = (((1,), (1,)), ((), ()))
        if has_state:
            m_ref[...] = m_in[...]
            l_ref[...] = l_in[...]
            acc_ref[...] = acc_in[...]
        else:
            m_ref[...] = jnp.full(m_ref.shape, NEG, jnp.float32)
            l_ref[...] = jnp.zeros(l_ref.shape, jnp.float32)
            acc_ref[...] = jnp.zeros(acc_ref.shape, jnp.float32)
        if has_text:
            s = lax.dot_general(q, text_ref[0], dims, preferred_element_type=jnp.float32) * scale
            m_old = m_ref[...]
            m_new = jnp.maximum(m_old, jnp.max(s, axis=1, keepdims=True))
            alpha = jnp.exp(m_old - m_new)
            p = jnp.exp(s - m_new)
            l_ref[...] = alpha * l_ref[...] + jnp.sum(p, axis=1, keepdims=True)
            acc_ref[...] = alpha * acc_ref[...] + jnp.dot(
                p.astype(jnp.bfloat16), text_ref[1], preferred_element_type=jnp.float32
            )
            m_ref[...] = m_new
        reach_t = reach_ref[head, 0]
        reach_h = reach_ref[head, 1]
        for tile_ref, b in zip(tile_refs, blocks):
            off_t, off_h = abs(b // 3 - 1), abs(b % 3 - 1)

            def block(tile_ref=tile_ref, b=b):
                s = lax.dot_general(q, tile_ref[0], dims, preferred_element_type=jnp.float32)
                s = s * scale + bias_ref[b]
                m_old = m_ref[...]
                m_new = jnp.maximum(m_old, jnp.max(s, axis=1, keepdims=True))
                alpha = jnp.exp(m_old - m_new)
                p = jnp.exp(s - m_new)
                l_ref[...] = alpha * l_ref[...] + jnp.sum(p, axis=1, keepdims=True)
                acc_ref[...] = alpha * acc_ref[...] + jnp.dot(
                    p.astype(jnp.bfloat16), tile_ref[1], preferred_element_type=jnp.float32
                )
                m_ref[...] = m_new

            if off_t == 0 and off_h == 0:
                block()
            else:
                pl.when(jnp.logical_and(reach_t >= off_t, reach_h >= off_h))(block)
        if final:
            out = acc_ref[...] / l_ref[...]
            out = jnp.where(qvalid_ref[...] > 0, out, 0.0)
            o_ref[...] = out.astype(o_ref.dtype)
        else:
            m_out[...] = m_ref[...]
            l_out[...] = l_ref[...]
            acc_out[...] = acc_ref[...]

    return kernel


def attend(reach, queries, text, tiles, bias, state=None, qvalid=None):
    tile_len, col_width = queries.shape
    heads = col_width // HD
    blocks = [b for _, _, b in tiles]
    specs = [pl.BlockSpec((tile_len, HD), lambda h, r: (0, h))]
    args = [queries]
    if text is not None:
        specs.append(pl.BlockSpec((2, text.shape[1], HD), lambda h, r: (0, 0, h)))
        args.append(text)
    for array, index, _ in tiles:
        if index is None:
            specs.append(pl.BlockSpec((2, tile_len, HD), lambda h, r: (0, 0, h)))
        else:
            specs.append(
                pl.BlockSpec((None, 2, tile_len, HD), lambda h, r, i=index: (i, 0, 0, h))
            )
        args.append(array)
    specs.append(pl.BlockSpec(bias.shape, lambda h, r: (0, 0, 0)))
    args.append(bias)
    row_spec = pl.BlockSpec((None, tile_len, 1), lambda h, r: (h, 0, 0))
    acc_spec = pl.BlockSpec((tile_len, HD), lambda h, r: (0, h))
    if state is not None:
        specs += [row_spec, row_spec, acc_spec]
        args += list(state)
    final = qvalid is not None
    if final:
        specs.append(pl.BlockSpec(qvalid.shape, lambda h, r: (0, 0)))
        args.append(qvalid)
        out_specs = pl.BlockSpec((tile_len, HD), lambda h, r: (0, h))
        out_shape = jax.ShapeDtypeStruct((tile_len, col_width), jnp.bfloat16)
    else:
        out_specs = [row_spec, row_spec, acc_spec]
        row_shape = jax.ShapeDtypeStruct((heads, tile_len, 1), jnp.float32)
        out_shape = [row_shape, row_shape, jax.ShapeDtypeStruct((tile_len, col_width), jnp.float32)]
    grid_spec = pltpu.PrefetchScalarGridSpec(
        num_scalar_prefetch=1,
        grid=(heads,),
        in_specs=specs,
        out_specs=out_specs,
        scratch_shapes=[
            pltpu.VMEM((tile_len, 1), jnp.float32),
            pltpu.VMEM((tile_len, 1), jnp.float32),
            pltpu.VMEM((tile_len, HD), jnp.float32),
        ],
    )
    kernel = make_kernel(blocks, text is not None, state is not None, final)
    return pl.pallas_call(kernel, grid_spec=grid_spec, out_shape=out_shape)(reach, *args)


def per_device(image_q, image_kv, text_kv, residual, out_weight, out_gate, head_reach, tile_extent):
    tile_len = image_q.shape[2]
    col_width = image_q.shape[3]
    tm_size = lax.axis_size("tm")
    height_size = lax.axis_size("height")
    mp_size = lax.axis_size("mp")

    own = image_kv[0, 0]
    h_before = lax.ppermute(own, "height", shift_pairs(height_size, 1))
    h_after = lax.ppermute(own, "height", shift_pairs(height_size, -1))
    text_group = exchange(text_halves(text_kv), tm_size, 1)
    sent, text_group, h_before, h_after = lax.optimization_barrier(
        (own, text_group, h_before, h_after)
    )
    t_before = lax.ppermute(sent, "tm", shift_pairs(tm_size, 1))
    t_after = lax.ppermute(sent, "tm", shift_pairs(tm_size, -1))
    step = 2
    while step < tm_size:
        text_group = exchange(text_group, tm_size, step)
        step *= 2
    text = join_halves(text_group)
    time_start = lax.axis_index("tm")
    height_start = lax.axis_index("height")
    zero_index = jnp.int32(0)
    padded_ext = jnp.pad(tile_extent, ((0, 0), (1, 1), (1, 1)))
    local_ext = lax.dynamic_slice(padded_ext, (zero_index, time_start, height_start), (2, 3, 3))
    key_valid = token_masks(local_ext)
    bias = jnp.where(key_valid, 0.0, NEG).astype(jnp.float32).reshape(9, 1, tile_len)
    qvalid = key_valid[1, 1].astype(jnp.float32).reshape(tile_len, 1)

    queries = image_q[0, 0]
    near = [(own, None, 4), (h_before, None, 3), (h_after, None, 5)]
    state = attend(head_reach, queries, None, near, bias)
    t_before, t_after, state = lax.optimization_barrier((t_before, t_after, state))
    time_pair = jnp.stack([t_before, t_after])
    c_before = lax.ppermute(time_pair, "height", shift_pairs(height_size, 1))
    c_after = lax.ppermute(time_pair, "height", shift_pairs(height_size, -1))
    across = [(t_before, None, 1), (t_after, None, 7)]
    state = attend(head_reach, queries, text, across, bias, state)
    corners = [(c_before, 0, 0), (c_after, 0, 2), (c_before, 1, 6), (c_after, 1, 8)]
    attended = attend(head_reach, queries, None, corners, bias, state, qvalid)

    mp_index = lax.axis_index("mp")
    chunk = out_weight.shape[1] // mp_size
    received = []
    for step in (2, 1, 3):
        target = (mp_index + step) % mp_size
        w_part = lax.dynamic_slice_in_dim(out_weight, target * chunk, chunk, 1)
        part = jnp.dot(attended, w_part, preferred_element_type=jnp.float32).astype(jnp.bfloat16)
        pairs = [(i, (i + step) % mp_size) for i in range(mp_size)]
        received.append(lax.ppermute(part, "mp", pairs))
    w_own = lax.dynamic_slice_in_dim(out_weight, mp_index * chunk, chunk, 1)
    branch = jnp.dot(attended, w_own, preferred_element_type=jnp.float32).astype(jnp.bfloat16)
    branch = branch.astype(jnp.float32)
    for part in received:
        branch = branch + part.astype(jnp.float32)
    updated = residual[0, 0].astype(jnp.float32) + out_gate * branch
    return updated.astype(jnp.bfloat16)[None, None]


def solution(mesh):
    return jax.shard_map(
        per_device,
        mesh=mesh,
        in_specs=(
            P("tm", "height", None, "mp"),
            P("tm", "height", None, None, "mp"),
            P(None, "tm", "mp"),
            P("tm", "height", None, "mp"),
            P("mp", None),
            P("mp"),
            P("mp", None),
            P(),
        ),
        out_specs=P("tm", "height", None, "mp"),
        check_vma=False,
    )
```

```python
import math

import jax
import jax.numpy as jnp
from jax import lax
from jax.experimental import pallas as pl
from jax.experimental.pallas import tpu as pltpu
from jax.sharding import PartitionSpec as P

HD = 128
TXT = 256
TILE_F = 6
TILE_R = 8
TILE_C = 8
NEG = -1e30


def token_masks(extent_pair):
    positions = jnp.arange(TILE_F * TILE_R * TILE_C, dtype=jnp.int32)
    frame_of = positions // (TILE_R * TILE_C)
    row_of = positions // TILE_C % TILE_R
    frame_ok = frame_of < extent_pair[0][..., None]
    row_ok = row_of < extent_pair[1][..., None]
    return jnp.logical_and(frame_ok, row_ok)


def shift_pairs(devices, step):
    return [(i, i + step) for i in range(devices) if 0 <= i + step < devices]


def text_halves(text_kv):
    half_width = text_kv.shape[2] // 2
    half = lax.axis_index("height") % 2
    return lax.dynamic_slice_in_dim(text_kv, half * half_width, half_width, 2)


def exchange(block, devices, step):
    position = lax.axis_index("tm")
    other = lax.ppermute(block, "tm", [(i, i ^ step) for i in range(devices)])
    low_first = jnp.concatenate([block, other], axis=1)
    high_first = jnp.concatenate([other, block], axis=1)
    return jnp.where((position & step) == 0, low_first, high_first)


def join_halves(mine):
    half = lax.axis_index("height") % 2
    pairs = [(i, i ^ 1) for i in range(lax.axis_size("height"))]
    other = lax.ppermute(mine, "height", pairs)
    low_first = jnp.concatenate([mine, other], axis=2)
    high_first = jnp.concatenate([other, mine], axis=2)
    return jnp.where(half == 0, low_first, high_first)


def make_kernel(blocks, has_text, has_state, final):
    count = len(blocks)

    def kernel(reach_ref, q_ref, *rest):
        rest = list(rest)
        text_ref = rest.pop(0) if has_text else None
        tile_refs = rest[:count]
        rest = rest[count:]
        bias_ref = rest.pop(0)
        if has_state:
            m_in, l_in, acc_in = rest[:3]
            rest = rest[3:]
        if final:
            qvalid_ref = rest.pop(0)
            o_ref = rest.pop(0)
        else:
            m_out, l_out, acc_out = rest[:3]
            rest = rest[3:]
        m_ref, l_ref, acc_ref = rest
        head = pl.program_id(0)
        scale = 1.0 / math.sqrt(HD)
        q = q_ref[...]
        dims = (((1,), (1,)), ((), ()))
        if has_state:
            m_ref[...] = m_in[...]
            l_ref[...] = l_in[...]
            acc_ref[...] = acc_in[...]
        else:
            m_ref[...] = jnp.full(m_ref.shape, NEG, jnp.float32)
            l_ref[...] = jnp.zeros(l_ref.shape, jnp.float32)
            acc_ref[...] = jnp.zeros(acc_ref.shape, jnp.float32)
        if has_text:
            s = lax.dot_general(q, text_ref[0], dims, preferred_element_type=jnp.float32) * scale
            m_old = m_ref[...]
            m_new = jnp.maximum(m_old, jnp.max(s, axis=1, keepdims=True))
            alpha = jnp.exp(m_old - m_new)
            p = jnp.exp(s - m_new)
            l_ref[...] = alpha * l_ref[...] + jnp.sum(p, axis=1, keepdims=True)
            acc_ref[...] = alpha * acc_ref[...] + jnp.dot(
                p.astype(jnp.bfloat16), text_ref[1], preferred_element_type=jnp.float32
            )
            m_ref[...] = m_new
        reach_t = reach_ref[head, 0]
        reach_h = reach_ref[head, 1]
        groups = {}
        for tile_ref, b in zip(tile_refs, blocks):
            groups.setdefault((abs(b // 3 - 1), abs(b % 3 - 1)), []).append((tile_ref, b))
        for (off_t, off_h), members in groups.items():

            def block(members=members):
                scores = []
                for tile_ref, b in members:
                    s = lax.dot_general(q, tile_ref[0], dims, preferred_element_type=jnp.float32)
                    scores.append(s * scale + bias_ref[b])
                m_old = m_ref[...]
                m_new = m_old
                for s in scores:
                    m_new = jnp.maximum(m_new, jnp.max(s, axis=1, keepdims=True))
                alpha = jnp.exp(m_old - m_new)
                total = alpha * l_ref[...]
                acc = alpha * acc_ref[...]
                for s, (tile_ref, _) in zip(scores, members):
                    p = jnp.exp(s - m_new)
                    total = total + jnp.sum(p, axis=1, keepdims=True)
                    acc = acc + jnp.dot(
                        p.astype(jnp.bfloat16), tile_ref[1], preferred_element_type=jnp.float32
                    )
                l_ref[...] = total
                acc_ref[...] = acc
                m_ref[...] = m_new

            if off_t == 0 and off_h == 0:
                block()
            else:
                pl.when(jnp.logical_and(reach_t >= off_t, reach_h >= off_h))(block)
        if final:
            out = acc_ref[...] / l_ref[...]
            out = jnp.where(qvalid_ref[...] > 0, out, 0.0)
            o_ref[...] = out.astype(o_ref.dtype)
        else:
            m_out[...] = m_ref[...]
            l_out[...] = l_ref[...]
            acc_out[...] = acc_ref[...]

    return kernel


def attend(reach, queries, text, tiles, bias, state=None, qvalid=None):
    tile_len, col_width = queries.shape
    heads = col_width // HD
    blocks = [b for _, _, b in tiles]
    specs = [pl.BlockSpec((tile_len, HD), lambda h, r: (0, h))]
    args = [queries]
    if text is not None:
        specs.append(pl.BlockSpec((2, text.shape[1], HD), lambda h, r: (0, 0, h)))
        args.append(text)
    for array, index, _ in tiles:
        if index is None:
            specs.append(pl.BlockSpec((2, tile_len, HD), lambda h, r: (0, 0, h)))
        else:
            specs.append(
                pl.BlockSpec((None, 2, tile_len, HD), lambda h, r, i=index: (i, 0, 0, h))
            )
        args.append(array)
    specs.append(pl.BlockSpec(bias.shape, lambda h, r: (0, 0, 0)))
    args.append(bias)
    row_spec = pl.BlockSpec((None, tile_len, 1), lambda h, r: (h, 0, 0))
    acc_spec = pl.BlockSpec((tile_len, HD), lambda h, r: (0, h))
    if state is not None:
        specs += [row_spec, row_spec, acc_spec]
        args += list(state)
    final = qvalid is not None
    if final:
        specs.append(pl.BlockSpec(qvalid.shape, lambda h, r: (0, 0)))
        args.append(qvalid)
        out_specs = pl.BlockSpec((tile_len, HD), lambda h, r: (0, h))
        out_shape = jax.ShapeDtypeStruct((tile_len, col_width), jnp.bfloat16)
    else:
        out_specs = [row_spec, row_spec, acc_spec]
        row_shape = jax.ShapeDtypeStruct((heads, tile_len, 1), jnp.float32)
        out_shape = [row_shape, row_shape, jax.ShapeDtypeStruct((tile_len, col_width), jnp.float32)]
    grid_spec = pltpu.PrefetchScalarGridSpec(
        num_scalar_prefetch=1,
        grid=(heads,),
        in_specs=specs,
        out_specs=out_specs,
        scratch_shapes=[
            pltpu.VMEM((tile_len, 1), jnp.float32),
            pltpu.VMEM((tile_len, 1), jnp.float32),
            pltpu.VMEM((tile_len, HD), jnp.float32),
        ],
    )
    kernel = make_kernel(blocks, text is not None, state is not None, final)
    return pl.pallas_call(kernel, grid_spec=grid_spec, out_shape=out_shape)(reach, *args)


def per_device(image_q, image_kv, text_kv, residual, out_weight, out_gate, head_reach, tile_extent):
    tile_len = image_q.shape[2]
    col_width = image_q.shape[3]
    tm_size = lax.axis_size("tm")
    height_size = lax.axis_size("height")
    mp_size = lax.axis_size("mp")

    own = image_kv[0, 0]
    h_before = lax.ppermute(own, "height", shift_pairs(height_size, 1))
    h_after = lax.ppermute(own, "height", shift_pairs(height_size, -1))
    text_group = text_halves(text_kv)
    step = 1
    while step < tm_size:
        text_group = exchange(text_group, tm_size, step)
        step *= 2
    text = join_halves(text_group)
    sent, text, h_before, h_after = lax.optimization_barrier((own, text, h_before, h_after))
    t_before = lax.ppermute(sent, "tm", shift_pairs(tm_size, 1))
    t_after = lax.ppermute(sent, "tm", shift_pairs(tm_size, -1))
    time_start = lax.axis_index("tm")
    height_start = lax.axis_index("height")
    zero_index = jnp.int32(0)
    padded_ext = jnp.pad(tile_extent, ((0, 0), (1, 1), (1, 1)))
    local_ext = lax.dynamic_slice(padded_ext, (zero_index, time_start, height_start), (2, 3, 3))
    key_valid = token_masks(local_ext)
    bias = jnp.where(key_valid, 0.0, NEG).astype(jnp.float32).reshape(9, 1, tile_len)
    qvalid = key_valid[1, 1].astype(jnp.float32).reshape(tile_len, 1)

    queries = image_q[0, 0]
    near = [(own, None, 4), (h_before, None, 3), (h_after, None, 5)]
    state = attend(head_reach, queries, None, near, bias)
    t_before, t_after, state = lax.optimization_barrier((t_before, t_after, state))
    time_pair = jnp.stack([t_before, t_after])
    c_before = lax.ppermute(time_pair, "height", shift_pairs(height_size, 1))
    c_after = lax.ppermute(time_pair, "height", shift_pairs(height_size, -1))
    across = [(t_before, None, 1), (t_after, None, 7)]
    state = attend(head_reach, queries, text, across, bias, state)
    corners = [(c_before, 0, 0), (c_after, 0, 2), (c_before, 1, 6), (c_after, 1, 8)]
    attended = attend(head_reach, queries, None, corners, bias, state, qvalid)

    mp_index = lax.axis_index("mp")
    chunk = out_weight.shape[1] // mp_size
    projected = jnp.dot(attended, out_weight, preferred_element_type=jnp.float32)
    projected = projected.astype(jnp.bfloat16)
    received = []
    for step in (2, 1, 3):
        target = (mp_index + step) % mp_size
        part = lax.dynamic_slice_in_dim(projected, target * chunk, chunk, 1)
        pairs = [(i, (i + step) % mp_size) for i in range(mp_size)]
        received.append(lax.ppermute(part, "mp", pairs))
    branch = lax.dynamic_slice_in_dim(projected, mp_index * chunk, chunk, 1).astype(jnp.float32)
    for part in received:
        branch = branch + part.astype(jnp.float32)
    updated = residual[0, 0].astype(jnp.float32) + out_gate * branch
    return updated.astype(jnp.bfloat16)[None, None]


def solution(mesh):
    return jax.shard_map(
        per_device,
        mesh=mesh,
        in_specs=(
            P("tm", "height", None, "mp"),
            P("tm", "height", None, None, "mp"),
            P(None, "tm", "mp"),
            P("tm", "height", None, "mp"),
            P("mp", None),
            P("mp"),
            P("mp", None),
            P(),
        ),
        out_specs=P("tm", "height", None, "mp"),
        check_vma=False,
    )
```

```python
import math

import jax
import jax.numpy as jnp
from jax import lax
from jax.experimental import pallas as pl
from jax.experimental.pallas import tpu as pltpu
from jax.sharding import PartitionSpec as P

HD = 128
TXT = 256
TILE_F = 6
TILE_R = 8
TILE_C = 8
NEG = -1e30


def token_masks(extent_pair):
    positions = jnp.arange(TILE_F * TILE_R * TILE_C, dtype=jnp.int32)
    frame_of = positions // (TILE_R * TILE_C)
    row_of = positions // TILE_C % TILE_R
    frame_ok = frame_of < extent_pair[0][..., None]
    row_ok = row_of < extent_pair[1][..., None]
    return jnp.logical_and(frame_ok, row_ok)


def shift_pairs(devices, step):
    return [(i, i + step) for i in range(devices) if 0 <= i + step < devices]


def diagonal_pairs(tm_size, height_size, step):
    pairs = []
    for t in range(tm_size):
        if not 0 <= t + step < tm_size:
            continue
        for h in range(1, height_size - 1, 2):
            pairs.append((t * height_size + h, (t + step) * height_size + h + 1))
            pairs.append((t * height_size + h + 1, (t + step) * height_size + h))
    return pairs


def text_halves(text_kv):
    half_width = text_kv.shape[2] // 2
    half = lax.axis_index("height") % 2
    return lax.dynamic_slice_in_dim(text_kv, half * half_width, half_width, 2)


def exchange(block, devices, step):
    position = lax.axis_index("tm")
    other = lax.ppermute(block, "tm", [(i, i ^ step) for i in range(devices)])
    low_first = jnp.concatenate([block, other], axis=1)
    high_first = jnp.concatenate([other, block], axis=1)
    return jnp.where((position & step) == 0, low_first, high_first)


def join_halves(mine):
    half = lax.axis_index("height") % 2
    pairs = [(i, i ^ 1) for i in range(lax.axis_size("height"))]
    other = lax.ppermute(mine, "height", pairs)
    low_first = jnp.concatenate([mine, other], axis=2)
    high_first = jnp.concatenate([other, mine], axis=2)
    return jnp.where(half == 0, low_first, high_first)


def make_kernel(blocks, has_text, has_state, final):
    count = len(blocks)

    def kernel(reach_ref, q_ref, *rest):
        rest = list(rest)
        text_ref = rest.pop(0) if has_text else None
        tile_refs = rest[:count]
        rest = rest[count:]
        bias_ref = rest.pop(0)
        if has_state:
            m_in, l_in, acc_in = rest[:3]
            rest = rest[3:]
        if final:
            qvalid_ref = rest.pop(0)
            o_ref = rest.pop(0)
        else:
            m_out, l_out, acc_out = rest[:3]
            rest = rest[3:]
        m_ref, l_ref, acc_ref = rest
        head = pl.program_id(0)
        scale = 1.0 / math.sqrt(HD)
        q = q_ref[...]
        dims = (((1,), (1,)), ((), ()))
        if has_state:
            m_ref[...] = m_in[...]
            l_ref[...] = l_in[...]
            acc_ref[...] = acc_in[...]
        else:
            m_ref[...] = jnp.full(m_ref.shape, NEG, jnp.float32)
            l_ref[...] = jnp.zeros(l_ref.shape, jnp.float32)
            acc_ref[...] = jnp.zeros(acc_ref.shape, jnp.float32)
        if has_text:
            s = lax.dot_general(q, text_ref[0], dims, preferred_element_type=jnp.float32) * scale
            m_old = m_ref[...]
            m_new = jnp.maximum(m_old, jnp.max(s, axis=1, keepdims=True))
            alpha = jnp.exp(m_old - m_new)
            p = jnp.exp(s - m_new)
            l_ref[...] = alpha * l_ref[...] + jnp.sum(p, axis=1, keepdims=True)
            acc_ref[...] = alpha * acc_ref[...] + jnp.dot(
                p.astype(jnp.bfloat16), text_ref[1], preferred_element_type=jnp.float32
            )
            m_ref[...] = m_new
        reach_t = reach_ref[head, 0]
        reach_h = reach_ref[head, 1]
        groups = {}
        for tile_ref, b in zip(tile_refs, blocks):
            groups.setdefault((abs(b // 3 - 1), abs(b % 3 - 1)), []).append((tile_ref, b))
        for (off_t, off_h), members in groups.items():

            def block(members=members):
                scores = []
                for tile_ref, b in members:
                    s = lax.dot_general(q, tile_ref[0], dims, preferred_element_type=jnp.float32)
                    scores.append(s * scale + bias_ref[b])
                m_old = m_ref[...]
                m_new = m_old
                for s in scores:
                    m_new = jnp.maximum(m_new, jnp.max(s, axis=1, keepdims=True))
                alpha = jnp.exp(m_old - m_new)
                total = alpha * l_ref[...]
                acc = alpha * acc_ref[...]
                for s, (tile_ref, _) in zip(scores, members):
                    p = jnp.exp(s - m_new)
                    total = total + jnp.sum(p, axis=1, keepdims=True)
                    acc = acc + jnp.dot(
                        p.astype(jnp.bfloat16), tile_ref[1], preferred_element_type=jnp.float32
                    )
                l_ref[...] = total
                acc_ref[...] = acc
                m_ref[...] = m_new

            if off_t == 0 and off_h == 0:
                block()
            else:
                pl.when(jnp.logical_and(reach_t >= off_t, reach_h >= off_h))(block)
        if final:
            out = acc_ref[...] / l_ref[...]
            out = jnp.where(qvalid_ref[...] > 0, out, 0.0)
            o_ref[...] = out.astype(o_ref.dtype)
        else:
            m_out[...] = m_ref[...]
            l_out[...] = l_ref[...]
            acc_out[...] = acc_ref[...]

    return kernel


def attend(reach, queries, text, tiles, bias, state=None, qvalid=None):
    tile_len, col_width = queries.shape
    heads = col_width // HD
    blocks = [b for _, _, b in tiles]
    specs = [pl.BlockSpec((tile_len, HD), lambda h, r: (0, h))]
    args = [queries]
    if text is not None:
        specs.append(pl.BlockSpec((2, text.shape[1], HD), lambda h, r: (0, 0, h)))
        args.append(text)
    for array, index, _ in tiles:
        if index is None:
            specs.append(pl.BlockSpec((2, tile_len, HD), lambda h, r: (0, 0, h)))
        else:
            specs.append(
                pl.BlockSpec((None, 2, tile_len, HD), lambda h, r, i=index: (i, 0, 0, h))
            )
        args.append(array)
    specs.append(pl.BlockSpec(bias.shape, lambda h, r: (0, 0, 0)))
    args.append(bias)
    row_spec = pl.BlockSpec((None, tile_len, 1), lambda h, r: (h, 0, 0))
    acc_spec = pl.BlockSpec((tile_len, HD), lambda h, r: (0, h))
    if state is not None:
        specs += [row_spec, row_spec, acc_spec]
        args += list(state)
    final = qvalid is not None
    if final:
        specs.append(pl.BlockSpec(qvalid.shape, lambda h, r: (0, 0)))
        args.append(qvalid)
        out_specs = pl.BlockSpec((tile_len, HD), lambda h, r: (0, h))
        out_shape = jax.ShapeDtypeStruct((tile_len, col_width), jnp.bfloat16)
    else:
        out_specs = [row_spec, row_spec, acc_spec]
        row_shape = jax.ShapeDtypeStruct((heads, tile_len, 1), jnp.float32)
        out_shape = [row_shape, row_shape, jax.ShapeDtypeStruct((tile_len, col_width), jnp.float32)]
    grid_spec = pltpu.PrefetchScalarGridSpec(
        num_scalar_prefetch=1,
        grid=(heads,),
        in_specs=specs,
        out_specs=out_specs,
        scratch_shapes=[
            pltpu.VMEM((tile_len, 1), jnp.float32),
            pltpu.VMEM((tile_len, 1), jnp.float32),
            pltpu.VMEM((tile_len, HD), jnp.float32),
        ],
    )
    kernel = make_kernel(blocks, text is not None, state is not None, final)
    return pl.pallas_call(kernel, grid_spec=grid_spec, out_shape=out_shape)(reach, *args)


def per_device(image_q, image_kv, text_kv, residual, out_weight, out_gate, head_reach, tile_extent):
    tile_len = image_q.shape[2]
    col_width = image_q.shape[3]
    tm_size = lax.axis_size("tm")
    height_size = lax.axis_size("height")
    mp_size = lax.axis_size("mp")

    own = image_kv[0, 0]
    h_before = lax.ppermute(own, "height", shift_pairs(height_size, 1))
    h_after = lax.ppermute(own, "height", shift_pairs(height_size, -1))
    text_group = text_halves(text_kv)
    step = 1
    while step < tm_size:
        text_group = exchange(text_group, tm_size, step)
        step *= 2
    text = join_halves(text_group)
    sent, text, h_before, h_after = lax.optimization_barrier((own, text, h_before, h_after))
    t_before = lax.ppermute(sent, "tm", shift_pairs(tm_size, 1))
    t_after = lax.ppermute(sent, "tm", shift_pairs(tm_size, -1))
    diag_prev = lax.ppermute(sent, ("tm", "height"), diagonal_pairs(tm_size, height_size, 1))
    diag_next = lax.ppermute(sent, ("tm", "height"), diagonal_pairs(tm_size, height_size, -1))
    time_start = lax.axis_index("tm")
    height_start = lax.axis_index("height")
    zero_index = jnp.int32(0)
    padded_ext = jnp.pad(tile_extent, ((0, 0), (1, 1), (1, 1)))
    local_ext = lax.dynamic_slice(padded_ext, (zero_index, time_start, height_start), (2, 3, 3))
    key_valid = token_masks(local_ext)
    bias = jnp.where(key_valid, 0.0, NEG).astype(jnp.float32).reshape(9, 1, tile_len)
    qvalid = key_valid[1, 1].astype(jnp.float32).reshape(tile_len, 1)

    queries = image_q[0, 0]
    near = [(own, None, 4), (h_before, None, 3), (h_after, None, 5)]
    state = attend(head_reach, queries, None, near, bias)
    t_before, t_after, diag_prev, diag_next, state = lax.optimization_barrier(
        (t_before, t_after, diag_prev, diag_next, state)
    )
    time_pair = jnp.stack([t_before, t_after])
    even = [i for i in range(0, height_size - 1, 2)]
    near_before = lax.ppermute(time_pair, "height", [(i, i + 1) for i in even])
    near_after = lax.ppermute(time_pair, "height", [(i + 1, i) for i in even])
    across = [(t_before, None, 1), (t_after, None, 7)]
    state = attend(head_reach, queries, text, across, bias, state)
    height_index = lax.axis_index("height")
    from_before = jnp.logical_and(height_index % 2 == 0, height_index > 0)
    from_after = jnp.logical_and(height_index % 2 == 1, height_index < height_size - 1)
    corners = [
        (jnp.where(from_before, diag_prev, near_before[0]), None, 0),
        (jnp.where(from_after, diag_prev, near_after[0]), None, 2),
        (jnp.where(from_before, diag_next, near_before[1]), None, 6),
        (jnp.where(from_after, diag_next, near_after[1]), None, 8),
    ]
    attended = attend(head_reach, queries, None, corners, bias, state, qvalid)

    mp_index = lax.axis_index("mp")
    chunk = out_weight.shape[1] // mp_size
    projected = jnp.dot(attended, out_weight, preferred_element_type=jnp.float32)
    projected = projected.astype(jnp.bfloat16)
    received = []
    for step in (2, 1, 3):
        target = (mp_index + step) % mp_size
        part = lax.dynamic_slice_in_dim(projected, target * chunk, chunk, 1)
        pairs = [(i, (i + step) % mp_size) for i in range(mp_size)]
        received.append(lax.ppermute(part, "mp", pairs))
    branch = lax.dynamic_slice_in_dim(projected, mp_index * chunk, chunk, 1).astype(jnp.float32)
    for part in received:
        branch = branch + part.astype(jnp.float32)
    updated = residual[0, 0].astype(jnp.float32) + out_gate * branch
    return updated.astype(jnp.bfloat16)[None, None]


def solution(mesh):
    return jax.shard_map(
        per_device,
        mesh=mesh,
        in_specs=(
            P("tm", "height", None, "mp"),
            P("tm", "height", None, None, "mp"),
            P(None, "tm", "mp"),
            P("tm", "height", None, "mp"),
            P("mp", None),
            P("mp"),
            P("mp", None),
            P(),
        ),
        out_specs=P("tm", "height", None, "mp"),
        check_vma=False,
    )
```

```python
import math

import jax
import jax.numpy as jnp
from jax import lax
from jax.experimental import pallas as pl
from jax.experimental.pallas import tpu as pltpu
from jax.sharding import PartitionSpec as P

HD = 128
TXT = 256
TILE_F = 6
TILE_R = 8
TILE_C = 8
NEG = -1e30


def token_masks(extent_pair):
    positions = jnp.arange(TILE_F * TILE_R * TILE_C, dtype=jnp.int32)
    frame_of = positions // (TILE_R * TILE_C)
    row_of = positions // TILE_C % TILE_R
    frame_ok = frame_of < extent_pair[0][..., None]
    row_ok = row_of < extent_pair[1][..., None]
    return jnp.logical_and(frame_ok, row_ok)


def shift_pairs(devices, step):
    return [(i, i + step) for i in range(devices) if 0 <= i + step < devices]


def diagonal_pairs(tm_size, height_size, step, rise):
    pairs = []
    for t in range(tm_size):
        if not 0 <= t + step < tm_size:
            continue
        for h in range(1, height_size - 1, 2):
            if rise:
                pairs.append((t * height_size + h, (t + step) * height_size + h + 1))
            else:
                pairs.append((t * height_size + h + 1, (t + step) * height_size + h))
    return pairs


def text_halves(text_kv):
    half_width = text_kv.shape[2] // 2
    half = lax.axis_index("height") % 2
    return lax.dynamic_slice_in_dim(text_kv, half * half_width, half_width, 2)


def exchange(block, devices, step):
    position = lax.axis_index("tm")
    other = lax.ppermute(block, "tm", [(i, i ^ step) for i in range(devices)])
    low_first = jnp.concatenate([block, other], axis=1)
    high_first = jnp.concatenate([other, block], axis=1)
    return jnp.where((position & step) == 0, low_first, high_first)


def join_halves(mine):
    half = lax.axis_index("height") % 2
    pairs = [(i, i ^ 1) for i in range(lax.axis_size("height"))]
    other = lax.ppermute(mine, "height", pairs)
    low_first = jnp.concatenate([mine, other], axis=2)
    high_first = jnp.concatenate([other, mine], axis=2)
    return jnp.where(half == 0, low_first, high_first)


def load(tile_ref, part):
    main, extra = tile_ref
    if extra is None:
        return main[part]
    return main[part] + extra[part]


def make_kernel(blocks, extras, has_text, has_state, final):
    count = len(blocks)

    def kernel(reach_ref, q_ref, *rest):
        rest = list(rest)
        text_ref = rest.pop(0) if has_text else None
        tile_refs = rest[:count]
        rest = rest[count:]
        extra_refs = rest[:len(extras)]
        rest = rest[len(extras):]
        extra_of = dict(zip(extras, extra_refs))
        bias_ref = rest.pop(0)
        if has_state:
            m_in, l_in, acc_in = rest[:3]
            rest = rest[3:]
        if final:
            qvalid_ref = rest.pop(0)
            o_ref = rest.pop(0)
        else:
            m_out, l_out, acc_out = rest[:3]
            rest = rest[3:]
        m_ref, l_ref, acc_ref = rest
        head = pl.program_id(0)
        scale = 1.0 / math.sqrt(HD)
        q = q_ref[...]
        dims = (((1,), (1,)), ((), ()))
        if has_state:
            m_ref[...] = m_in[...]
            l_ref[...] = l_in[...]
            acc_ref[...] = acc_in[...]
        else:
            m_ref[...] = jnp.full(m_ref.shape, NEG, jnp.float32)
            l_ref[...] = jnp.zeros(l_ref.shape, jnp.float32)
            acc_ref[...] = jnp.zeros(acc_ref.shape, jnp.float32)
        if has_text:
            s = lax.dot_general(q, text_ref[0], dims, preferred_element_type=jnp.float32) * scale
            m_old = m_ref[...]
            m_new = jnp.maximum(m_old, jnp.max(s, axis=1, keepdims=True))
            alpha = jnp.exp(m_old - m_new)
            p = jnp.exp(s - m_new)
            l_ref[...] = alpha * l_ref[...] + jnp.sum(p, axis=1, keepdims=True)
            acc_ref[...] = alpha * acc_ref[...] + jnp.dot(
                p.astype(jnp.bfloat16), text_ref[1], preferred_element_type=jnp.float32
            )
            m_ref[...] = m_new
        reach_t = reach_ref[head, 0]
        reach_h = reach_ref[head, 1]
        groups = {}
        for tile_ref, b in zip(tile_refs, blocks):
            tile_ref = (tile_ref, extra_of.get(b))
            groups.setdefault((abs(b // 3 - 1), abs(b % 3 - 1)), []).append((tile_ref, b))
        for (off_t, off_h), members in groups.items():

            def block(members=members):
                scores = []
                for tile_ref, b in members:
                    s = lax.dot_general(q, load(tile_ref, 0), dims, preferred_element_type=jnp.float32)
                    scores.append(s * scale + bias_ref[b])
                m_old = m_ref[...]
                m_new = m_old
                for s in scores:
                    m_new = jnp.maximum(m_new, jnp.max(s, axis=1, keepdims=True))
                alpha = jnp.exp(m_old - m_new)
                total = alpha * l_ref[...]
                acc = alpha * acc_ref[...]
                for s, (tile_ref, _) in zip(scores, members):
                    p = jnp.exp(s - m_new)
                    total = total + jnp.sum(p, axis=1, keepdims=True)
                    acc = acc + jnp.dot(
                        p.astype(jnp.bfloat16), load(tile_ref, 1), preferred_element_type=jnp.float32
                    )
                l_ref[...] = total
                acc_ref[...] = acc
                m_ref[...] = m_new

            if off_t == 0 and off_h == 0:
                block()
            else:
                pl.when(jnp.logical_and(reach_t >= off_t, reach_h >= off_h))(block)
        if final:
            out = acc_ref[...] / l_ref[...]
            out = jnp.where(qvalid_ref[...] > 0, out, 0.0)
            o_ref[...] = out.astype(o_ref.dtype)
        else:
            m_out[...] = m_ref[...]
            l_out[...] = l_ref[...]
            acc_out[...] = acc_ref[...]

    return kernel


def attend(reach, queries, text, tiles, bias, state=None, qvalid=None, extra=None):
    tile_len, col_width = queries.shape
    heads = col_width // HD
    blocks = [b for _, _, b in tiles]
    specs = [pl.BlockSpec((tile_len, HD), lambda h, r: (0, h))]
    args = [queries]
    if text is not None:
        specs.append(pl.BlockSpec((2, text.shape[1], HD), lambda h, r: (0, 0, h)))
        args.append(text)
    def add_tile(array, index):
        if index is None:
            specs.append(pl.BlockSpec((2, tile_len, HD), lambda h, r: (0, 0, h)))
        else:
            specs.append(
                pl.BlockSpec((None, 2, tile_len, HD), lambda h, r, i=index: (i, 0, 0, h))
            )
        args.append(array)

    for array, index, _ in tiles:
        add_tile(array, index)
    extras = [b for b in blocks if b in (extra or {})]
    for b in extras:
        add_tile(*extra[b])
    specs.append(pl.BlockSpec(bias.shape, lambda h, r: (0, 0, 0)))
    args.append(bias)
    row_spec = pl.BlockSpec((None, tile_len, 1), lambda h, r: (h, 0, 0))
    acc_spec = pl.BlockSpec((tile_len, HD), lambda h, r: (0, h))
    if state is not None:
        specs += [row_spec, row_spec, acc_spec]
        args += list(state)
    final = qvalid is not None
    if final:
        specs.append(pl.BlockSpec(qvalid.shape, lambda h, r: (0, 0)))
        args.append(qvalid)
        out_specs = pl.BlockSpec((tile_len, HD), lambda h, r: (0, h))
        out_shape = jax.ShapeDtypeStruct((tile_len, col_width), jnp.bfloat16)
    else:
        out_specs = [row_spec, row_spec, acc_spec]
        row_shape = jax.ShapeDtypeStruct((heads, tile_len, 1), jnp.float32)
        out_shape = [row_shape, row_shape, jax.ShapeDtypeStruct((tile_len, col_width), jnp.float32)]
    grid_spec = pltpu.PrefetchScalarGridSpec(
        num_scalar_prefetch=1,
        grid=(heads,),
        in_specs=specs,
        out_specs=out_specs,
        scratch_shapes=[
            pltpu.VMEM((tile_len, 1), jnp.float32),
            pltpu.VMEM((tile_len, 1), jnp.float32),
            pltpu.VMEM((tile_len, HD), jnp.float32),
        ],
    )
    kernel = make_kernel(blocks, extras, text is not None, state is not None, final)
    return pl.pallas_call(kernel, grid_spec=grid_spec, out_shape=out_shape)(reach, *args)


def per_device(image_q, image_kv, text_kv, residual, out_weight, out_gate, head_reach, tile_extent):
    tile_len = image_q.shape[2]
    col_width = image_q.shape[3]
    tm_size = lax.axis_size("tm")
    height_size = lax.axis_size("height")
    mp_size = lax.axis_size("mp")

    own = image_kv[0, 0]
    h_before = lax.ppermute(own, "height", shift_pairs(height_size, 1))
    h_after = lax.ppermute(own, "height", shift_pairs(height_size, -1))
    text_group = text_halves(text_kv)
    step = 1
    while step < tm_size:
        text_group = exchange(text_group, tm_size, step)
        step *= 2
    text = join_halves(text_group)
    sent, text, h_before, h_after = lax.optimization_barrier((own, text, h_before, h_after))
    t_before = lax.ppermute(sent, "tm", shift_pairs(tm_size, 1))
    t_after = lax.ppermute(sent, "tm", shift_pairs(tm_size, -1))
    time_start = lax.axis_index("tm")
    height_start = lax.axis_index("height")
    zero_index = jnp.int32(0)
    padded_ext = jnp.pad(tile_extent, ((0, 0), (1, 1), (1, 1)))
    local_ext = lax.dynamic_slice(padded_ext, (zero_index, time_start, height_start), (2, 3, 3))
    key_valid = token_masks(local_ext)
    bias = jnp.where(key_valid, 0.0, NEG).astype(jnp.float32).reshape(9, 1, tile_len)
    qvalid = key_valid[1, 1].astype(jnp.float32).reshape(tile_len, 1)

    queries = image_q[0, 0]
    near = [(own, None, 4), (h_before, None, 3), (h_after, None, 5)]
    state = attend(head_reach, queries, None, near, bias)
    t_before, t_after, sent, state = lax.optimization_barrier((t_before, t_after, sent, state))
    time_pair = jnp.stack([t_before, t_after])
    even = list(range(0, height_size - 1, 2))
    odd = list(range(1, height_size - 1, 2))
    near_before = lax.ppermute(time_pair, "height", [(i, i + 1) for i in even])
    near_after = lax.ppermute(time_pair, "height", [(i + 1, i) for i in even])
    cross_before = lax.ppermute(t_before, "height", [(i, i + 1) for i in odd])
    cross_after = lax.ppermute(t_before, "height", [(i + 1, i) for i in odd])
    diag_down = lax.ppermute(sent, ("tm", "height"), diagonal_pairs(tm_size, height_size, -1, True))
    diag_up = lax.ppermute(sent, ("tm", "height"), diagonal_pairs(tm_size, height_size, -1, False))
    across = [(t_before, None, 1), (t_after, None, 7)]
    state = attend(head_reach, queries, text, across, bias, state)
    corners = [(near_before, 0, 0), (near_after, 0, 2), (near_before, 1, 6), (near_after, 1, 8)]
    extra = {0: (cross_before, None), 2: (cross_after, None), 6: (diag_down, None), 8: (diag_up, None)}
    attended = attend(head_reach, queries, None, corners, bias, state, qvalid, extra)

    mp_index = lax.axis_index("mp")
    chunk = out_weight.shape[1] // mp_size
    projected = jnp.dot(attended, out_weight, preferred_element_type=jnp.float32)
    projected = projected.astype(jnp.bfloat16)
    received = []
    for step in (2, 1, 3):
        target = (mp_index + step) % mp_size
        part = lax.dynamic_slice_in_dim(projected, target * chunk, chunk, 1)
        pairs = [(i, (i + step) % mp_size) for i in range(mp_size)]
        received.append(lax.ppermute(part, "mp", pairs))
    branch = lax.dynamic_slice_in_dim(projected, mp_index * chunk, chunk, 1).astype(jnp.float32)
    for part in received:
        branch = branch + part.astype(jnp.float32)
    updated = residual[0, 0].astype(jnp.float32) + out_gate * branch
    return updated.astype(jnp.bfloat16)[None, None]


def solution(mesh):
    return jax.shard_map(
        per_device,
        mesh=mesh,
        in_specs=(
            P("tm", "height", None, "mp"),
            P("tm", "height", None, None, "mp"),
            P(None, "tm", "mp"),
            P("tm", "height", None, "mp"),
            P("mp", None),
            P("mp"),
            P("mp", None),
            P(),
        ),
        out_specs=P("tm", "height", None, "mp"),
        check_vma=False,
    )
```

```python
import math

import jax
import jax.numpy as jnp
from jax import lax
from jax.experimental import pallas as pl
from jax.experimental.pallas import tpu as pltpu
from jax.sharding import PartitionSpec as P

HD = 128
TXT = 256
TILE_F = 6
TILE_R = 8
TILE_C = 8
NEG = -1e30


def token_masks(extent_pair):
    positions = jnp.arange(TILE_F * TILE_R * TILE_C, dtype=jnp.int32)
    frame_of = positions // (TILE_R * TILE_C)
    row_of = positions // TILE_C % TILE_R
    frame_ok = frame_of < extent_pair[0][..., None]
    row_ok = row_of < extent_pair[1][..., None]
    return jnp.logical_and(frame_ok, row_ok)


def shift_pairs(devices, step):
    return [(i, i + step) for i in range(devices) if 0 <= i + step < devices]


def text_halves(text_kv):
    half_width = text_kv.shape[2] // 2
    half = lax.axis_index("height") % 2
    return lax.dynamic_slice_in_dim(text_kv, half * half_width, half_width, 2)


def exchange(block, devices, step):
    position = lax.axis_index("tm")
    other = lax.ppermute(block, "tm", [(i, i ^ step) for i in range(devices)])
    low_first = jnp.concatenate([block, other], axis=1)
    high_first = jnp.concatenate([other, block], axis=1)
    return jnp.where((position & step) == 0, low_first, high_first)


def join_halves(mine):
    half = lax.axis_index("height") % 2
    pairs = [(i, i ^ 1) for i in range(lax.axis_size("height"))]
    other = lax.ppermute(mine, "height", pairs)
    low_first = jnp.concatenate([mine, other], axis=2)
    high_first = jnp.concatenate([other, mine], axis=2)
    return jnp.where(half == 0, low_first, high_first)


def make_kernel(blocks, has_text, has_state, final):
    count = len(blocks)

    def kernel(reach_ref, q_ref, *rest):
        rest = list(rest)
        text_ref = rest.pop(0) if has_text else None
        tile_refs = rest[:count]
        rest = rest[count:]
        bias_ref = rest.pop(0)
        if has_state:
            m_in, l_in, acc_in = rest[:3]
            rest = rest[3:]
        if final:
            qvalid_ref = rest.pop(0)
            o_ref = rest.pop(0)
        else:
            m_out, l_out, acc_out = rest[:3]
            rest = rest[3:]
        m_ref, l_ref, acc_ref = rest
        head = pl.program_id(0)
        scale = 1.0 / math.sqrt(HD)
        q = q_ref[...]
        dims = (((1,), (1,)), ((), ()))
        if has_state:
            m_ref[...] = m_in[...]
            l_ref[...] = l_in[...]
            acc_ref[...] = acc_in[...]
        else:
            m_ref[...] = jnp.full(m_ref.shape, NEG, jnp.float32)
            l_ref[...] = jnp.zeros(l_ref.shape, jnp.float32)
            acc_ref[...] = jnp.zeros(acc_ref.shape, jnp.float32)
        if has_text:
            s = lax.dot_general(q, text_ref[0], dims, preferred_element_type=jnp.float32) * scale
            m_old = m_ref[...]
            m_new = jnp.maximum(m_old, jnp.max(s, axis=1, keepdims=True))
            alpha = jnp.exp(m_old - m_new)
            p = jnp.exp(s - m_new)
            l_ref[...] = alpha * l_ref[...] + jnp.sum(p, axis=1, keepdims=True)
            acc_ref[...] = alpha * acc_ref[...] + jnp.dot(
                p.astype(jnp.bfloat16), text_ref[1], preferred_element_type=jnp.float32
            )
            m_ref[...] = m_new
        reach_t = reach_ref[head, 0]
        reach_h = reach_ref[head, 1]
        groups = {}
        for tile_ref, b in zip(tile_refs, blocks):
            groups.setdefault((abs(b // 3 - 1), abs(b % 3 - 1)), []).append((tile_ref, b))
        for (off_t, off_h), members in groups.items():

            def block(members=members):
                scores = []
                for tile_ref, b in members:
                    s = lax.dot_general(q, tile_ref[0], dims, preferred_element_type=jnp.float32)
                    scores.append(s * scale + bias_ref[b])
                m_old = m_ref[...]
                m_new = m_old
                for s in scores:
                    m_new = jnp.maximum(m_new, jnp.max(s, axis=1, keepdims=True))
                alpha = jnp.exp(m_old - m_new)
                total = alpha * l_ref[...]
                acc = alpha * acc_ref[...]
                for s, (tile_ref, _) in zip(scores, members):
                    p = jnp.exp(s - m_new)
                    total = total + jnp.sum(p, axis=1, keepdims=True)
                    acc = acc + jnp.dot(
                        p.astype(jnp.bfloat16), tile_ref[1], preferred_element_type=jnp.float32
                    )
                l_ref[...] = total
                acc_ref[...] = acc
                m_ref[...] = m_new

            if off_t == 0 and off_h == 0:
                block()
            else:
                pl.when(jnp.logical_and(reach_t >= off_t, reach_h >= off_h))(block)
        if final:
            out = acc_ref[...] / l_ref[...]
            out = jnp.where(qvalid_ref[...] > 0, out, 0.0)
            o_ref[...] = out.astype(o_ref.dtype)
        else:
            m_out[...] = m_ref[...]
            l_out[...] = l_ref[...]
            acc_out[...] = acc_ref[...]

    return kernel


def attend(reach, queries, text, tiles, bias, state=None, qvalid=None):
    tile_len, col_width = queries.shape
    heads = col_width // HD
    blocks = [b for _, _, b in tiles]
    specs = [pl.BlockSpec((tile_len, HD), lambda h, r: (0, h))]
    args = [queries]
    if text is not None:
        specs.append(pl.BlockSpec((2, text.shape[1], HD), lambda h, r: (0, 0, h)))
        args.append(text)
    for array, index, _ in tiles:
        if index is None:
            specs.append(pl.BlockSpec((2, tile_len, HD), lambda h, r: (0, 0, h)))
        else:
            specs.append(
                pl.BlockSpec((None, 2, tile_len, HD), lambda h, r, i=index: (i, 0, 0, h))
            )
        args.append(array)
    specs.append(pl.BlockSpec(bias.shape, lambda h, r: (0, 0, 0)))
    args.append(bias)
    row_spec = pl.BlockSpec((None, tile_len, 1), lambda h, r: (h, 0, 0))
    acc_spec = pl.BlockSpec((tile_len, HD), lambda h, r: (0, h))
    if state is not None:
        specs += [row_spec, row_spec, acc_spec]
        args += list(state)
    final = qvalid is not None
    if final:
        specs.append(pl.BlockSpec(qvalid.shape, lambda h, r: (0, 0)))
        args.append(qvalid)
        out_specs = pl.BlockSpec((tile_len, HD), lambda h, r: (0, h))
        out_shape = jax.ShapeDtypeStruct((tile_len, col_width), jnp.bfloat16)
    else:
        out_specs = [row_spec, row_spec, acc_spec]
        row_shape = jax.ShapeDtypeStruct((heads, tile_len, 1), jnp.float32)
        out_shape = [row_shape, row_shape, jax.ShapeDtypeStruct((tile_len, col_width), jnp.float32)]
    grid_spec = pltpu.PrefetchScalarGridSpec(
        num_scalar_prefetch=1,
        grid=(heads,),
        in_specs=specs,
        out_specs=out_specs,
        scratch_shapes=[
            pltpu.VMEM((tile_len, 1), jnp.float32),
            pltpu.VMEM((tile_len, 1), jnp.float32),
            pltpu.VMEM((tile_len, HD), jnp.float32),
        ],
    )
    kernel = make_kernel(blocks, text is not None, state is not None, final)
    return pl.pallas_call(kernel, grid_spec=grid_spec, out_shape=out_shape)(reach, *args)


def per_device(image_q, image_kv, text_kv, residual, out_weight, out_gate, head_reach, tile_extent):
    tile_len = image_q.shape[2]
    col_width = image_q.shape[3]
    tm_size = lax.axis_size("tm")
    height_size = lax.axis_size("height")
    mp_size = lax.axis_size("mp")

    own = image_kv[0, 0]
    h_before = lax.ppermute(own, "height", shift_pairs(height_size, 1))
    h_after = lax.ppermute(own, "height", shift_pairs(height_size, -1))
    text_group = text_halves(text_kv)
    step = 1
    while step < tm_size:
        text_group = exchange(text_group, tm_size, step)
        step *= 2
    text = join_halves(text_group)
    time_start = lax.axis_index("tm")
    height_start = lax.axis_index("height")
    zero_index = jnp.int32(0)
    padded_ext = jnp.pad(tile_extent, ((0, 0), (1, 1), (1, 1)))
    local_ext = lax.dynamic_slice(padded_ext, (zero_index, time_start, height_start), (2, 3, 3))
    key_valid = token_masks(local_ext)
    bias = jnp.where(key_valid, 0.0, NEG).astype(jnp.float32).reshape(9, 1, tile_len)
    qvalid = key_valid[1, 1].astype(jnp.float32).reshape(tile_len, 1)

    sent, text, h_before, h_after, bias, qvalid = lax.optimization_barrier(
        (own, text, h_before, h_after, bias, qvalid)
    )
    t_before = lax.ppermute(sent, "tm", shift_pairs(tm_size, 1))
    t_after = lax.ppermute(sent, "tm", shift_pairs(tm_size, -1))
    queries = image_q[0, 0]
    near = [(own, None, 4), (h_before, None, 3), (h_after, None, 5)]
    state = attend(head_reach, queries, None, near, bias)
    t_before, t_after, state = lax.optimization_barrier((t_before, t_after, state))
    time_pair = jnp.stack([t_before, t_after])
    c_before = lax.ppermute(time_pair, "height", shift_pairs(height_size, 1))
    c_after = lax.ppermute(time_pair, "height", shift_pairs(height_size, -1))
    across = [(t_before, None, 1), (t_after, None, 7)]
    state = attend(head_reach, queries, text, across, bias, state)
    corners = [(c_before, 0, 0), (c_after, 0, 2), (c_before, 1, 6), (c_after, 1, 8)]
    attended = attend(head_reach, queries, None, corners, bias, state, qvalid)

    mp_index = lax.axis_index("mp")
    chunk = out_weight.shape[1] // mp_size
    projected = jnp.dot(attended, out_weight, preferred_element_type=jnp.float32)
    projected = projected.astype(jnp.bfloat16)
    received = []
    for step in (2, 1, 3):
        target = (mp_index + step) % mp_size
        part = lax.dynamic_slice_in_dim(projected, target * chunk, chunk, 1)
        pairs = [(i, (i + step) % mp_size) for i in range(mp_size)]
        received.append(lax.ppermute(part, "mp", pairs))
    branch = lax.dynamic_slice_in_dim(projected, mp_index * chunk, chunk, 1).astype(jnp.float32)
    for part in received:
        branch = branch + part.astype(jnp.float32)
    updated = residual[0, 0].astype(jnp.float32) + out_gate * branch
    return updated.astype(jnp.bfloat16)[None, None]


def solution(mesh):
    return jax.shard_map(
        per_device,
        mesh=mesh,
        in_specs=(
            P("tm", "height", None, "mp"),
            P("tm", "height", None, None, "mp"),
            P(None, "tm", "mp"),
            P("tm", "height", None, "mp"),
            P("mp", None),
            P("mp"),
            P("mp", None),
            P(),
        ),
        out_specs=P("tm", "height", None, "mp"),
        check_vma=False,
    )
```

```python
import math

import jax
import jax.numpy as jnp
from jax import lax
from jax.experimental import pallas as pl
from jax.experimental.pallas import tpu as pltpu
from jax.sharding import PartitionSpec as P

HD = 128
TXT = 256
TILE_F = 6
TILE_R = 8
TILE_C = 8
NEG = -1e30


def token_masks(extent_pair):
    positions = jnp.arange(TILE_F * TILE_R * TILE_C, dtype=jnp.int32)
    frame_of = positions // (TILE_R * TILE_C)
    row_of = positions // TILE_C % TILE_R
    frame_ok = frame_of < extent_pair[0][..., None]
    row_ok = row_of < extent_pair[1][..., None]
    return jnp.logical_and(frame_ok, row_ok)


def shift_pairs(devices, step):
    return [(i, i + step) for i in range(devices) if 0 <= i + step < devices]


def diagonal_pairs(tm_size, height_size, step):
    pairs = []
    for t in range(tm_size):
        if not 0 <= t + step < tm_size:
            continue
        for h in range(1, height_size - 1, 2):
            pairs.append((t * height_size + h, (t + step) * height_size + h + 1))
            pairs.append((t * height_size + h + 1, (t + step) * height_size + h))
    return pairs


def text_halves(text_kv):
    half_width = text_kv.shape[2] // 2
    half = lax.axis_index("height") % 2
    return lax.dynamic_slice_in_dim(text_kv, half * half_width, half_width, 2)


def exchange(block, devices, step):
    position = lax.axis_index("tm")
    other = lax.ppermute(block, "tm", [(i, i ^ step) for i in range(devices)])
    low_first = jnp.concatenate([block, other], axis=1)
    high_first = jnp.concatenate([other, block], axis=1)
    return jnp.where((position & step) == 0, low_first, high_first)


def join_halves(mine):
    half = lax.axis_index("height") % 2
    pairs = [(i, i ^ 1) for i in range(lax.axis_size("height"))]
    other = lax.ppermute(mine, "height", pairs)
    low_first = jnp.concatenate([mine, other], axis=2)
    high_first = jnp.concatenate([other, mine], axis=2)
    return jnp.where(half == 0, low_first, high_first)


def make_kernel(blocks, has_text, has_state, final):
    count = len(blocks)

    def kernel(reach_ref, q_ref, *rest):
        rest = list(rest)
        text_ref = rest.pop(0) if has_text else None
        tile_refs = rest[:count]
        rest = rest[count:]
        bias_ref = rest.pop(0)
        if has_state:
            m_in, l_in, acc_in = rest[:3]
            rest = rest[3:]
        if final:
            qvalid_ref = rest.pop(0)
            o_ref = rest.pop(0)
        else:
            m_out, l_out, acc_out = rest[:3]
            rest = rest[3:]
        m_ref, l_ref, acc_ref = rest
        head = pl.program_id(0)
        scale = 1.0 / math.sqrt(HD)
        q = q_ref[...]
        dims = (((1,), (1,)), ((), ()))
        if has_state:
            m_ref[...] = m_in[...]
            l_ref[...] = l_in[...]
            acc_ref[...] = acc_in[...]
        else:
            m_ref[...] = jnp.full(m_ref.shape, NEG, jnp.float32)
            l_ref[...] = jnp.zeros(l_ref.shape, jnp.float32)
            acc_ref[...] = jnp.zeros(acc_ref.shape, jnp.float32)
        if has_text:
            s = lax.dot_general(q, text_ref[0], dims, preferred_element_type=jnp.float32) * scale
            m_old = m_ref[...]
            m_new = jnp.maximum(m_old, jnp.max(s, axis=1, keepdims=True))
            alpha = jnp.exp(m_old - m_new)
            p = jnp.exp(s - m_new)
            l_ref[...] = alpha * l_ref[...] + jnp.sum(p, axis=1, keepdims=True)
            acc_ref[...] = alpha * acc_ref[...] + jnp.dot(
                p.astype(jnp.bfloat16), text_ref[1], preferred_element_type=jnp.float32
            )
            m_ref[...] = m_new
        reach_t = reach_ref[head, 0]
        reach_h = reach_ref[head, 1]
        groups = {}
        for tile_ref, b in zip(tile_refs, blocks):
            groups.setdefault((abs(b // 3 - 1), abs(b % 3 - 1)), []).append((tile_ref, b))
        for (off_t, off_h), members in groups.items():

            def block(members=members):
                scores = []
                for tile_ref, b in members:
                    s = lax.dot_general(q, tile_ref[0], dims, preferred_element_type=jnp.float32)
                    scores.append(s * scale + bias_ref[b])
                m_old = m_ref[...]
                m_new = m_old
                for s in scores:
                    m_new = jnp.maximum(m_new, jnp.max(s, axis=1, keepdims=True))
                alpha = jnp.exp(m_old - m_new)
                total = alpha * l_ref[...]
                acc = alpha * acc_ref[...]
                for s, (tile_ref, _) in zip(scores, members):
                    p = jnp.exp(s - m_new)
                    total = total + jnp.sum(p, axis=1, keepdims=True)
                    acc = acc + jnp.dot(
                        p.astype(jnp.bfloat16), tile_ref[1], preferred_element_type=jnp.float32
                    )
                l_ref[...] = total
                acc_ref[...] = acc
                m_ref[...] = m_new

            if off_t == 0 and off_h == 0:
                block()
            else:
                pl.when(jnp.logical_and(reach_t >= off_t, reach_h >= off_h))(block)
        if final:
            out = acc_ref[...] / l_ref[...]
            out = jnp.where(qvalid_ref[...] > 0, out, 0.0)
            o_ref[...] = out.astype(o_ref.dtype)
        else:
            m_out[...] = m_ref[...]
            l_out[...] = l_ref[...]
            acc_out[...] = acc_ref[...]

    return kernel


def attend(reach, queries, text, tiles, bias, state=None, qvalid=None):
    tile_len, col_width = queries.shape
    heads = col_width // HD
    blocks = [b for _, _, b in tiles]
    specs = [pl.BlockSpec((tile_len, HD), lambda h, r: (0, h))]
    args = [queries]
    if text is not None:
        specs.append(pl.BlockSpec((2, text.shape[1], HD), lambda h, r: (0, 0, h)))
        args.append(text)
    for array, index, _ in tiles:
        if index is None:
            specs.append(pl.BlockSpec((2, tile_len, HD), lambda h, r: (0, 0, h)))
        else:
            specs.append(
                pl.BlockSpec((None, 2, tile_len, HD), lambda h, r, i=index: (i, 0, 0, h))
            )
        args.append(array)
    specs.append(pl.BlockSpec(bias.shape, lambda h, r: (0, 0, 0)))
    args.append(bias)
    row_spec = pl.BlockSpec((None, tile_len, 1), lambda h, r: (h, 0, 0))
    acc_spec = pl.BlockSpec((tile_len, HD), lambda h, r: (0, h))
    if state is not None:
        specs += [row_spec, row_spec, acc_spec]
        args += list(state)
    final = qvalid is not None
    if final:
        specs.append(pl.BlockSpec(qvalid.shape, lambda h, r: (0, 0)))
        args.append(qvalid)
        out_specs = pl.BlockSpec((tile_len, HD), lambda h, r: (0, h))
        out_shape = jax.ShapeDtypeStruct((tile_len, col_width), jnp.bfloat16)
    else:
        out_specs = [row_spec, row_spec, acc_spec]
        row_shape = jax.ShapeDtypeStruct((heads, tile_len, 1), jnp.float32)
        out_shape = [row_shape, row_shape, jax.ShapeDtypeStruct((tile_len, col_width), jnp.float32)]
    grid_spec = pltpu.PrefetchScalarGridSpec(
        num_scalar_prefetch=1,
        grid=(heads,),
        in_specs=specs,
        out_specs=out_specs,
        scratch_shapes=[
            pltpu.VMEM((tile_len, 1), jnp.float32),
            pltpu.VMEM((tile_len, 1), jnp.float32),
            pltpu.VMEM((tile_len, HD), jnp.float32),
        ],
    )
    kernel = make_kernel(blocks, text is not None, state is not None, final)
    return pl.pallas_call(kernel, grid_spec=grid_spec, out_shape=out_shape)(reach, *args)


def per_device(image_q, image_kv, text_kv, residual, out_weight, out_gate, head_reach, tile_extent):
    tile_len = image_q.shape[2]
    col_width = image_q.shape[3]
    tm_size = lax.axis_size("tm")
    height_size = lax.axis_size("height")
    mp_size = lax.axis_size("mp")

    own = image_kv[0, 0]
    h_before = lax.ppermute(own, "height", shift_pairs(height_size, 1))
    h_after = lax.ppermute(own, "height", shift_pairs(height_size, -1))
    text_group = text_halves(text_kv)
    step = 1
    while step < tm_size:
        text_group = exchange(text_group, tm_size, step)
        step *= 2
    text = join_halves(text_group)
    time_start = lax.axis_index("tm")
    height_start = lax.axis_index("height")
    zero_index = jnp.int32(0)
    padded_ext = jnp.pad(tile_extent, ((0, 0), (1, 1), (1, 1)))
    local_ext = lax.dynamic_slice(padded_ext, (zero_index, time_start, height_start), (2, 3, 3))
    key_valid = token_masks(local_ext)
    bias = jnp.where(key_valid, 0.0, NEG).astype(jnp.float32).reshape(9, 1, tile_len)
    qvalid = key_valid[1, 1].astype(jnp.float32).reshape(tile_len, 1)

    sent, text, h_before, h_after, bias, qvalid = lax.optimization_barrier(
        (own, text, h_before, h_after, bias, qvalid)
    )
    t_before = lax.ppermute(sent, "tm", shift_pairs(tm_size, 1))
    t_after = lax.ppermute(sent, "tm", shift_pairs(tm_size, -1))
    queries = image_q[0, 0]
    near = [(own, None, 4), (h_before, None, 3), (h_after, None, 5)]
    state = attend(head_reach, queries, None, near, bias)
    t_before, t_after, sent, state = lax.optimization_barrier((t_before, t_after, sent, state))
    earlier_low = lax.ppermute(t_before, "height", shift_pairs(height_size, 1))
    earlier_high = lax.ppermute(t_before, "height", shift_pairs(height_size, -1))
    partner = lax.ppermute(t_after, "height", [(i, i ^ 1) for i in range(height_size)])
    diagonal = lax.ppermute(sent, ("tm", "height"), diagonal_pairs(tm_size, height_size, -1))
    across = [(t_before, None, 1), (t_after, None, 7)]
    state = attend(head_reach, queries, text, across, bias, state)
    odd_height = lax.axis_index("height") % 2 == 1
    corners = [
        (earlier_low, None, 0),
        (earlier_high, None, 2),
        (jnp.where(odd_height, partner, diagonal), None, 6),
        (jnp.where(odd_height, diagonal, partner), None, 8),
    ]
    attended = attend(head_reach, queries, None, corners, bias, state, qvalid)

    mp_index = lax.axis_index("mp")
    chunk = out_weight.shape[1] // mp_size
    projected = jnp.dot(attended, out_weight, preferred_element_type=jnp.float32)
    projected = projected.astype(jnp.bfloat16)
    received = []
    for step in (2, 1, 3):
        target = (mp_index + step) % mp_size
        part = lax.dynamic_slice_in_dim(projected, target * chunk, chunk, 1)
        pairs = [(i, (i + step) % mp_size) for i in range(mp_size)]
        received.append(lax.ppermute(part, "mp", pairs))
    branch = lax.dynamic_slice_in_dim(projected, mp_index * chunk, chunk, 1).astype(jnp.float32)
    for part in received:
        branch = branch + part.astype(jnp.float32)
    updated = residual[0, 0].astype(jnp.float32) + out_gate * branch
    return updated.astype(jnp.bfloat16)[None, None]


def solution(mesh):
    return jax.shard_map(
        per_device,
        mesh=mesh,
        in_specs=(
            P("tm", "height", None, "mp"),
            P("tm", "height", None, None, "mp"),
            P(None, "tm", "mp"),
            P("tm", "height", None, "mp"),
            P("mp", None),
            P("mp"),
            P("mp", None),
            P(),
        ),
        out_specs=P("tm", "height", None, "mp"),
        check_vma=False,
    )
```

```python
import math

import jax
import jax.numpy as jnp
from jax import lax
from jax.experimental import pallas as pl
from jax.experimental.pallas import tpu as pltpu
from jax.sharding import PartitionSpec as P

HD = 128
TXT = 256
TILE_F = 6
TILE_R = 8
TILE_C = 8
NEG = -1e30


def token_masks(extent_pair):
    positions = jnp.arange(TILE_F * TILE_R * TILE_C, dtype=jnp.int32)
    frame_of = positions // (TILE_R * TILE_C)
    row_of = positions // TILE_C % TILE_R
    frame_ok = frame_of < extent_pair[0][..., None]
    row_ok = row_of < extent_pair[1][..., None]
    return jnp.logical_and(frame_ok, row_ok)


def shift_pairs(devices, step):
    return [(i, i + step) for i in range(devices) if 0 <= i + step < devices]


def diagonal_pairs(tm_size, height_size, step):
    pairs = []
    for t in range(tm_size):
        if not 0 <= t + step < tm_size:
            continue
        for h in range(1, height_size - 1, 2):
            pairs.append((t * height_size + h, (t + step) * height_size + h + 1))
            pairs.append((t * height_size + h + 1, (t + step) * height_size + h))
    return pairs


def text_halves(text_kv):
    half_width = text_kv.shape[2] // 2
    half = lax.axis_index("height") % 2
    return lax.dynamic_slice_in_dim(text_kv, half * half_width, half_width, 2)


def exchange(block, devices, step):
    position = lax.axis_index("tm")
    other = lax.ppermute(block, "tm", [(i, i ^ step) for i in range(devices)])
    low_first = jnp.concatenate([block, other], axis=1)
    high_first = jnp.concatenate([other, block], axis=1)
    return jnp.where((position & step) == 0, low_first, high_first)


def join_halves(mine):
    half = lax.axis_index("height") % 2
    pairs = [(i, i ^ 1) for i in range(lax.axis_size("height"))]
    other = lax.ppermute(mine, "height", pairs)
    low_first = jnp.concatenate([mine, other], axis=2)
    high_first = jnp.concatenate([other, mine], axis=2)
    return jnp.where(half == 0, low_first, high_first)


def make_kernel(blocks, has_text, has_state, final):
    count = len(blocks)

    def kernel(reach_ref, q_ref, *rest):
        rest = list(rest)
        text_ref = rest.pop(0) if has_text else None
        tile_refs = rest[:count]
        rest = rest[count:]
        bias_ref = rest.pop(0)
        if has_state:
            m_in, l_in, acc_in = rest[:3]
            rest = rest[3:]
        if final:
            qvalid_ref = rest.pop(0)
            o_ref = rest.pop(0)
        else:
            m_out, l_out, acc_out = rest[:3]
            rest = rest[3:]
        m_ref, l_ref, acc_ref = rest
        head = pl.program_id(0)
        scale = 1.0 / math.sqrt(HD)
        q = q_ref[...]
        dims = (((1,), (1,)), ((), ()))
        if has_state:
            m_ref[...] = m_in[...]
            l_ref[...] = l_in[...]
            acc_ref[...] = acc_in[...]
        else:
            m_ref[...] = jnp.full(m_ref.shape, NEG, jnp.float32)
            l_ref[...] = jnp.zeros(l_ref.shape, jnp.float32)
            acc_ref[...] = jnp.zeros(acc_ref.shape, jnp.float32)
        if has_text:
            s = lax.dot_general(q, text_ref[0], dims, preferred_element_type=jnp.float32) * scale
            m_old = m_ref[...]
            m_new = jnp.maximum(m_old, jnp.max(s, axis=1, keepdims=True))
            alpha = jnp.exp(m_old - m_new)
            p = jnp.exp(s - m_new)
            l_ref[...] = alpha * l_ref[...] + jnp.sum(p, axis=1, keepdims=True)
            acc_ref[...] = alpha * acc_ref[...] + jnp.dot(
                p.astype(jnp.bfloat16), text_ref[1], preferred_element_type=jnp.float32
            )
            m_ref[...] = m_new
        reach_t = reach_ref[head, 0]
        reach_h = reach_ref[head, 1]
        groups = {}
        for tile_ref, b in zip(tile_refs, blocks):
            groups.setdefault((abs(b // 3 - 1), abs(b % 3 - 1)), []).append((tile_ref, b))
        for (off_t, off_h), members in groups.items():

            def block(members=members):
                scores = []
                for tile_ref, b in members:
                    s = lax.dot_general(q, tile_ref[0], dims, preferred_element_type=jnp.float32)
                    scores.append(s * scale + bias_ref[b])
                m_old = m_ref[...]
                m_new = m_old
                for s in scores:
                    m_new = jnp.maximum(m_new, jnp.max(s, axis=1, keepdims=True))
                alpha = jnp.exp(m_old - m_new)
                total = alpha * l_ref[...]
                acc = alpha * acc_ref[...]
                for s, (tile_ref, _) in zip(scores, members):
                    p = jnp.exp(s - m_new)
                    total = total + jnp.sum(p, axis=1, keepdims=True)
                    acc = acc + jnp.dot(
                        p.astype(jnp.bfloat16), tile_ref[1], preferred_element_type=jnp.float32
                    )
                l_ref[...] = total
                acc_ref[...] = acc
                m_ref[...] = m_new

            if off_t == 0 and off_h == 0:
                block()
            else:
                pl.when(jnp.logical_and(reach_t >= off_t, reach_h >= off_h))(block)
        if final:
            out = acc_ref[...] / l_ref[...]
            out = jnp.where(qvalid_ref[...] > 0, out, 0.0)
            o_ref[...] = out.astype(o_ref.dtype)
        else:
            m_out[...] = m_ref[...]
            l_out[...] = l_ref[...]
            acc_out[...] = acc_ref[...]

    return kernel


def attend(reach, queries, text, tiles, bias, state=None, qvalid=None):
    tile_len, col_width = queries.shape
    heads = col_width // HD
    blocks = [b for _, _, b in tiles]
    specs = [pl.BlockSpec((tile_len, HD), lambda h, r: (0, h))]
    args = [queries]
    if text is not None:
        specs.append(pl.BlockSpec((2, text.shape[1], HD), lambda h, r: (0, 0, h)))
        args.append(text)
    for array, index, _ in tiles:
        if index is None:
            specs.append(pl.BlockSpec((2, tile_len, HD), lambda h, r: (0, 0, h)))
        else:
            specs.append(
                pl.BlockSpec((None, 2, tile_len, HD), lambda h, r, i=index: (i, 0, 0, h))
            )
        args.append(array)
    specs.append(pl.BlockSpec(bias.shape, lambda h, r: (0, 0, 0)))
    args.append(bias)
    row_spec = pl.BlockSpec((None, tile_len, 1), lambda h, r: (h, 0, 0))
    acc_spec = pl.BlockSpec((tile_len, HD), lambda h, r: (0, h))
    if state is not None:
        specs += [row_spec, row_spec, acc_spec]
        args += list(state)
    final = qvalid is not None
    if final:
        specs.append(pl.BlockSpec(qvalid.shape, lambda h, r: (0, 0)))
        args.append(qvalid)
        out_specs = pl.BlockSpec((tile_len, HD), lambda h, r: (0, h))
        out_shape = jax.ShapeDtypeStruct((tile_len, col_width), jnp.bfloat16)
    else:
        out_specs = [row_spec, row_spec, acc_spec]
        row_shape = jax.ShapeDtypeStruct((heads, tile_len, 1), jnp.float32)
        out_shape = [row_shape, row_shape, jax.ShapeDtypeStruct((tile_len, col_width), jnp.float32)]
    grid_spec = pltpu.PrefetchScalarGridSpec(
        num_scalar_prefetch=1,
        grid=(heads,),
        in_specs=specs,
        out_specs=out_specs,
        scratch_shapes=[
            pltpu.VMEM((tile_len, 1), jnp.float32),
            pltpu.VMEM((tile_len, 1), jnp.float32),
            pltpu.VMEM((tile_len, HD), jnp.float32),
        ],
    )
    kernel = make_kernel(blocks, text is not None, state is not None, final)
    return pl.pallas_call(kernel, grid_spec=grid_spec, out_shape=out_shape)(reach, *args)


def per_device(image_q, image_kv, text_kv, residual, out_weight, out_gate, head_reach, tile_extent):
    tile_len = image_q.shape[2]
    col_width = image_q.shape[3]
    tm_size = lax.axis_size("tm")
    height_size = lax.axis_size("height")
    mp_size = lax.axis_size("mp")

    own = image_kv[0, 0]
    h_before = lax.ppermute(own, "height", shift_pairs(height_size, 1))
    h_after = lax.ppermute(own, "height", shift_pairs(height_size, -1))
    text_group = text_halves(text_kv)
    step = 1
    while step < tm_size:
        text_group = exchange(text_group, tm_size, step)
        step *= 2
    text = join_halves(text_group)
    time_start = lax.axis_index("tm")
    height_start = lax.axis_index("height")
    zero_index = jnp.int32(0)
    padded_ext = jnp.pad(tile_extent, ((0, 0), (1, 1), (1, 1)))
    local_ext = lax.dynamic_slice(padded_ext, (zero_index, time_start, height_start), (2, 3, 3))
    key_valid = token_masks(local_ext)
    bias = jnp.where(key_valid, 0.0, NEG).astype(jnp.float32).reshape(9, 1, tile_len)
    qvalid = key_valid[1, 1].astype(jnp.float32).reshape(tile_len, 1)

    sent, text, h_before, h_after, bias, qvalid = lax.optimization_barrier(
        (own, text, h_before, h_after, bias, qvalid)
    )
    t_before = lax.ppermute(sent, "tm", shift_pairs(tm_size, 1))
    t_after = lax.ppermute(sent, "tm", shift_pairs(tm_size, -1))
    queries = image_q[0, 0]
    near = [(own, None, 4), (h_before, None, 3), (h_after, None, 5)]
    state = attend(head_reach, queries, text, near, bias)
    t_before, t_after, sent, state = lax.optimization_barrier((t_before, t_after, sent, state))
    earlier_low = lax.ppermute(t_before, "height", shift_pairs(height_size, 1))
    earlier_high = lax.ppermute(t_before, "height", shift_pairs(height_size, -1))
    partner = lax.ppermute(t_after, "height", [(i, i ^ 1) for i in range(height_size)])
    diagonal = lax.ppermute(sent, ("tm", "height"), diagonal_pairs(tm_size, height_size, -1))
    across = [(t_before, None, 1), (t_after, None, 7)]
    state = attend(head_reach, queries, None, across, bias, state)
    odd_height = lax.axis_index("height") % 2 == 1
    corners = [
        (earlier_low, None, 0),
        (earlier_high, None, 2),
        (jnp.where(odd_height, partner, diagonal), None, 6),
        (jnp.where(odd_height, diagonal, partner), None, 8),
    ]
    attended = attend(head_reach, queries, None, corners, bias, state, qvalid)

    mp_index = lax.axis_index("mp")
    chunk = out_weight.shape[1] // mp_size
    projected = jnp.dot(attended, out_weight, preferred_element_type=jnp.float32)
    projected = projected.astype(jnp.bfloat16)
    received = []
    for step in (2, 1, 3):
        target = (mp_index + step) % mp_size
        part = lax.dynamic_slice_in_dim(projected, target * chunk, chunk, 1)
        pairs = [(i, (i + step) % mp_size) for i in range(mp_size)]
        received.append(lax.ppermute(part, "mp", pairs))
    branch = lax.dynamic_slice_in_dim(projected, mp_index * chunk, chunk, 1).astype(jnp.float32)
    for part in received:
        branch = branch + part.astype(jnp.float32)
    updated = residual[0, 0].astype(jnp.float32) + out_gate * branch
    return updated.astype(jnp.bfloat16)[None, None]


def solution(mesh):
    return jax.shard_map(
        per_device,
        mesh=mesh,
        in_specs=(
            P("tm", "height", None, "mp"),
            P("tm", "height", None, None, "mp"),
            P(None, "tm", "mp"),
            P("tm", "height", None, "mp"),
            P("mp", None),
            P("mp"),
            P("mp", None),
            P(),
        ),
        out_specs=P("tm", "height", None, "mp"),
        check_vma=False,
    )
```

```python
import math

import jax
import jax.numpy as jnp
from jax import lax
from jax.experimental import pallas as pl
from jax.experimental.pallas import tpu as pltpu
from jax.sharding import PartitionSpec as P

HD = 128
TXT = 256
TILE_F = 6
TILE_R = 8
TILE_C = 8
NEG = -1e30


def token_masks(extent_pair):
    positions = jnp.arange(TILE_F * TILE_R * TILE_C, dtype=jnp.int32)
    frame_of = positions // (TILE_R * TILE_C)
    row_of = positions // TILE_C % TILE_R
    frame_ok = frame_of < extent_pair[0][..., None]
    row_ok = row_of < extent_pair[1][..., None]
    return jnp.logical_and(frame_ok, row_ok)


def shift_pairs(devices, step):
    return [(i, i + step) for i in range(devices) if 0 <= i + step < devices]


def diagonal_pairs(tm_size, height_size, step):
    pairs = []
    for t in range(tm_size):
        if not 0 <= t + step < tm_size:
            continue
        for h in range(1, height_size - 1, 2):
            pairs.append((t * height_size + h, (t + step) * height_size + h + 1))
            pairs.append((t * height_size + h + 1, (t + step) * height_size + h))
    return pairs


def text_halves(text_kv):
    half_width = text_kv.shape[2] // 2
    half = lax.axis_index("height") % 2
    return lax.dynamic_slice_in_dim(text_kv, half * half_width, half_width, 2)


def exchange(block, devices, step):
    position = lax.axis_index("tm")
    other = lax.ppermute(block, "tm", [(i, i ^ step) for i in range(devices)])
    low_first = jnp.concatenate([block, other], axis=1)
    high_first = jnp.concatenate([other, block], axis=1)
    return jnp.where((position & step) == 0, low_first, high_first)


def join_halves(mine):
    half = lax.axis_index("height") % 2
    pairs = [(i, i ^ 1) for i in range(lax.axis_size("height"))]
    other = lax.ppermute(mine, "height", pairs)
    low_first = jnp.concatenate([mine, other], axis=2)
    high_first = jnp.concatenate([other, mine], axis=2)
    return jnp.where(half == 0, low_first, high_first)


def make_kernel(blocks, extras, has_text, has_state, final, heads):
    count = len(blocks)

    def kernel(reach_ref, q_ref, *rest):
        rest = list(rest)
        text_ref = rest.pop(0) if has_text else None
        tile_refs = rest[:count]
        rest = rest[count:]
        extra_of = dict(zip(extras, rest[:len(extras)]))
        rest = rest[len(extras):]
        bias_ref = rest.pop(0)
        if has_state:
            m_in, l_in, acc_in = rest[:3]
            rest = rest[3:]
        if final:
            qvalid_ref = rest.pop(0)
            o_ref = rest.pop(0)
        else:
            m_out, l_out, acc_out = rest[:3]
            rest = rest[3:]
        m_ref, l_ref, acc_ref = rest
        head = pl.program_id(0)
        scale = 1.0 / math.sqrt(HD)
        q = q_ref[...]
        dims = (((1,), (1,)), ((), ()))
        if has_state:
            m_ref[...] = m_in[...]
            l_ref[...] = l_in[...]
            acc_ref[...] = acc_in[...]
        else:
            m_ref[...] = jnp.full(m_ref.shape, NEG, jnp.float32)
            l_ref[...] = jnp.zeros(l_ref.shape, jnp.float32)
            acc_ref[...] = jnp.zeros(acc_ref.shape, jnp.float32)
        if has_text:
            s = lax.dot_general(q, text_ref[0], dims, preferred_element_type=jnp.float32) * scale
            m_old = m_ref[...]
            m_new = jnp.maximum(m_old, jnp.max(s, axis=1, keepdims=True))
            alpha = jnp.exp(m_old - m_new)
            p = jnp.exp(s - m_new)
            l_ref[...] = alpha * l_ref[...] + jnp.sum(p, axis=1, keepdims=True)
            acc_ref[...] = alpha * acc_ref[...] + jnp.dot(
                p.astype(jnp.bfloat16), text_ref[1], preferred_element_type=jnp.float32
            )
            m_ref[...] = m_new
        reach_t = reach_ref[head, 0]
        reach_h = reach_ref[head, 1]
        weight = reach_ref[heads, 0].astype(jnp.float32)

        def load(tile_ref, b, part):
            if b not in extra_of:
                return tile_ref[part]
            main = tile_ref[part].astype(jnp.float32)
            other = extra_of[b][part].astype(jnp.float32)
            return (main * weight + other * (1.0 - weight)).astype(jnp.bfloat16)
        groups = {}
        for tile_ref, b in zip(tile_refs, blocks):
            groups.setdefault((abs(b // 3 - 1), abs(b % 3 - 1)), []).append((tile_ref, b))
        for (off_t, off_h), members in groups.items():

            def block(members=members):
                scores = []
                for tile_ref, b in members:
                    s = lax.dot_general(q, load(tile_ref, b, 0), dims, preferred_element_type=jnp.float32)
                    scores.append(s * scale + bias_ref[b])
                m_old = m_ref[...]
                m_new = m_old
                for s in scores:
                    m_new = jnp.maximum(m_new, jnp.max(s, axis=1, keepdims=True))
                alpha = jnp.exp(m_old - m_new)
                total = alpha * l_ref[...]
                acc = alpha * acc_ref[...]
                for s, (tile_ref, b) in zip(scores, members):
                    p = jnp.exp(s - m_new)
                    total = total + jnp.sum(p, axis=1, keepdims=True)
                    acc = acc + jnp.dot(
                        p.astype(jnp.bfloat16), load(tile_ref, b, 1), preferred_element_type=jnp.float32
                    )
                l_ref[...] = total
                acc_ref[...] = acc
                m_ref[...] = m_new

            if off_t == 0 and off_h == 0:
                block()
            else:
                pl.when(jnp.logical_and(reach_t >= off_t, reach_h >= off_h))(block)
        if final:
            out = acc_ref[...] / l_ref[...]
            out = jnp.where(qvalid_ref[...] > 0, out, 0.0)
            o_ref[...] = out.astype(o_ref.dtype)
        else:
            m_out[...] = m_ref[...]
            l_out[...] = l_ref[...]
            acc_out[...] = acc_ref[...]

    return kernel


def attend(reach, queries, text, tiles, bias, state=None, qvalid=None, extra=None):
    tile_len, col_width = queries.shape
    heads = col_width // HD
    blocks = [b for _, _, b in tiles]
    specs = [pl.BlockSpec((tile_len, HD), lambda h, r: (0, h))]
    args = [queries]
    if text is not None:
        specs.append(pl.BlockSpec((2, text.shape[1], HD), lambda h, r: (0, 0, h)))
        args.append(text)
    def add_tile(array, index):
        if index is None:
            specs.append(pl.BlockSpec((2, tile_len, HD), lambda h, r: (0, 0, h)))
        else:
            specs.append(
                pl.BlockSpec((None, 2, tile_len, HD), lambda h, r, i=index: (i, 0, 0, h))
            )
        args.append(array)

    for array, index, _ in tiles:
        add_tile(array, index)
    extras = [b for b in blocks if b in (extra or {})]
    for b in extras:
        add_tile(*extra[b])
    specs.append(pl.BlockSpec(bias.shape, lambda h, r: (0, 0, 0)))
    args.append(bias)
    row_spec = pl.BlockSpec((None, tile_len, 1), lambda h, r: (h, 0, 0))
    acc_spec = pl.BlockSpec((tile_len, HD), lambda h, r: (0, h))
    if state is not None:
        specs += [row_spec, row_spec, acc_spec]
        args += list(state)
    final = qvalid is not None
    if final:
        specs.append(pl.BlockSpec(qvalid.shape, lambda h, r: (0, 0)))
        args.append(qvalid)
        out_specs = pl.BlockSpec((tile_len, HD), lambda h, r: (0, h))
        out_shape = jax.ShapeDtypeStruct((tile_len, col_width), jnp.bfloat16)
    else:
        out_specs = [row_spec, row_spec, acc_spec]
        row_shape = jax.ShapeDtypeStruct((heads, tile_len, 1), jnp.float32)
        out_shape = [row_shape, row_shape, jax.ShapeDtypeStruct((tile_len, col_width), jnp.float32)]
    grid_spec = pltpu.PrefetchScalarGridSpec(
        num_scalar_prefetch=1,
        grid=(heads,),
        in_specs=specs,
        out_specs=out_specs,
        scratch_shapes=[
            pltpu.VMEM((tile_len, 1), jnp.float32),
            pltpu.VMEM((tile_len, 1), jnp.float32),
            pltpu.VMEM((tile_len, HD), jnp.float32),
        ],
    )
    kernel = make_kernel(blocks, extras, text is not None, state is not None, final, heads)
    return pl.pallas_call(kernel, grid_spec=grid_spec, out_shape=out_shape)(reach, *args)


def per_device(image_q, image_kv, text_kv, residual, out_weight, out_gate, head_reach, tile_extent):
    tile_len = image_q.shape[2]
    col_width = image_q.shape[3]
    tm_size = lax.axis_size("tm")
    height_size = lax.axis_size("height")
    mp_size = lax.axis_size("mp")

    own = image_kv[0, 0]
    h_before = lax.ppermute(own, "height", shift_pairs(height_size, 1))
    h_after = lax.ppermute(own, "height", shift_pairs(height_size, -1))
    text_group = text_halves(text_kv)
    step = 1
    while step < tm_size:
        text_group = exchange(text_group, tm_size, step)
        step *= 2
    text = join_halves(text_group)
    time_start = lax.axis_index("tm")
    height_start = lax.axis_index("height")
    zero_index = jnp.int32(0)
    padded_ext = jnp.pad(tile_extent, ((0, 0), (1, 1), (1, 1)))
    local_ext = lax.dynamic_slice(padded_ext, (zero_index, time_start, height_start), (2, 3, 3))
    key_valid = token_masks(local_ext)
    bias = jnp.where(key_valid, 0.0, NEG).astype(jnp.float32).reshape(9, 1, tile_len)
    qvalid = key_valid[1, 1].astype(jnp.float32).reshape(tile_len, 1)

    sent, text, h_before, h_after, bias, qvalid = lax.optimization_barrier(
        (own, text, h_before, h_after, bias, qvalid)
    )
    t_before = lax.ppermute(sent, "tm", shift_pairs(tm_size, 1))
    t_after = lax.ppermute(sent, "tm", shift_pairs(tm_size, -1))
    queries = image_q[0, 0]
    odd = (lax.axis_index("height") % 2).astype(head_reach.dtype)
    reach_odd = jnp.concatenate([head_reach, jnp.stack([odd, odd])[None]], axis=0)
    near = [(own, None, 4), (h_before, None, 3), (h_after, None, 5)]
    state = attend(head_reach, queries, text, near, bias)
    t_before, t_after, sent, state = lax.optimization_barrier((t_before, t_after, sent, state))
    earlier_low = lax.ppermute(t_before, "height", shift_pairs(height_size, 1))
    earlier_high = lax.ppermute(t_before, "height", shift_pairs(height_size, -1))
    partner = lax.ppermute(t_after, "height", [(i, i ^ 1) for i in range(height_size)])
    diagonal = lax.ppermute(sent, ("tm", "height"), diagonal_pairs(tm_size, height_size, -1))
    across = [(t_before, None, 1), (t_after, None, 7)]
    state = attend(head_reach, queries, None, across, bias, state)
    corners = [(earlier_low, None, 0), (earlier_high, None, 2), (partner, None, 6), (diagonal, None, 8)]
    extra = {6: (diagonal, None), 8: (partner, None)}
    attended = attend(reach_odd, queries, None, corners, bias, state, qvalid, extra)

    mp_index = lax.axis_index("mp")
    chunk = out_weight.shape[1] // mp_size
    projected = jnp.dot(attended, out_weight, preferred_element_type=jnp.float32)
    projected = projected.astype(jnp.bfloat16)
    received = []
    for step in (2, 1, 3):
        target = (mp_index + step) % mp_size
        part = lax.dynamic_slice_in_dim(projected, target * chunk, chunk, 1)
        pairs = [(i, (i + step) % mp_size) for i in range(mp_size)]
        received.append(lax.ppermute(part, "mp", pairs))
    branch = lax.dynamic_slice_in_dim(projected, mp_index * chunk, chunk, 1).astype(jnp.float32)
    for part in received:
        branch = branch + part.astype(jnp.float32)
    updated = residual[0, 0].astype(jnp.float32) + out_gate * branch
    return updated.astype(jnp.bfloat16)[None, None]


def solution(mesh):
    return jax.shard_map(
        per_device,
        mesh=mesh,
        in_specs=(
            P("tm", "height", None, "mp"),
            P("tm", "height", None, None, "mp"),
            P(None, "tm", "mp"),
            P("tm", "height", None, "mp"),
            P("mp", None),
            P("mp"),
            P("mp", None),
            P(),
        ),
        out_specs=P("tm", "height", None, "mp"),
        check_vma=False,
    )
```

```python
import math

import jax
import jax.numpy as jnp
from jax import lax
from jax.experimental import pallas as pl
from jax.experimental.pallas import tpu as pltpu
from jax.sharding import PartitionSpec as P

HD = 128
TXT = 256
TILE_F = 6
TILE_R = 8
TILE_C = 8
NEG = -1e30


def token_masks(extent_pair):
    positions = jnp.arange(TILE_F * TILE_R * TILE_C, dtype=jnp.int32)
    frame_of = positions // (TILE_R * TILE_C)
    row_of = positions // TILE_C % TILE_R
    frame_ok = frame_of < extent_pair[0][..., None]
    row_ok = row_of < extent_pair[1][..., None]
    return jnp.logical_and(frame_ok, row_ok)


def shift_pairs(devices, step):
    return [(i, i + step) for i in range(devices) if 0 <= i + step < devices]


def diagonal_pairs(tm_size, height_size, step):
    pairs = []
    for t in range(tm_size):
        if not 0 <= t + step < tm_size:
            continue
        for h in range(1, height_size - 1, 2):
            pairs.append((t * height_size + h, (t + step) * height_size + h + 1))
            pairs.append((t * height_size + h + 1, (t + step) * height_size + h))
    return pairs


def text_halves(text_kv):
    half_width = text_kv.shape[2] // 2
    half = lax.axis_index("height") % 2
    return lax.dynamic_slice_in_dim(text_kv, half * half_width, half_width, 2)


def exchange(block, devices, step):
    position = lax.axis_index("tm")
    other = lax.ppermute(block, "tm", [(i, i ^ step) for i in range(devices)])
    low_first = jnp.concatenate([block, other], axis=1)
    high_first = jnp.concatenate([other, block], axis=1)
    return jnp.where((position & step) == 0, low_first, high_first)


def join_halves(mine):
    half = lax.axis_index("height") % 2
    pairs = [(i, i ^ 1) for i in range(lax.axis_size("height"))]
    other = lax.ppermute(mine, "height", pairs)
    low_first = jnp.concatenate([mine, other], axis=2)
    high_first = jnp.concatenate([other, mine], axis=2)
    return jnp.where(half == 0, low_first, high_first)


def make_kernel(blocks, has_text, has_state, final):
    count = len(blocks)

    def kernel(reach_ref, q_ref, *rest):
        rest = list(rest)
        text_ref = rest.pop(0) if has_text else None
        tile_refs = rest[:count]
        rest = rest[count:]
        bias_ref = rest.pop(0)
        if has_state:
            m_in, l_in, acc_in = rest[:3]
            rest = rest[3:]
        if final:
            qvalid_ref = rest.pop(0)
            o_ref = rest.pop(0)
        else:
            m_out, l_out, acc_out = rest[:3]
            rest = rest[3:]
        m_ref, l_ref, acc_ref = rest
        head = pl.program_id(0)
        scale = 1.0 / math.sqrt(HD)
        q = q_ref[...]
        dims = (((1,), (1,)), ((), ()))
        if has_state:
            m_ref[...] = m_in[...]
            l_ref[...] = l_in[...]
            acc_ref[...] = acc_in[...]
        else:
            m_ref[...] = jnp.full(m_ref.shape, NEG, jnp.float32)
            l_ref[...] = jnp.zeros(l_ref.shape, jnp.float32)
            acc_ref[...] = jnp.zeros(acc_ref.shape, jnp.float32)
        if has_text:
            s = lax.dot_general(q, text_ref[0], dims, preferred_element_type=jnp.float32) * scale
            m_old = m_ref[...]
            m_new = jnp.maximum(m_old, jnp.max(s, axis=1, keepdims=True))
            alpha = jnp.exp(m_old - m_new)
            p = jnp.exp(s - m_new)
            l_ref[...] = alpha * l_ref[...] + jnp.sum(p, axis=1, keepdims=True)
            acc_ref[...] = alpha * acc_ref[...] + jnp.dot(
                p.astype(jnp.bfloat16), text_ref[1], preferred_element_type=jnp.float32
            )
            m_ref[...] = m_new
        reach_t = reach_ref[head, 0]
        reach_h = reach_ref[head, 1]
        groups = {}
        for tile_ref, b in zip(tile_refs, blocks):
            groups.setdefault((abs(b // 3 - 1), abs(b % 3 - 1)), []).append((tile_ref, b))
        for (off_t, off_h), members in groups.items():

            def block(members=members):
                scores = []
                for tile_ref, b in members:
                    s = lax.dot_general(q, tile_ref[0], dims, preferred_element_type=jnp.float32)
                    scores.append(s * scale + bias_ref[b])
                m_old = m_ref[...]
                m_new = m_old
                for s in scores:
                    m_new = jnp.maximum(m_new, jnp.max(s, axis=1, keepdims=True))
                alpha = jnp.exp(m_old - m_new)
                total = alpha * l_ref[...]
                acc = alpha * acc_ref[...]
                for s, (tile_ref, _) in zip(scores, members):
                    p = jnp.exp(s - m_new)
                    total = total + jnp.sum(p, axis=1, keepdims=True)
                    acc = acc + jnp.dot(
                        p.astype(jnp.bfloat16), tile_ref[1], preferred_element_type=jnp.float32
                    )
                l_ref[...] = total
                acc_ref[...] = acc
                m_ref[...] = m_new

            if off_t == 0 and off_h == 0:
                block()
            else:
                pl.when(jnp.logical_and(reach_t >= off_t, reach_h >= off_h))(block)
        if final:
            out = acc_ref[...] / l_ref[...]
            out = jnp.where(qvalid_ref[...] > 0, out, 0.0)
            o_ref[...] = out.astype(o_ref.dtype)
        else:
            m_out[...] = m_ref[...]
            l_out[...] = l_ref[...]
            acc_out[...] = acc_ref[...]

    return kernel


def attend(reach, queries, text, tiles, bias, state=None, qvalid=None):
    tile_len, col_width = queries.shape
    heads = col_width // HD
    blocks = [b for _, _, b in tiles]
    specs = [pl.BlockSpec((tile_len, HD), lambda h, r: (0, h))]
    args = [queries]
    if text is not None:
        specs.append(pl.BlockSpec((2, text.shape[1], HD), lambda h, r: (0, 0, h)))
        args.append(text)
    for array, index, _ in tiles:
        if index is None:
            specs.append(pl.BlockSpec((2, tile_len, HD), lambda h, r: (0, 0, h)))
        else:
            specs.append(
                pl.BlockSpec((None, 2, tile_len, HD), lambda h, r, i=index: (i, 0, 0, h))
            )
        args.append(array)
    specs.append(pl.BlockSpec(bias.shape, lambda h, r: (0, 0, 0)))
    args.append(bias)
    row_spec = pl.BlockSpec((None, tile_len, 1), lambda h, r: (h, 0, 0))
    acc_spec = pl.BlockSpec((tile_len, HD), lambda h, r: (0, h))
    if state is not None:
        specs += [row_spec, row_spec, acc_spec]
        args += list(state)
    final = qvalid is not None
    if final:
        specs.append(pl.BlockSpec(qvalid.shape, lambda h, r: (0, 0)))
        args.append(qvalid)
        out_specs = pl.BlockSpec((tile_len, HD), lambda h, r: (0, h))
        out_shape = jax.ShapeDtypeStruct((tile_len, col_width), jnp.bfloat16)
    else:
        out_specs = [row_spec, row_spec, acc_spec]
        row_shape = jax.ShapeDtypeStruct((heads, tile_len, 1), jnp.float32)
        out_shape = [row_shape, row_shape, jax.ShapeDtypeStruct((tile_len, col_width), jnp.float32)]
    grid_spec = pltpu.PrefetchScalarGridSpec(
        num_scalar_prefetch=1,
        grid=(heads,),
        in_specs=specs,
        out_specs=out_specs,
        scratch_shapes=[
            pltpu.VMEM((tile_len, 1), jnp.float32),
            pltpu.VMEM((tile_len, 1), jnp.float32),
            pltpu.VMEM((tile_len, HD), jnp.float32),
        ],
    )
    kernel = make_kernel(blocks, text is not None, state is not None, final)
    return pl.pallas_call(kernel, grid_spec=grid_spec, out_shape=out_shape)(reach, *args)


def per_device(image_q, image_kv, text_kv, residual, out_weight, out_gate, head_reach, tile_extent):
    tile_len = image_q.shape[2]
    col_width = image_q.shape[3]
    tm_size = lax.axis_size("tm")
    height_size = lax.axis_size("height")
    mp_size = lax.axis_size("mp")

    own = image_kv[0, 0]
    h_before = lax.ppermute(own, "height", shift_pairs(height_size, 1))
    h_after = lax.ppermute(own, "height", shift_pairs(height_size, -1))
    text_group = text_halves(text_kv)
    step = 1
    while 2 * step < tm_size:
        text_group = exchange(text_group, tm_size, step)
        step *= 2
    time_start = lax.axis_index("tm")
    height_start = lax.axis_index("height")
    zero_index = jnp.int32(0)
    padded_ext = jnp.pad(tile_extent, ((0, 0), (1, 1), (1, 1)))
    local_ext = lax.dynamic_slice(padded_ext, (zero_index, time_start, height_start), (2, 3, 3))
    key_valid = token_masks(local_ext)
    bias = jnp.where(key_valid, 0.0, NEG).astype(jnp.float32).reshape(9, 1, tile_len)
    qvalid = key_valid[1, 1].astype(jnp.float32).reshape(tile_len, 1)

    sent, text_group, h_before, h_after, bias, qvalid = lax.optimization_barrier(
        (own, text_group, h_before, h_after, bias, qvalid)
    )
    t_before = lax.ppermute(sent, "tm", shift_pairs(tm_size, 1))
    t_after = lax.ppermute(sent, "tm", shift_pairs(tm_size, -1))
    if step < tm_size:
        text_group = exchange(text_group, tm_size, step)
    text = join_halves(text_group)
    queries = image_q[0, 0]
    near = [(own, None, 4), (h_before, None, 3), (h_after, None, 5)]
    state = attend(head_reach, queries, text, near, bias)
    t_before, t_after, sent, state = lax.optimization_barrier((t_before, t_after, sent, state))
    earlier_low = lax.ppermute(t_before, "height", shift_pairs(height_size, 1))
    earlier_high = lax.ppermute(t_before, "height", shift_pairs(height_size, -1))
    partner = lax.ppermute(t_after, "height", [(i, i ^ 1) for i in range(height_size)])
    diagonal = lax.ppermute(sent, ("tm", "height"), diagonal_pairs(tm_size, height_size, -1))
    across = [(t_before, None, 1), (t_after, None, 7)]
    state = attend(head_reach, queries, None, across, bias, state)
    odd_height = lax.axis_index("height") % 2 == 1
    corners = [
        (earlier_low, None, 0),
        (earlier_high, None, 2),
        (jnp.where(odd_height, partner, diagonal), None, 6),
        (jnp.where(odd_height, diagonal, partner), None, 8),
    ]
    attended = attend(head_reach, queries, None, corners, bias, state, qvalid)

    mp_index = lax.axis_index("mp")
    chunk = out_weight.shape[1] // mp_size
    projected = jnp.dot(attended, out_weight, preferred_element_type=jnp.float32)
    projected = projected.astype(jnp.bfloat16)
    received = []
    for step in (2, 1, 3):
        target = (mp_index + step) % mp_size
        part = lax.dynamic_slice_in_dim(projected, target * chunk, chunk, 1)
        pairs = [(i, (i + step) % mp_size) for i in range(mp_size)]
        received.append(lax.ppermute(part, "mp", pairs))
    branch = lax.dynamic_slice_in_dim(projected, mp_index * chunk, chunk, 1).astype(jnp.float32)
    for part in received:
        branch = branch + part.astype(jnp.float32)
    updated = residual[0, 0].astype(jnp.float32) + out_gate * branch
    return updated.astype(jnp.bfloat16)[None, None]


def solution(mesh):
    return jax.shard_map(
        per_device,
        mesh=mesh,
        in_specs=(
            P("tm", "height", None, "mp"),
            P("tm", "height", None, None, "mp"),
            P(None, "tm", "mp"),
            P("tm", "height", None, "mp"),
            P("mp", None),
            P("mp"),
            P("mp", None),
            P(),
        ),
        out_specs=P("tm", "height", None, "mp"),
        check_vma=False,
    )
```

```python
import math

import jax
import jax.numpy as jnp
from jax import lax
from jax.experimental import pallas as pl
from jax.experimental.pallas import tpu as pltpu
from jax.sharding import PartitionSpec as P

HD = 128
TXT = 256
TILE_F = 6
TILE_R = 8
TILE_C = 8
NEG = -1e30


def token_masks(extent_pair):
    positions = jnp.arange(TILE_F * TILE_R * TILE_C, dtype=jnp.int32)
    frame_of = positions // (TILE_R * TILE_C)
    row_of = positions // TILE_C % TILE_R
    frame_ok = frame_of < extent_pair[0][..., None]
    row_ok = row_of < extent_pair[1][..., None]
    return jnp.logical_and(frame_ok, row_ok)


def shift_pairs(devices, step):
    return [(i, i + step) for i in range(devices) if 0 <= i + step < devices]


def diagonal_pairs(tm_size, height_size, step):
    pairs = []
    for t in range(tm_size):
        if not 0 <= t + step < tm_size:
            continue
        for h in range(1, height_size - 1, 2):
            pairs.append((t * height_size + h, (t + step) * height_size + h + 1))
            pairs.append((t * height_size + h + 1, (t + step) * height_size + h))
    return pairs


def text_halves(text_kv):
    half_width = text_kv.shape[2] // 2
    half = lax.axis_index("height") % 2
    return lax.dynamic_slice_in_dim(text_kv, half * half_width, half_width, 2)


def exchange(block, devices, step):
    position = lax.axis_index("tm")
    other = lax.ppermute(block, "tm", [(i, i ^ step) for i in range(devices)])
    low_first = jnp.concatenate([block, other], axis=1)
    high_first = jnp.concatenate([other, block], axis=1)
    return jnp.where((position & step) == 0, low_first, high_first)


def join_halves(mine):
    half = lax.axis_index("height") % 2
    pairs = [(i, i ^ 1) for i in range(lax.axis_size("height"))]
    other = lax.ppermute(mine, "height", pairs)
    low_first = jnp.concatenate([mine, other], axis=2)
    high_first = jnp.concatenate([other, mine], axis=2)
    return jnp.where(half == 0, low_first, high_first)


def make_kernel(blocks, has_text, has_state, final):
    count = len(blocks)

    def kernel(reach_ref, q_ref, *rest):
        rest = list(rest)
        text_ref = rest.pop(0) if has_text else None
        tile_refs = rest[:count]
        rest = rest[count:]
        bias_ref = rest.pop(0)
        if has_state:
            m_in, l_in, acc_in = rest[:3]
            rest = rest[3:]
        if final:
            qvalid_ref = rest.pop(0)
            o_ref = rest.pop(0)
        else:
            m_out, l_out, acc_out = rest[:3]
            rest = rest[3:]
        m_ref, l_ref, acc_ref = rest
        head = pl.program_id(0)
        scale = 1.0 / math.sqrt(HD)
        q = q_ref[...]
        dims = (((1,), (1,)), ((), ()))
        if has_state:
            m_ref[...] = m_in[...]
            l_ref[...] = l_in[...]
            acc_ref[...] = acc_in[...]
        else:
            m_ref[...] = jnp.full(m_ref.shape, NEG, jnp.float32)
            l_ref[...] = jnp.zeros(l_ref.shape, jnp.float32)
            acc_ref[...] = jnp.zeros(acc_ref.shape, jnp.float32)
        if has_text:
            s = lax.dot_general(q, text_ref[0], dims, preferred_element_type=jnp.float32) * scale
            m_old = m_ref[...]
            m_new = jnp.maximum(m_old, jnp.max(s, axis=1, keepdims=True))
            alpha = jnp.exp(m_old - m_new)
            p = jnp.exp(s - m_new)
            l_ref[...] = alpha * l_ref[...] + jnp.sum(p, axis=1, keepdims=True)
            acc_ref[...] = alpha * acc_ref[...] + jnp.dot(
                p.astype(jnp.bfloat16), text_ref[1], preferred_element_type=jnp.float32
            )
            m_ref[...] = m_new
        reach_t = reach_ref[head, 0]
        reach_h = reach_ref[head, 1]
        groups = {}
        for tile_ref, b in zip(tile_refs, blocks):
            groups.setdefault((abs(b // 3 - 1), abs(b % 3 - 1)), []).append((tile_ref, b))
        for (off_t, off_h), members in groups.items():

            def block(members=members):
                scores = []
                for tile_ref, b in members:
                    s = lax.dot_general(q, tile_ref[0], dims, preferred_element_type=jnp.float32)
                    scores.append(s * scale + bias_ref[b])
                m_old = m_ref[...]
                m_new = m_old
                for s in scores:
                    m_new = jnp.maximum(m_new, jnp.max(s, axis=1, keepdims=True))
                alpha = jnp.exp(m_old - m_new)
                total = alpha * l_ref[...]
                acc = alpha * acc_ref[...]
                for s, (tile_ref, _) in zip(scores, members):
                    p = jnp.exp(s - m_new)
                    total = total + jnp.sum(p, axis=1, keepdims=True)
                    acc = acc + jnp.dot(
                        p.astype(jnp.bfloat16), tile_ref[1], preferred_element_type=jnp.float32
                    )
                l_ref[...] = total
                acc_ref[...] = acc
                m_ref[...] = m_new

            if off_t == 0 and off_h == 0:
                block()
            else:
                pl.when(jnp.logical_and(reach_t >= off_t, reach_h >= off_h))(block)
        if final:
            out = acc_ref[...] / l_ref[...]
            out = jnp.where(qvalid_ref[...] > 0, out, 0.0)
            o_ref[...] = out.astype(o_ref.dtype)
        else:
            m_out[...] = m_ref[...]
            l_out[...] = l_ref[...]
            acc_out[...] = acc_ref[...]

    return kernel


def attend(reach, queries, text, tiles, bias, state=None, qvalid=None):
    tile_len, col_width = queries.shape
    heads = col_width // HD
    blocks = [b for _, _, b in tiles]
    specs = [pl.BlockSpec((tile_len, HD), lambda h, r: (0, h))]
    args = [queries]
    if text is not None:
        specs.append(pl.BlockSpec((2, text.shape[1], HD), lambda h, r: (0, 0, h)))
        args.append(text)
    for array, index, _ in tiles:
        if index is None:
            specs.append(pl.BlockSpec((2, tile_len, HD), lambda h, r: (0, 0, h)))
        else:
            specs.append(
                pl.BlockSpec((None, 2, tile_len, HD), lambda h, r, i=index: (i, 0, 0, h))
            )
        args.append(array)
    specs.append(pl.BlockSpec(bias.shape, lambda h, r: (0, 0, 0)))
    args.append(bias)
    row_spec = pl.BlockSpec((None, tile_len, 1), lambda h, r: (h, 0, 0))
    acc_spec = pl.BlockSpec((tile_len, HD), lambda h, r: (0, h))
    if state is not None:
        specs += [row_spec, row_spec, acc_spec]
        args += list(state)
    final = qvalid is not None
    if final:
        specs.append(pl.BlockSpec(qvalid.shape, lambda h, r: (0, 0)))
        args.append(qvalid)
        out_specs = pl.BlockSpec((tile_len, HD), lambda h, r: (0, h))
        out_shape = jax.ShapeDtypeStruct((tile_len, col_width), jnp.bfloat16)
    else:
        out_specs = [row_spec, row_spec, acc_spec]
        row_shape = jax.ShapeDtypeStruct((heads, tile_len, 1), jnp.float32)
        out_shape = [row_shape, row_shape, jax.ShapeDtypeStruct((tile_len, col_width), jnp.float32)]
    grid_spec = pltpu.PrefetchScalarGridSpec(
        num_scalar_prefetch=1,
        grid=(heads,),
        in_specs=specs,
        out_specs=out_specs,
        scratch_shapes=[
            pltpu.VMEM((tile_len, 1), jnp.float32),
            pltpu.VMEM((tile_len, 1), jnp.float32),
            pltpu.VMEM((tile_len, HD), jnp.float32),
        ],
    )
    kernel = make_kernel(blocks, text is not None, state is not None, final)
    return pl.pallas_call(kernel, grid_spec=grid_spec, out_shape=out_shape)(reach, *args)


def per_device(image_q, image_kv, text_kv, residual, out_weight, out_gate, head_reach, tile_extent):
    tile_len = image_q.shape[2]
    col_width = image_q.shape[3]
    tm_size = lax.axis_size("tm")
    height_size = lax.axis_size("height")
    mp_size = lax.axis_size("mp")

    own = image_kv[0, 0]
    h_before = lax.ppermute(own, "height", shift_pairs(height_size, 1))
    h_after = lax.ppermute(own, "height", shift_pairs(height_size, -1))
    text_group = text_halves(text_kv)
    step = 1
    while 4 * step < tm_size:
        text_group = exchange(text_group, tm_size, step)
        step *= 2
    time_start = lax.axis_index("tm")
    height_start = lax.axis_index("height")
    zero_index = jnp.int32(0)
    padded_ext = jnp.pad(tile_extent, ((0, 0), (1, 1), (1, 1)))
    local_ext = lax.dynamic_slice(padded_ext, (zero_index, time_start, height_start), (2, 3, 3))
    key_valid = token_masks(local_ext)
    bias = jnp.where(key_valid, 0.0, NEG).astype(jnp.float32).reshape(9, 1, tile_len)
    qvalid = key_valid[1, 1].astype(jnp.float32).reshape(tile_len, 1)

    sent, text_group, h_before, h_after, bias, qvalid = lax.optimization_barrier(
        (own, text_group, h_before, h_after, bias, qvalid)
    )
    t_before = lax.ppermute(sent, "tm", shift_pairs(tm_size, 1))
    t_after = lax.ppermute(sent, "tm", shift_pairs(tm_size, -1))
    while step < tm_size:
        text_group = exchange(text_group, tm_size, step)
        step *= 2
    text = join_halves(text_group)
    queries = image_q[0, 0]
    near = [(own, None, 4), (h_before, None, 3), (h_after, None, 5)]
    state = attend(head_reach, queries, text, near, bias)
    t_before, t_after, sent, state = lax.optimization_barrier((t_before, t_after, sent, state))
    earlier_low = lax.ppermute(t_before, "height", shift_pairs(height_size, 1))
    earlier_high = lax.ppermute(t_before, "height", shift_pairs(height_size, -1))
    partner = lax.ppermute(t_after, "height", [(i, i ^ 1) for i in range(height_size)])
    diagonal = lax.ppermute(sent, ("tm", "height"), diagonal_pairs(tm_size, height_size, -1))
    across = [(t_before, None, 1), (t_after, None, 7)]
    state = attend(head_reach, queries, None, across, bias, state)
    odd_height = lax.axis_index("height") % 2 == 1
    corners = [
        (earlier_low, None, 0),
        (earlier_high, None, 2),
        (jnp.where(odd_height, partner, diagonal), None, 6),
        (jnp.where(odd_height, diagonal, partner), None, 8),
    ]
    attended = attend(head_reach, queries, None, corners, bias, state, qvalid)

    mp_index = lax.axis_index("mp")
    chunk = out_weight.shape[1] // mp_size
    projected = jnp.dot(attended, out_weight, preferred_element_type=jnp.float32)
    projected = projected.astype(jnp.bfloat16)
    received = []
    for step in (2, 1, 3):
        target = (mp_index + step) % mp_size
        part = lax.dynamic_slice_in_dim(projected, target * chunk, chunk, 1)
        pairs = [(i, (i + step) % mp_size) for i in range(mp_size)]
        received.append(lax.ppermute(part, "mp", pairs))
    branch = lax.dynamic_slice_in_dim(projected, mp_index * chunk, chunk, 1).astype(jnp.float32)
    for part in received:
        branch = branch + part.astype(jnp.float32)
    updated = residual[0, 0].astype(jnp.float32) + out_gate * branch
    return updated.astype(jnp.bfloat16)[None, None]


def solution(mesh):
    return jax.shard_map(
        per_device,
        mesh=mesh,
        in_specs=(
            P("tm", "height", None, "mp"),
            P("tm", "height", None, None, "mp"),
            P(None, "tm", "mp"),
            P("tm", "height", None, "mp"),
            P("mp", None),
            P("mp"),
            P("mp", None),
            P(),
        ),
        out_specs=P("tm", "height", None, "mp"),
        check_vma=False,
    )
```

```python
import math

import jax
import jax.numpy as jnp
from jax import lax
from jax.experimental import pallas as pl
from jax.experimental.pallas import tpu as pltpu
from jax.sharding import PartitionSpec as P

HD = 128
TXT = 256
TILE_F = 6
TILE_R = 8
TILE_C = 8
NEG = -1e30


def token_masks(extent_pair):
    positions = jnp.arange(TILE_F * TILE_R * TILE_C, dtype=jnp.int32)
    frame_of = positions // (TILE_R * TILE_C)
    row_of = positions // TILE_C % TILE_R
    frame_ok = frame_of < extent_pair[0][..., None]
    row_ok = row_of < extent_pair[1][..., None]
    return jnp.logical_and(frame_ok, row_ok)


def shift_pairs(devices, step):
    return [(i, i + step) for i in range(devices) if 0 <= i + step < devices]


def diagonal_pairs(tm_size, height_size, step):
    pairs = []
    for t in range(tm_size):
        if not 0 <= t + step < tm_size:
            continue
        for h in range(1, height_size - 1, 2):
            pairs.append((t * height_size + h, (t + step) * height_size + h + 1))
            pairs.append((t * height_size + h + 1, (t + step) * height_size + h))
    return pairs


def text_halves(text_kv):
    half_width = text_kv.shape[2] // 2
    half = lax.axis_index("height") % 2
    return lax.dynamic_slice_in_dim(text_kv, half * half_width, half_width, 2)


def exchange(block, devices, step):
    position = lax.axis_index("tm")
    other = lax.ppermute(block, "tm", [(i, i ^ step) for i in range(devices)])
    low_first = jnp.concatenate([block, other], axis=1)
    high_first = jnp.concatenate([other, block], axis=1)
    return jnp.where((position & step) == 0, low_first, high_first)


def join_halves(mine):
    half = lax.axis_index("height") % 2
    pairs = [(i, i ^ 1) for i in range(lax.axis_size("height"))]
    other = lax.ppermute(mine, "height", pairs)
    low_first = jnp.concatenate([mine, other], axis=2)
    high_first = jnp.concatenate([other, mine], axis=2)
    return jnp.where(half == 0, low_first, high_first)


def make_kernel(blocks, extras, has_text, has_state, final, heads):
    count = len(blocks)

    def kernel(reach_ref, q_ref, *rest):
        rest = list(rest)
        text_ref = rest.pop(0) if has_text else None
        tile_refs = rest[:count]
        rest = rest[count:]
        extra_of = dict(zip(extras, rest[:len(extras)]))
        rest = rest[len(extras):]
        bias_ref = rest.pop(0)
        if has_state:
            m_in, l_in, acc_in = rest[:3]
            rest = rest[3:]
        if final:
            qvalid_ref = rest.pop(0)
            o_ref = rest.pop(0)
        else:
            m_out, l_out, acc_out = rest[:3]
            rest = rest[3:]
        m_ref, l_ref, acc_ref = rest
        head = pl.program_id(0)
        scale = 1.0 / math.sqrt(HD)
        q = q_ref[...]
        dims = (((1,), (1,)), ((), ()))
        if has_state:
            m_ref[...] = m_in[...]
            l_ref[...] = l_in[...]
            acc_ref[...] = acc_in[...]
        else:
            m_ref[...] = jnp.full(m_ref.shape, NEG, jnp.float32)
            l_ref[...] = jnp.zeros(l_ref.shape, jnp.float32)
            acc_ref[...] = jnp.zeros(acc_ref.shape, jnp.float32)
        if has_text:
            s = lax.dot_general(q, text_ref[0], dims, preferred_element_type=jnp.float32) * scale
            m_old = m_ref[...]
            m_new = jnp.maximum(m_old, jnp.max(s, axis=1, keepdims=True))
            alpha = jnp.exp(m_old - m_new)
            p = jnp.exp(s - m_new)
            l_ref[...] = alpha * l_ref[...] + jnp.sum(p, axis=1, keepdims=True)
            acc_ref[...] = alpha * acc_ref[...] + jnp.dot(
                p.astype(jnp.bfloat16), text_ref[1], preferred_element_type=jnp.float32
            )
            m_ref[...] = m_new
        reach_t = reach_ref[head, 0]
        reach_h = reach_ref[head, 1]
        weight = reach_ref[heads, 0].astype(jnp.float32)

        def load(tile_ref, b, part):
            if b not in extra_of:
                return tile_ref[part]
            main = tile_ref[part].astype(jnp.float32)
            other = extra_of[b][part].astype(jnp.float32)
            return (main * weight + other * (1.0 - weight)).astype(jnp.bfloat16)
        groups = {}
        for tile_ref, b in zip(tile_refs, blocks):
            groups.setdefault((abs(b // 3 - 1), abs(b % 3 - 1)), []).append((tile_ref, b))
        for (off_t, off_h), members in groups.items():

            def block(members=members):
                scores = []
                for tile_ref, b in members:
                    s = lax.dot_general(q, load(tile_ref, b, 0), dims, preferred_element_type=jnp.float32)
                    scores.append(s * scale + bias_ref[b])
                m_old = m_ref[...]
                m_new = m_old
                for s in scores:
                    m_new = jnp.maximum(m_new, jnp.max(s, axis=1, keepdims=True))
                alpha = jnp.exp(m_old - m_new)
                total = alpha * l_ref[...]
                acc = alpha * acc_ref[...]
                for s, (tile_ref, b) in zip(scores, members):
                    p = jnp.exp(s - m_new)
                    total = total + jnp.sum(p, axis=1, keepdims=True)
                    acc = acc + jnp.dot(
                        p.astype(jnp.bfloat16), load(tile_ref, b, 1), preferred_element_type=jnp.float32
                    )
                l_ref[...] = total
                acc_ref[...] = acc
                m_ref[...] = m_new

            if off_t == 0 and off_h == 0:
                block()
            else:
                pl.when(jnp.logical_and(reach_t >= off_t, reach_h >= off_h))(block)
        if final:
            out = acc_ref[...] / l_ref[...]
            out = jnp.where(qvalid_ref[...] > 0, out, 0.0)
            o_ref[...] = out.astype(o_ref.dtype)
        else:
            m_out[...] = m_ref[...]
            l_out[...] = l_ref[...]
            acc_out[...] = acc_ref[...]

    return kernel


def attend(reach, queries, text, tiles, bias, state=None, qvalid=None, extra=None):
    tile_len, col_width = queries.shape
    heads = col_width // HD
    blocks = [b for _, _, b in tiles]
    specs = [pl.BlockSpec((tile_len, HD), lambda h, r: (0, h))]
    args = [queries]
    if text is not None:
        specs.append(pl.BlockSpec((2, text.shape[1], HD), lambda h, r: (0, 0, h)))
        args.append(text)
    def add_tile(array, index):
        if index is None:
            specs.append(pl.BlockSpec((2, tile_len, HD), lambda h, r: (0, 0, h)))
        else:
            specs.append(
                pl.BlockSpec((None, 2, tile_len, HD), lambda h, r, i=index: (i, 0, 0, h))
            )
        args.append(array)

    for array, index, _ in tiles:
        add_tile(array, index)
    extras = [b for b in blocks if b in (extra or {})]
    for b in extras:
        add_tile(*extra[b])
    specs.append(pl.BlockSpec(bias.shape, lambda h, r: (0, 0, 0)))
    args.append(bias)
    row_spec = pl.BlockSpec((None, tile_len, 1), lambda h, r: (h, 0, 0))
    acc_spec = pl.BlockSpec((tile_len, HD), lambda h, r: (0, h))
    if state is not None:
        specs += [row_spec, row_spec, acc_spec]
        args += list(state)
    final = qvalid is not None
    if final:
        specs.append(pl.BlockSpec(qvalid.shape, lambda h, r: (0, 0)))
        args.append(qvalid)
        out_specs = pl.BlockSpec((tile_len, HD), lambda h, r: (0, h))
        out_shape = jax.ShapeDtypeStruct((tile_len, col_width), jnp.bfloat16)
    else:
        out_specs = [row_spec, row_spec, acc_spec]
        row_shape = jax.ShapeDtypeStruct((heads, tile_len, 1), jnp.float32)
        out_shape = [row_shape, row_shape, jax.ShapeDtypeStruct((tile_len, col_width), jnp.float32)]
    grid_spec = pltpu.PrefetchScalarGridSpec(
        num_scalar_prefetch=1,
        grid=(heads,),
        in_specs=specs,
        out_specs=out_specs,
        scratch_shapes=[
            pltpu.VMEM((tile_len, 1), jnp.float32),
            pltpu.VMEM((tile_len, 1), jnp.float32),
            pltpu.VMEM((tile_len, HD), jnp.float32),
        ],
    )
    kernel = make_kernel(blocks, extras, text is not None, state is not None, final, heads)
    return pl.pallas_call(kernel, grid_spec=grid_spec, out_shape=out_shape)(reach, *args)


def per_device(image_q, image_kv, text_kv, residual, out_weight, out_gate, head_reach, tile_extent):
    tile_len = image_q.shape[2]
    col_width = image_q.shape[3]
    tm_size = lax.axis_size("tm")
    height_size = lax.axis_size("height")
    mp_size = lax.axis_size("mp")

    own = image_kv[0, 0]
    h_before = lax.ppermute(own, "height", shift_pairs(height_size, 1))
    h_after = lax.ppermute(own, "height", shift_pairs(height_size, -1))
    text_group = text_halves(text_kv)
    step = 1
    while 2 * step < tm_size:
        text_group = exchange(text_group, tm_size, step)
        step *= 2
    time_start = lax.axis_index("tm")
    height_start = lax.axis_index("height")
    zero_index = jnp.int32(0)
    padded_ext = jnp.pad(tile_extent, ((0, 0), (1, 1), (1, 1)))
    local_ext = lax.dynamic_slice(padded_ext, (zero_index, time_start, height_start), (2, 3, 3))
    key_valid = token_masks(local_ext)
    bias = jnp.where(key_valid, 0.0, NEG).astype(jnp.float32).reshape(9, 1, tile_len)
    qvalid = key_valid[1, 1].astype(jnp.float32).reshape(tile_len, 1)

    sent, text_group, h_before, h_after, bias, qvalid = lax.optimization_barrier(
        (own, text_group, h_before, h_after, bias, qvalid)
    )
    t_before = lax.ppermute(sent, "tm", shift_pairs(tm_size, 1))
    t_after = lax.ppermute(sent, "tm", shift_pairs(tm_size, -1))
    if step < tm_size:
        text_group = exchange(text_group, tm_size, step)
    text = join_halves(text_group)
    queries = image_q[0, 0]
    odd = (lax.axis_index("height") % 2).astype(head_reach.dtype)
    reach_odd = jnp.concatenate([head_reach, jnp.stack([odd, odd])[None]], axis=0)
    near = [(own, None, 4), (h_before, None, 3), (h_after, None, 5)]
    state = attend(head_reach, queries, text, near, bias)
    t_before, t_after, sent, state = lax.optimization_barrier((t_before, t_after, sent, state))
    earlier_low = lax.ppermute(t_before, "height", shift_pairs(height_size, 1))
    earlier_high = lax.ppermute(t_before, "height", shift_pairs(height_size, -1))
    partner = lax.ppermute(t_after, "height", [(i, i ^ 1) for i in range(height_size)])
    diagonal = lax.ppermute(sent, ("tm", "height"), diagonal_pairs(tm_size, height_size, -1))
    across = [(t_before, None, 1), (t_after, None, 7)]
    state = attend(head_reach, queries, None, across, bias, state)
    corners = [(earlier_low, None, 0), (earlier_high, None, 2), (partner, None, 6), (diagonal, None, 8)]
    extra = {6: (diagonal, None), 8: (partner, None)}
    attended = attend(reach_odd, queries, None, corners, bias, state, qvalid, extra)

    mp_index = lax.axis_index("mp")
    chunk = out_weight.shape[1] // mp_size
    projected = jnp.dot(attended, out_weight, preferred_element_type=jnp.float32)
    projected = projected.astype(jnp.bfloat16)
    received = []
    for step in (2, 1, 3):
        target = (mp_index + step) % mp_size
        part = lax.dynamic_slice_in_dim(projected, target * chunk, chunk, 1)
        pairs = [(i, (i + step) % mp_size) for i in range(mp_size)]
        received.append(lax.ppermute(part, "mp", pairs))
    branch = lax.dynamic_slice_in_dim(projected, mp_index * chunk, chunk, 1).astype(jnp.float32)
    for part in received:
        branch = branch + part.astype(jnp.float32)
    updated = residual[0, 0].astype(jnp.float32) + out_gate * branch
    return updated.astype(jnp.bfloat16)[None, None]


def solution(mesh):
    return jax.shard_map(
        per_device,
        mesh=mesh,
        in_specs=(
            P("tm", "height", None, "mp"),
            P("tm", "height", None, None, "mp"),
            P(None, "tm", "mp"),
            P("tm", "height", None, "mp"),
            P("mp", None),
            P("mp"),
            P("mp", None),
            P(),
        ),
        out_specs=P("tm", "height", None, "mp"),
        check_vma=False,
    )
```
